256 devices in a mesh: seq: 32 (over y, x, core), tp: 8 (over z).
Axes of the slice: x: 4, y: 4, z: 8, core: 2. Of those that a mesh axis runs over, the one named last changes fastest.
Arguments:
- vis_feat: bfloat16 [512, 12800], P('seq', 'tp'), may hold values from -256 to 256
- ln_gain: float32 [12800], P('tp'), may hold values from 0.25 to 1.75
- proj_weight: bfloat16 [12800, 8192], P('tp', 'seq'), may hold values from -0.0546875 to 0.0546875
- text_embed: bfloat16 [8192, 8192], P('seq'), may hold values from -128 to 128
- rms_gain: float32 [8192], replicated, may hold values from 0.25 to 1.75
- wq: bfloat16 [8192, 4096], P('seq', 'tp'), may hold values from -1 to 1
- wk: bfloat16 [8192, 1024], P('seq', 'tp'), may hold values from -1 to 1
- wv: bfloat16 [8192, 1024], P('seq', 'tp'), may hold values from -0.0625 to 0.0625
- doc_ids: int32 [8192], P('seq'), may hold values from 0 to 63, as said below
- vis_slot: int32 [8192], P('seq'), may hold values from -1 to 31, as said below
- slot_token: int32 [1024], replicated, may hold values from -1 to 511, as said below
- token_slot: int32 [512], replicated, may hold values from 0 to 1023, as said below
- cotangent: bfloat16 [8192, 4096], P('seq', 'tp'), may hold values from -6 to 6
Outputs:
- context: bfloat16 [8192, 4096], P('seq', 'tp')
- vis_grad: bfloat16 [512, 12800], P('seq', 'tp')
The draws below stay inside these ranges and needn't reach their ends.
Inputs may be any that keep to these rules, and one draw needn't show every extreme that they name: `doc_ids`: document numbers never fall along the positions and rise by one at each new document; each document has 1 to 256 positions, and one has exactly 256. `vis_slot`: in each block of 256 positions the image positions form one run that ends at the block's last position, numbered 0, 1, 2 ... in order; a block has 0 to 32 of them, 512 in all, and some block has exactly 32. `slot_token`: entry b * 32 + j names the visual token at image position j of block b, or -1 where block b has fewer image positions; each visual token is named once. `token_slot`: for each visual token, the index of the entry of slot_token that names it.
All inputs are finite; a program needn't handle non-finite values.
Results may differ from the reference program's by a relative error of at most 0.025.
Values may be sent and summed in bfloat16 or wider, within the bound.
No kernel may reach another device: no remote copies, remote signals or barrier semaphores. Data moves between devices by JAX's collectives and lax.ppermute only.
A program may use at most 128 MiB of HBM per device.

```python
import math
import jax
import jax.numpy as jnp
from jax import lax

VF = 12800
D = 8192
HEAD = 128
KV = 8
HEADS = 32
TOK_DEV = 256
VIS_DEV = 16
CAPD = 32
GROUP = 4
TOKENS = 8192
VIS = 512
N_SEQ = 32


def routing_tables(key):
    groups = TOKENS // TOK_DEV
    pairs = groups // 2
    subkeys = jax.random.split(jax.random.fold_in(key, 501), 5)
    shifts = jax.random.randint(subkeys[0], (pairs,), 1 - VIS_DEV, VIS_DEV + 1)
    chosen = jax.random.randint(subkeys[1], (), 0, pairs)
    flip = jax.random.randint(subkeys[2], (), 0, 2) * 2 - 1
    flip = jnp.where(chosen == pairs - 1, 1, flip)
    shifts = jnp.where(jnp.arange(pairs) == chosen, flip * VIS_DEV, shifts)
    counts = jnp.stack([VIS_DEV + shifts, VIS_DEV - shifts], axis=1).reshape(groups)
    offsets = TOK_DEV - counts
    firsts = jnp.cumsum(counts) - counts
    order = jax.random.permutation(subkeys[4], VIS)
    lanes = jnp.arange(CAPD)
    live = lanes[None, :] < counts[:, None]
    picked = order[jnp.clip(firsts[:, None] + lanes[None, :], 0, VIS - 1)]
    slot_token = jnp.where(live, picked, -1).reshape(groups * CAPD)
    local = jnp.arange(TOK_DEV)[None, :] - offsets[:, None]
    vis_slot = jnp.where((local >= 0) & (local < counts[:, None]), local, -1).reshape(TOKENS)
    slot_ids = jnp.arange(groups * CAPD)
    target = jnp.where(live.reshape(groups * CAPD), picked.reshape(groups * CAPD), VIS)
    token_slot = jnp.zeros((VIS,), jnp.int32).at[target].set(slot_ids, mode='drop')
    return (slot_token.astype(jnp.int32), vis_slot.astype(jnp.int32), token_slot.astype(jnp.int32))


def draw_slot_token(key, part):
    return routing_tables(key)[0]


def draw_vis_slot(key, part):
    return routing_tables(key)[1]


def draw_token_slot(key, part):
    return routing_tables(key)[2]


def draw_doc_ids(key, part):
    groups = TOKENS // TOK_DEV
    quarter = TOK_DEV // 4
    half = TOK_DEV // 2
    subkeys = jax.random.split(jax.random.fold_in(key, 801), 3)
    index = jnp.arange(groups)
    starts = jax.random.randint(subkeys[0], (groups,), quarter, half + 1)
    gaps = jax.random.randint(subkeys[1], (groups,), 0, quarter)
    chosen = jax.random.randint(subkeys[2], (), 0, groups - 1)
    starts = jnp.where(index == chosen, quarter, starts)
    starts = jnp.where(index == chosen + 1, half, starts)
    gaps = jnp.where(starts == half, jnp.maximum(gaps, 1), gaps)
    gaps = jnp.where(index == chosen, 0, gaps)
    firsts = index * TOK_DEV
    first_cuts = (firsts + starts)[1:]
    second_cuts = firsts + half + gaps
    marks = jnp.zeros((TOKENS,), jnp.int32).at[first_cuts].set(1).at[second_cuts].set(1)
    return jnp.cumsum(marks).astype(jnp.int32)


def draw_vis_feat(key, part):
    subkeys = jax.random.split(jax.random.fold_in(key, 601), 3)
    rows = jnp.exp(jax.random.uniform(subkeys[1], (VIS, 1), minval=0.0, maxval=math.log(10.0)))
    ramp = jnp.exp(math.log(3.0) * jnp.arange(VF).astype(jnp.float32) / VF)
    rough = jnp.exp(jax.random.uniform(subkeys[2], (VF,), minval=-0.35, maxval=0.35))
    base = jnp.clip(jax.random.normal(subkeys[0], (VIS, VF)), -6.0, 6.0)
    return (base * rows * (ramp * rough)[None, :]).astype(jnp.bfloat16)


def draw_text_embed(key, part):
    subkeys = jax.random.split(jax.random.fold_in(key, 703), 2)
    rows = jnp.exp(jax.random.uniform(subkeys[1], (TOKENS, 1), minval=0.0, maxval=math.log(10.0)))
    base = jnp.clip(jax.random.normal(subkeys[0], (TOKENS, D)), -6.0, 6.0)
    return (base * rows).astype(jnp.bfloat16)


def draw_wq(key, part):
    base = jnp.clip(jax.random.normal(jax.random.fold_in(key, 704), (D, HEADS * HEAD)), -6.0, 6.0) / math.sqrt(D)
    return base.astype(jnp.bfloat16)


def draw_wk(key, part):
    base = jnp.clip(jax.random.normal(jax.random.fold_in(key, 705), (D, KV * HEAD)), -6.0, 6.0) / math.sqrt(D)
    return base.astype(jnp.bfloat16)


def shard_levels(key, extent, cuts, least, high):
    factor_of, own = 1.0, jax.random.fold_in(key, 6)
    for dim, blocks in cuts:
        draws = jnp.exp(jax.random.uniform(jax.random.fold_in(own, dim), (blocks,), jnp.float32, least / len(cuts), high / len(cuts)))
        factor_of = factor_of * jnp.repeat(draws, extent[dim] // blocks).reshape([-1 if axis == dim else 1 for axis in range(len(extent))])
    return factor_of


def scatter_about(own_key, dims, scale, bound, shards=(), kind=jnp.bfloat16):
    loudness = shard_levels(own_key, dims, shards, -0.22, 0.18) if shards else 1.0
    values = jax.random.normal(own_key, dims, jnp.float32) * scale * loudness
    return jnp.minimum(jnp.maximum(values, -bound), bound).astype(kind)


def setup_inputs(seed: int = 0) -> dict:
    arg_keys = jax.random.split(jax.random.key(seed), 14)
    return {
        "vis_feat": draw_vis_feat(jax.random.fold_in(arg_keys[13], 71), 0),
        "ln_gain": jnp.clip(1.0 + 0.15 * jax.random.normal(arg_keys[1], (VF,), jnp.float32), 0.25, 1.75),
        "proj_weight": scatter_about(arg_keys[2], (VF, D), VF ** -0.5, 0.0546875, ((0, 8), (1, 32))),
        "text_embed": draw_text_embed(jax.random.fold_in(arg_keys[13], 71), 0),
        "rms_gain": jnp.clip(1.0 + 0.15 * jax.random.normal(arg_keys[4], (D,), jnp.float32), 0.25, 1.75),
        "wq": draw_wq(jax.random.fold_in(arg_keys[13], 71), 0),
        "wk": draw_wk(jax.random.fold_in(arg_keys[13], 71), 0),
        "wv": scatter_about(arg_keys[7], (D, KV * HEAD), D ** -0.5, 0.0625, ((0, 32), (1, 8))),
        "doc_ids": draw_doc_ids(jax.random.fold_in(arg_keys[13], 71), 0),
        "vis_slot": draw_vis_slot(jax.random.fold_in(arg_keys[13], 71), 0),
        "slot_token": draw_slot_token(jax.random.fold_in(arg_keys[13], 71), 0),
        "token_slot": draw_token_slot(jax.random.fold_in(arg_keys[13], 71), 0),
        "cotangent": scatter_about(arg_keys[12], (TOKENS, HEADS * HEAD), 1.0, 6.0, ((0, 32), (1, 8))),
    }


ln_eps = 1e-05
rms_eps = 1e-06
rope_base = 1000000.0
masked_score = -1e+30

def rope_tables(positions, head_width):
    half = head_width // 2
    frequency = rope_base ** (-(jnp.arange(half).astype(jnp.float32) * 2.0 / head_width))
    angle = positions.astype(jnp.float32)[:, None] * frequency[None, :]
    return (jnp.cos(angle), jnp.sin(angle))

def rotate(values, cosine, sine):
    half = values.shape[-1] // 2
    first = values[..., :half]
    second = values[..., half:]
    cos_rows = cosine[:, None, :]
    sin_rows = sine[:, None, :]
    return jnp.concatenate([first * cos_rows - second * sin_rows, second * cos_rows + first * sin_rows], axis=-1)

def unrotate(grads, cosine, sine):
    half = grads.shape[-1] // 2
    first = grads[..., :half]
    second = grads[..., half:]
    cos_rows = cosine[:, None, :]
    sin_rows = sine[:, None, :]
    return jnp.concatenate([first * cos_rows + second * sin_rows, second * cos_rows - first * sin_rows], axis=-1)

def norm_backward(rows, grads, gain):
    inv_rms = lax.rsqrt(lax.optimization_barrier(jnp.mean(rows * rows, axis=1, keepdims=True)) + rms_eps)
    scaled = grads * gain[None, :]
    inner = lax.optimization_barrier(jnp.mean(rows * scaled, axis=1, keepdims=True))
    return inv_rms * scaled - rows * (inv_rms * inv_rms * inv_rms) * inner

def attention_block(queries, keys, values, grads, allowed):
    scale = 1.0 / math.sqrt(queries.shape[-1])
    wide_q = queries.astype(jnp.float32)
    wide_k = keys.astype(jnp.float32)
    wide_v = values.astype(jnp.float32)
    wide_g = grads.astype(jnp.float32)
    scores = jnp.einsum('qhgd,khd->hgqk', wide_q, wide_k) * scale
    masked = jnp.where(allowed[None, None], scores, masked_score)
    peak = lax.optimization_barrier(jnp.max(masked, axis=-1, keepdims=True))
    raised = jnp.where(allowed[None, None], jnp.exp(masked - peak), 0.0)
    shares = raised / lax.optimization_barrier(jnp.sum(raised, axis=-1, keepdims=True))
    shares_low = shares.astype(jnp.bfloat16)
    wide_s = shares_low.astype(jnp.float32)
    context = jnp.einsum('hgqk,khd->qhgd', wide_s, wide_v).astype(jnp.bfloat16)
    share_grads = jnp.einsum('qhgd,khd->hgqk', wide_g, wide_v)
    delta = lax.optimization_barrier(jnp.sum(shares * share_grads, axis=-1, keepdims=True))
    score_grads = (shares * (share_grads - delta) * scale).astype(jnp.bfloat16).astype(jnp.float32)
    query_grads = jnp.einsum('hgqk,khd->qhgd', score_grads, wide_k)
    key_grads = jnp.einsum('hgqk,qhgd->khd', score_grads, wide_q)
    value_grads = jnp.einsum('hgqk,qhgd->khd', wide_s, wide_g)
    return (context, query_grads, key_grads, value_grads)

def reference(vis_feat, ln_gain, proj_weight, text_embed, rms_gain, wq, wk, wv, doc_ids, vis_slot, slot_token, token_slot, cotangent):
    features = vis_feat.astype(jnp.float32)
    row_mean = lax.optimization_barrier(jnp.sum(features, axis=1)) / VF
    row_var = lax.optimization_barrier(jnp.sum(features * features, axis=1)) / VF - row_mean * row_mean
    inv_std = lax.rsqrt(row_var + ln_eps)
    centred = (features - row_mean[:, None]) * inv_std[:, None]
    vis_normed = (centred * ln_gain[None, :]).astype(jnp.bfloat16)
    vis_embed = jnp.dot(vis_normed, proj_weight, preferred_element_type=jnp.float32).astype(jnp.bfloat16)
    positions = jnp.arange(TOKENS, dtype=jnp.int32)
    blocks = positions // TOK_DEV
    is_image = vis_slot >= 0
    slot_total = N_SEQ * CAPD
    global_slot = jnp.where(is_image, blocks * CAPD + vis_slot, slot_total).astype(jnp.int32)
    token_at = jnp.where(is_image, slot_token[jnp.minimum(global_slot, slot_total - 1)], 0).astype(jnp.int32)
    hidden = jnp.where(is_image[:, None], vis_embed[token_at], text_embed)
    hidden_wide = hidden.astype(jnp.float32)
    inv_rms = lax.rsqrt(lax.optimization_barrier(jnp.mean(hidden_wide * hidden_wide, axis=1, keepdims=True)) + rms_eps)
    normed = (hidden_wide * inv_rms * rms_gain[None, :]).astype(jnp.bfloat16)
    query_proj = jnp.dot(normed, wq, preferred_element_type=jnp.float32)
    key_proj = jnp.dot(normed, wk, preferred_element_type=jnp.float32)
    value_proj = jnp.dot(normed, wv, preferred_element_type=jnp.float32)
    cosine, sine = rope_tables(positions, HEAD)
    roped_queries = rotate(query_proj.reshape(TOKENS, HEADS, HEAD), cosine, sine).astype(jnp.bfloat16)
    roped_keys = rotate(key_proj.reshape(TOKENS, KV, HEAD), cosine, sine).astype(jnp.bfloat16)
    values = value_proj.astype(jnp.bfloat16).reshape(TOKENS, KV, HEAD)
    front = jnp.zeros((TOK_DEV, KV, HEAD), jnp.bfloat16)
    key_padded = jnp.concatenate([front, roped_keys], axis=0)
    value_padded = jnp.concatenate([front, values], axis=0)
    doc_marks = (doc_ids + 1).astype(jnp.int32)
    doc_padded = jnp.concatenate([jnp.zeros((TOK_DEV,), jnp.int32), doc_marks], axis=0)
    pos_padded = jnp.concatenate([positions[:TOK_DEV] - TOK_DEV, positions], axis=0)
    query_four = roped_queries.reshape(TOKENS, KV, GROUP, HEAD)
    grad_four = cotangent.reshape(TOKENS, KV, GROUP, HEAD)

    def one_block(index):
        start = (index * TOK_DEV).astype(jnp.int32)
        block_q = lax.dynamic_slice_in_dim(query_four, start, TOK_DEV, 0)
        block_g = lax.dynamic_slice_in_dim(grad_four, start, TOK_DEV, 0)
        block_k = lax.dynamic_slice_in_dim(key_padded, start, 2 * TOK_DEV, 0)
        block_v = lax.dynamic_slice_in_dim(value_padded, start, 2 * TOK_DEV, 0)
        query_docs = lax.dynamic_slice_in_dim(doc_marks, start, TOK_DEV, 0)
        key_docs = lax.dynamic_slice_in_dim(doc_padded, start, 2 * TOK_DEV, 0)
        query_pos = lax.dynamic_slice_in_dim(positions, start, TOK_DEV, 0)
        key_pos = lax.dynamic_slice_in_dim(pos_padded, start, 2 * TOK_DEV, 0)
        allowed = (key_docs[None, :] == query_docs[:, None]) & (key_pos[None, :] <= query_pos[:, None])
        return attention_block(block_q, block_k, block_v, block_g, allowed)
    context, query_grads, key_grads, value_grads = lax.map(one_block, jnp.arange(N_SEQ, dtype=jnp.int32))
    context = context.reshape(TOKENS, HEADS * HEAD)
    tail = jnp.zeros((1, TOK_DEV, KV, HEAD), jnp.float32)
    key_total = key_grads[:, TOK_DEV:] + jnp.concatenate([key_grads[1:, :TOK_DEV], tail], axis=0)
    value_total = value_grads[:, TOK_DEV:] + jnp.concatenate([value_grads[1:, :TOK_DEV], tail], axis=0)
    query_pre = unrotate(query_grads.reshape(TOKENS, HEADS, HEAD), cosine, sine).astype(jnp.bfloat16).reshape(TOKENS, HEADS * HEAD)
    key_pre = unrotate(key_total.reshape(TOKENS, KV, HEAD), cosine, sine).astype(jnp.bfloat16).reshape(TOKENS, KV * HEAD)
    value_pre = value_total.astype(jnp.bfloat16).reshape(TOKENS, KV * HEAD)
    slot_pos = jnp.zeros((slot_total,), jnp.int32).at[global_slot].set(positions, mode='drop')
    where_token = slot_pos[token_slot]
    norm_grads = jnp.dot(query_pre[where_token], wq.T, preferred_element_type=jnp.float32)
    norm_grads = norm_grads + jnp.dot(key_pre[where_token], wk.T, preferred_element_type=jnp.float32)
    norm_grads = norm_grads + jnp.dot(value_pre[where_token], wv.T, preferred_element_type=jnp.float32)
    embed_grads = norm_backward(vis_embed.astype(jnp.float32), norm_grads, rms_gain).astype(jnp.bfloat16)
    feature_grads = jnp.dot(embed_grads, proj_weight.T, preferred_element_type=jnp.float32)
    scaled = feature_grads * ln_gain[None, :]
    grad_mean = lax.optimization_barrier(jnp.sum(scaled, axis=1)) / VF
    grad_inner = lax.optimization_barrier(jnp.sum(scaled * centred, axis=1)) / VF
    vis_grad = (inv_std[:, None] * (scaled - grad_mean[:, None] - centred * grad_inner[:, None])).astype(jnp.bfloat16)
    return (context, vis_grad)
```

```python
import math

import jax
import jax.numpy as jnp
from jax import lax
from jax.sharding import PartitionSpec as P

VF = 12800
HEAD = 128
CAPD = 32
GROUP = 4


ln_eps = 1e-05
rms_eps = 1e-06
rope_base = 1000000.0
masked_score = -1e30


def shifted(x, axis, by):
    peers = lax.axis_size(axis)
    pairs = [(i, i + by) for i in range(peers) if 0 <= i + by < peers]
    return lax.ppermute(x, axis, pairs)


def rope_tables(positions, head_width):
    half = head_width // 2
    frequency = rope_base ** (-(jnp.arange(half).astype(jnp.float32) * 2.0 / head_width))
    angle = positions.astype(jnp.float32)[:, None] * frequency[None, :]
    return (jnp.cos(angle), jnp.sin(angle))


def rotate(values, cosine, sine):
    half = values.shape[-1] // 2
    first = values[..., :half]
    second = values[..., half:]
    cos_rows = cosine[:, None, :]
    sin_rows = sine[:, None, :]
    return jnp.concatenate(
        [first * cos_rows - second * sin_rows, second * cos_rows + first * sin_rows], axis=-1
    )


def unrotate(grads, cosine, sine):
    half = grads.shape[-1] // 2
    first = grads[..., :half]
    second = grads[..., half:]
    cos_rows = cosine[:, None, :]
    sin_rows = sine[:, None, :]
    return jnp.concatenate(
        [first * cos_rows + second * sin_rows, second * cos_rows - first * sin_rows], axis=-1
    )


def norm_backward(rows, grads, gain):
    inv_rms = lax.rsqrt(jnp.mean(rows * rows, axis=1, keepdims=True) + rms_eps)
    scaled = grads * gain[None, :]
    inner = jnp.mean(rows * scaled, axis=1, keepdims=True)
    return inv_rms * scaled - rows * (inv_rms * inv_rms * inv_rms) * inner


def attention_block(queries, keys, values, grads, allowed):
    scale = 1.0 / math.sqrt(queries.shape[-1])
    scores = jnp.einsum("qhgd,khd->hgqk", queries, keys, preferred_element_type=jnp.float32) * scale
    masked = jnp.where(allowed[None, None], scores, masked_score)
    peak = jnp.max(masked, axis=-1, keepdims=True)
    raised = jnp.where(allowed[None, None], jnp.exp(masked - peak), 0.0)
    shares = raised / jnp.sum(raised, axis=-1, keepdims=True)
    shares_low = shares.astype(jnp.bfloat16)
    context = jnp.einsum(
        "hgqk,khd->qhgd", shares_low, values, preferred_element_type=jnp.float32
    ).astype(jnp.bfloat16)
    share_grads = jnp.einsum("qhgd,khd->hgqk", grads, values, preferred_element_type=jnp.float32)
    delta = jnp.sum(shares * share_grads, axis=-1, keepdims=True)
    score_grads = (shares * (share_grads - delta) * scale).astype(jnp.bfloat16)
    query_grads = jnp.einsum(
        "hgqk,khd->qhgd", score_grads, keys, preferred_element_type=jnp.float32
    )
    key_grads = jnp.einsum(
        "hgqk,qhgd->khd", score_grads, queries, preferred_element_type=jnp.float32
    )
    value_grads = jnp.einsum(
        "hgqk,qhgd->khd", shares_low, grads, preferred_element_type=jnp.float32
    )
    return (context, query_grads, key_grads, value_grads)


def on_device(
    vis_feat,
    ln_gain,
    proj_weight,
    text_embed,
    rms_gain,
    wq,
    wk,
    wv,
    doc_ids,
    vis_slot,
    slot_token,
    token_slot,
    cotangent,
):
    seq_count = lax.axis_size("seq")
    my_index = lax.axis_index("seq")
    tok_rows = text_embed.shape[0]
    slot_cols = proj_weight.shape[1]
    features = vis_feat.astype(jnp.float32)
    row_total, row_squares = lax.psum(
        (jnp.sum(features, axis=1), jnp.sum(features * features, axis=1)), "tp"
    )
    row_mean = row_total / VF
    row_var = row_squares / VF - row_mean * row_mean
    inv_std = lax.rsqrt(row_var + ln_eps)
    centred = (features - row_mean[:, None]) * inv_std[:, None]
    vis_normed = (centred * ln_gain[None, :]).astype(jnp.bfloat16)
    partial_embed = jnp.dot(
        lax.all_gather(vis_normed, "seq", axis=0, tiled=True),
        proj_weight,
        preferred_element_type=jnp.float32,
    )
    slot_live = (slot_token >= 0)[:, None]
    slot_index = jnp.maximum(slot_token, 0)
    summed = lax.psum(partial_embed, "tp")
    embed_rows = jnp.take(summed.astype(jnp.bfloat16), slot_index, axis=0)
    outgoing = jnp.where(slot_live, embed_rows, jnp.zeros_like(embed_rows)).reshape(
        seq_count, CAPD, slot_cols
    )
    arrived = lax.all_to_all(outgoing, "seq", split_axis=0, concat_axis=2, tiled=True)[0]
    lanes = jnp.arange(CAPD, dtype=jnp.int32)
    one_hot = (vis_slot[:, None] == lanes[None, :]).astype(jnp.bfloat16)
    placed = jnp.dot(one_hot, arrived, preferred_element_type=jnp.float32).astype(jnp.bfloat16)
    is_image = vis_slot >= 0
    hidden = jnp.where(is_image[:, None], placed, text_embed)
    hidden_wide = hidden.astype(jnp.float32)
    inv_rms = lax.rsqrt(jnp.mean(hidden_wide * hidden_wide, axis=1, keepdims=True) + rms_eps)
    normed = (hidden_wide * inv_rms * rms_gain[None, :]).astype(jnp.bfloat16)
    stacked = jnp.concatenate([wq, wk, wv], axis=1)
    query_cols = wq.shape[1]
    key_cols = wk.shape[1]
    gathered = lax.all_gather(stacked, "seq", axis=0, tiled=True)
    projected = jnp.dot(normed, gathered, preferred_element_type=jnp.float32)
    local_heads = query_cols // HEAD
    local_groups = key_cols // HEAD
    positions = my_index * tok_rows + jnp.arange(tok_rows, dtype=jnp.int32)
    cosine, sine = rope_tables(positions, HEAD)
    queries = rotate(
        projected[:, :query_cols].reshape(tok_rows, local_heads, HEAD), cosine, sine
    ).astype(jnp.bfloat16)
    keys = rotate(
        projected[:, query_cols : query_cols + key_cols].reshape(tok_rows, local_groups, HEAD),
        cosine,
        sine,
    ).astype(jnp.bfloat16)
    values = (
        projected[:, query_cols + key_cols :]
        .astype(jnp.bfloat16)
        .reshape(tok_rows, local_groups, HEAD)
    )
    doc_marks = (doc_ids + 1).astype(jnp.bfloat16)
    prev_keys, prev_values, prev_docs = shifted((keys, values, doc_marks), "seq", 1)
    all_keys = jnp.concatenate([prev_keys, keys], axis=0)
    all_values = jnp.concatenate([prev_values, values], axis=0)
    query_docs = doc_marks.astype(jnp.float32)
    key_docs = jnp.concatenate([prev_docs.astype(jnp.float32), query_docs], axis=0)
    key_positions = jnp.concatenate([positions - tok_rows, positions], axis=0)
    allowed = (key_docs[None, :] == query_docs[:, None]) & (
        key_positions[None, :] <= positions[:, None]
    )
    grads = cotangent.reshape(tok_rows, local_groups, GROUP, HEAD)
    context, query_grads, key_grads, value_grads = attention_block(
        queries.reshape(tok_rows, local_groups, GROUP, HEAD), all_keys, all_values, grads, allowed
    )
    back_keys, back_values = (
        shifted(key_grads[:tok_rows].astype(jnp.bfloat16), "seq", -1).astype(jnp.float32),
        shifted(value_grads[:tok_rows].astype(jnp.bfloat16), "seq", -1).astype(jnp.float32),
    )
    key_total = key_grads[tok_rows:] + back_keys
    value_total = value_grads[tok_rows:] + back_values
    query_pre = (
        unrotate(query_grads.reshape(tok_rows, local_heads, HEAD), cosine, sine)
        .astype(jnp.bfloat16)
        .reshape(tok_rows, query_cols)
    )
    key_pre = unrotate(key_total, cosine, sine).astype(jnp.bfloat16).reshape(tok_rows, key_cols)
    value_pre = value_total.astype(jnp.bfloat16).reshape(tok_rows, key_cols)
    proj_grads = jnp.concatenate([query_pre, key_pre, value_pre], axis=1)
    selected = lax.dot_general(
        one_hot, proj_grads, (((0,), (0,)), ((), ())), preferred_element_type=jnp.float32
    ).astype(jnp.bfloat16)
    norm_part = lax.dot_general(
        selected, gathered, (((1,), (1,)), ((), ())), preferred_element_type=jnp.float32
    )
    norm_grads = lax.psum(norm_part.astype(jnp.bfloat16), "tp").astype(jnp.float32)
    embed_grads = norm_backward(arrived.astype(jnp.float32), norm_grads, rms_gain).astype(
        jnp.bfloat16
    )
    by_owner = embed_grads.reshape(CAPD, seq_count, slot_cols).transpose(1, 0, 2)
    returned = lax.all_to_all(by_owner, "seq", split_axis=0, concat_axis=0, tiled=True)
    token_grads = jnp.take(returned.reshape(seq_count * CAPD, slot_cols), token_slot, axis=0)
    feature_grads = lax.psum_scatter(
        lax.dot_general(
            token_grads, proj_weight, (((1,), (1,)), ((), ())), preferred_element_type=jnp.float32
        ).astype(jnp.bfloat16),
        "seq",
        scatter_dimension=0,
        tiled=True,
    ).astype(jnp.float32)
    scaled = feature_grads * ln_gain[None, :]
    grad_total, grad_inner = lax.psum(
        (jnp.sum(scaled, axis=1), jnp.sum(scaled * centred, axis=1)), "tp"
    )
    vis_grad = (
        inv_std[:, None]
        * (scaled - (grad_total / VF)[:, None] - centred * (grad_inner / VF)[:, None])
    ).astype(jnp.bfloat16)
    return (context.reshape(tok_rows, query_cols), vis_grad)


def solution(mesh):
    return jax.shard_map(
        on_device,
        mesh=mesh,
        in_specs=(
            P("seq", "tp"),
            P("tp"),
            P("tp", "seq"),
            P("seq", None),
            P(),
            P("seq", "tp"),
            P("seq", "tp"),
            P("seq", "tp"),
            P("seq"),
            P("seq"),
            P(),
            P(),
            P("seq", "tp"),
        ),
        out_specs=(P("seq", "tp"), P("seq", "tp")),
        check_vma=False,
    )
```

```python
import math

import jax
import jax.numpy as jnp
from jax import lax
from jax.sharding import PartitionSpec as P

VF = 12800
HEAD = 128
CAPD = 32
GROUP = 4


ln_eps = 1e-05
rms_eps = 1e-06
rope_base = 1000000.0
masked_score = -1e30


def shifted(x, axis, by):
    peers = lax.axis_size(axis)
    pairs = [(i, i + by) for i in range(peers) if 0 <= i + by < peers]
    return lax.ppermute(x, axis, pairs)


def bit_of(axis, b):
    return (lax.axis_index(axis) // (1 << b)) % 2


def bit_pairs(axis, b):
    peers = lax.axis_size(axis)
    return [(i, i ^ (1 << b)) for i in range(peers)]


def xor_sum(x, axis, nbits):
    for b in range(nbits):
        x = x + lax.ppermute(x, axis, bit_pairs(axis, b))
    return x


def halving_scatter(x, axis, first, nbits, order):
    bits = list(range(nbits - 1, -1, -1))
    acc = x.astype(jnp.float32)
    for b in order:
        dim = first + bits.index(b)
        mine = bit_of(axis, b)
        keep = lax.dynamic_index_in_dim(acc, mine, axis=dim, keepdims=False)
        send = lax.dynamic_index_in_dim(acc, 1 - mine, axis=dim, keepdims=False)
        got = lax.ppermute(send.astype(jnp.bfloat16), axis, bit_pairs(axis, b))
        acc = keep + got.astype(jnp.float32)
        bits.remove(b)
    return acc


def doubling_gather(x, axis, nbits, order):
    acc = x
    done = []
    for b in order:
        mine = bit_of(axis, b)
        got = lax.ppermute(acc, axis, bit_pairs(axis, b))
        low = jnp.where(mine == 0, acc, got)
        high = jnp.where(mine == 0, got, acc)
        acc = jnp.stack([low, high])
        done.insert(0, b)
    rest = list(range(nbits, acc.ndim))
    return acc.transpose([done.index(b) for b in range(nbits - 1, -1, -1)] + rest)


def log2(n):
    return n.bit_length() - 1


def rope_tables(positions, head_width):
    half = head_width // 2
    frequency = rope_base ** (-(jnp.arange(half).astype(jnp.float32) * 2.0 / head_width))
    angle = positions.astype(jnp.float32)[:, None] * frequency[None, :]
    return (jnp.cos(angle), jnp.sin(angle))


def rotate(values, cosine, sine):
    half = values.shape[-1] // 2
    first = values[..., :half]
    second = values[..., half:]
    cos_rows = cosine[:, None, :]
    sin_rows = sine[:, None, :]
    return jnp.concatenate(
        [first * cos_rows - second * sin_rows, second * cos_rows + first * sin_rows], axis=-1
    )


def unrotate(grads, cosine, sine):
    half = grads.shape[-1] // 2
    first = grads[..., :half]
    second = grads[..., half:]
    cos_rows = cosine[:, None, :]
    sin_rows = sine[:, None, :]
    return jnp.concatenate(
        [first * cos_rows + second * sin_rows, second * cos_rows - first * sin_rows], axis=-1
    )


def norm_backward(rows, grads, gain):
    inv_rms = lax.rsqrt(jnp.mean(rows * rows, axis=1, keepdims=True) + rms_eps)
    scaled = grads * gain[None, :]
    inner = jnp.mean(rows * scaled, axis=1, keepdims=True)
    return inv_rms * scaled - rows * (inv_rms * inv_rms * inv_rms) * inner


def attention_block(queries, keys, values, grads, allowed):
    scale = 1.0 / math.sqrt(queries.shape[-1])
    scores = jnp.einsum("qhgd,khd->hgqk", queries, keys, preferred_element_type=jnp.float32) * scale
    masked = jnp.where(allowed[None, None], scores, masked_score)
    peak = jnp.max(masked, axis=-1, keepdims=True)
    raised = jnp.where(allowed[None, None], jnp.exp(masked - peak), 0.0)
    shares = raised / jnp.sum(raised, axis=-1, keepdims=True)
    shares_low = shares.astype(jnp.bfloat16)
    context = jnp.einsum(
        "hgqk,khd->qhgd", shares_low, values, preferred_element_type=jnp.float32
    ).astype(jnp.bfloat16)
    share_grads = jnp.einsum("qhgd,khd->hgqk", grads, values, preferred_element_type=jnp.float32)
    delta = jnp.sum(shares * share_grads, axis=-1, keepdims=True)
    score_grads = (shares * (share_grads - delta) * scale).astype(jnp.bfloat16)
    query_grads = jnp.einsum(
        "hgqk,khd->qhgd", score_grads, keys, preferred_element_type=jnp.float32
    )
    key_grads = jnp.einsum(
        "hgqk,qhgd->khd", score_grads, queries, preferred_element_type=jnp.float32
    )
    value_grads = jnp.einsum(
        "hgqk,qhgd->khd", shares_low, grads, preferred_element_type=jnp.float32
    )
    return (context, query_grads, key_grads, value_grads)


def on_device(
    vis_feat,
    ln_gain,
    proj_weight,
    text_embed,
    rms_gain,
    wq,
    wk,
    wv,
    doc_ids,
    vis_slot,
    slot_token,
    token_slot,
    cotangent,
):
    seq_count = lax.axis_size("seq")
    my_index = lax.axis_index("seq")
    tok_rows = text_embed.shape[0]
    slot_cols = proj_weight.shape[1]
    features = vis_feat.astype(jnp.float32)
    tp_count = lax.axis_size("tp")
    tp_bits = log2(tp_count)
    seq_bits = log2(seq_count)
    row_total, row_squares = xor_sum(
        jnp.stack([jnp.sum(features, axis=1), jnp.sum(features * features, axis=1)]), "tp", tp_bits
    )
    row_mean = row_total / VF
    row_var = row_squares / VF - row_mean * row_mean
    inv_std = lax.rsqrt(row_var + ln_eps)
    centred = (features - row_mean[:, None]) * inv_std[:, None]
    vis_normed = (centred * ln_gain[None, :]).astype(jnp.bfloat16)
    all_normed = doubling_gather(vis_normed, "seq", seq_bits, list(range(seq_bits - 1, -1, -1)))
    partial_embed = jnp.dot(
        all_normed.reshape(seq_count * vis_feat.shape[0], vis_feat.shape[1]),
        proj_weight,
        preferred_element_type=jnp.float32,
    )
    slot_live = (slot_token >= 0)[:, None]
    slot_index = jnp.maximum(slot_token, 0)
    vis_total = partial_embed.shape[0]
    embed_part = halving_scatter(
        partial_embed.reshape([2] * tp_bits + [vis_total // tp_count, slot_cols]),
        "tp", 0, tp_bits, list(range(tp_bits)),
    ).astype(jnp.bfloat16)
    summed = doubling_gather(embed_part, "tp", tp_bits, list(range(tp_bits - 1, -1, -1))).reshape(
        vis_total, slot_cols
    )
    embed_rows = jnp.take(summed.astype(jnp.bfloat16), slot_index, axis=0)
    outgoing = jnp.where(slot_live, embed_rows, jnp.zeros_like(embed_rows)).reshape(
        seq_count, CAPD, slot_cols
    )
    arrived = lax.all_to_all(outgoing, "seq", split_axis=0, concat_axis=2, tiled=True)[0]
    lanes = jnp.arange(CAPD, dtype=jnp.int32)
    one_hot = (vis_slot[:, None] == lanes[None, :]).astype(jnp.bfloat16)
    placed = jnp.dot(one_hot, arrived, preferred_element_type=jnp.float32).astype(jnp.bfloat16)
    is_image = vis_slot >= 0
    hidden = jnp.where(is_image[:, None], placed, text_embed)
    hidden_wide = hidden.astype(jnp.float32)
    inv_rms = lax.rsqrt(jnp.mean(hidden_wide * hidden_wide, axis=1, keepdims=True) + rms_eps)
    normed = (hidden_wide * inv_rms * rms_gain[None, :]).astype(jnp.bfloat16)
    stacked = jnp.concatenate([wq, wk, wv], axis=1)
    query_cols = wq.shape[1]
    key_cols = wk.shape[1]
    gathered = lax.all_gather(stacked, "seq", axis=0, tiled=True)
    projected = jnp.dot(normed, gathered, preferred_element_type=jnp.float32)
    local_heads = query_cols // HEAD
    local_groups = key_cols // HEAD
    positions = my_index * tok_rows + jnp.arange(tok_rows, dtype=jnp.int32)
    cosine, sine = rope_tables(positions, HEAD)
    queries = rotate(
        projected[:, :query_cols].reshape(tok_rows, local_heads, HEAD), cosine, sine
    ).astype(jnp.bfloat16)
    keys = rotate(
        projected[:, query_cols : query_cols + key_cols].reshape(tok_rows, local_groups, HEAD),
        cosine,
        sine,
    ).astype(jnp.bfloat16)
    values = (
        projected[:, query_cols + key_cols :]
        .astype(jnp.bfloat16)
        .reshape(tok_rows, local_groups, HEAD)
    )
    doc_marks = (doc_ids + 1).astype(jnp.bfloat16)
    prev_keys, prev_values, prev_docs = shifted((keys, values, doc_marks), "seq", 1)
    all_keys = jnp.concatenate([prev_keys, keys], axis=0)
    all_values = jnp.concatenate([prev_values, values], axis=0)
    query_docs = doc_marks.astype(jnp.float32)
    key_docs = jnp.concatenate([prev_docs.astype(jnp.float32), query_docs], axis=0)
    key_positions = jnp.concatenate([positions - tok_rows, positions], axis=0)
    allowed = (key_docs[None, :] == query_docs[:, None]) & (
        key_positions[None, :] <= positions[:, None]
    )
    grads = cotangent.reshape(tok_rows, local_groups, GROUP, HEAD)
    context, query_grads, key_grads, value_grads = attention_block(
        queries.reshape(tok_rows, local_groups, GROUP, HEAD), all_keys, all_values, grads, allowed
    )
    back_keys, back_values = (
        shifted(key_grads[:tok_rows].astype(jnp.bfloat16), "seq", -1).astype(jnp.float32),
        shifted(value_grads[:tok_rows].astype(jnp.bfloat16), "seq", -1).astype(jnp.float32),
    )
    key_total = key_grads[tok_rows:] + back_keys
    value_total = value_grads[tok_rows:] + back_values
    query_pre = (
        unrotate(query_grads.reshape(tok_rows, local_heads, HEAD), cosine, sine)
        .astype(jnp.bfloat16)
        .reshape(tok_rows, query_cols)
    )
    key_pre = unrotate(key_total, cosine, sine).astype(jnp.bfloat16).reshape(tok_rows, key_cols)
    value_pre = value_total.astype(jnp.bfloat16).reshape(tok_rows, key_cols)
    proj_grads = jnp.concatenate([query_pre, key_pre, value_pre], axis=1)
    selected = lax.dot_general(
        one_hot, proj_grads, (((0,), (0,)), ((), ())), preferred_element_type=jnp.float32
    ).astype(jnp.bfloat16)
    width = gathered.shape[0]
    norm_part = jnp.einsum(
        "sc,kdc->ksd",
        selected,
        gathered.reshape(tp_count, width // tp_count, gathered.shape[1]),
        preferred_element_type=jnp.float32,
    )
    norm_block = halving_scatter(
        norm_part.reshape([2] * tp_bits + list(norm_part.shape[1:])),
        "tp", 0, tp_bits, list(range(tp_bits)),
    ).astype(jnp.bfloat16)
    norm_grads = (
        doubling_gather(norm_block, "tp", tp_bits, list(range(tp_bits - 1, -1, -1)))
        .reshape(tp_count, CAPD, width // tp_count)
        .transpose(1, 0, 2)
        .reshape(CAPD, width)
        .astype(jnp.float32)
    )
    embed_grads = norm_backward(arrived.astype(jnp.float32), norm_grads, rms_gain).astype(
        jnp.bfloat16
    )
    by_owner = embed_grads.reshape(CAPD, seq_count, slot_cols).transpose(1, 0, 2)
    returned = lax.all_to_all(by_owner, "seq", split_axis=0, concat_axis=0, tiled=True)
    token_grads = jnp.take(returned.reshape(seq_count * CAPD, slot_cols), token_slot, axis=0)
    own_rows = vis_feat.shape[0]
    feature_part = lax.dot_general(
        token_grads, proj_weight, (((1,), (1,)), ((), ())), preferred_element_type=jnp.float32
    )
    feature_grads = halving_scatter(
        feature_part.reshape([2] * seq_bits + [own_rows, feature_part.shape[1]]),
        "seq", 0, seq_bits, list(range(seq_bits)),
    )
    scaled = feature_grads * ln_gain[None, :]
    grad_total, grad_inner = xor_sum(
        jnp.stack([jnp.sum(scaled, axis=1), jnp.sum(scaled * centred, axis=1)]), "tp", tp_bits
    )
    vis_grad = (
        inv_std[:, None]
        * (scaled - (grad_total / VF)[:, None] - centred * (grad_inner / VF)[:, None])
    ).astype(jnp.bfloat16)
    return (context.reshape(tok_rows, query_cols), vis_grad)


def solution(mesh):
    return jax.shard_map(
        on_device,
        mesh=mesh,
        in_specs=(
            P("seq", "tp"),
            P("tp"),
            P("tp", "seq"),
            P("seq", None),
            P(),
            P("seq", "tp"),
            P("seq", "tp"),
            P("seq", "tp"),
            P("seq"),
            P("seq"),
            P(),
            P(),
            P("seq", "tp"),
        ),
        out_specs=(P("seq", "tp"), P("seq", "tp")),
        check_vma=False,
    )
```

```python
import math

import jax
import jax.numpy as jnp
from jax import lax
from jax.sharding import PartitionSpec as P

VF = 12800
HEAD = 128
CAPD = 32
GROUP = 4


ln_eps = 1e-05
rms_eps = 1e-06
rope_base = 1000000.0
masked_score = -1e30


def shifted(x, axis, by):
    peers = lax.axis_size(axis)
    pairs = [(i, i + by) for i in range(peers) if 0 <= i + by < peers]
    return lax.ppermute(x, axis, pairs)


def bit_of(axis, b):
    return (lax.axis_index(axis) // (1 << b)) % 2


def bit_pairs(axis, b):
    peers = lax.axis_size(axis)
    return [(i, i ^ (1 << b)) for i in range(peers)]


def group_index(axis, bits):
    return sum(bit_of(axis, b) * (1 << k) for k, b in enumerate(bits))


def group_pairs(axis, bits, o):
    peers = lax.axis_size(axis)
    mask = sum(((o >> k) & 1) << b for k, b in enumerate(bits))
    return [(i, i ^ mask) for i in range(peers)]


def group_scatter(x, axis, bits, dim=0):
    me = group_index(axis, bits)
    acc = lax.dynamic_index_in_dim(x, me, dim, keepdims=False).astype(jnp.float32)
    for o in range(1, 1 << len(bits)):
        send = lax.dynamic_index_in_dim(x, jnp.bitwise_xor(me, o), dim, keepdims=False)
        got = lax.ppermute(send.astype(jnp.bfloat16), axis, group_pairs(axis, bits, o))
        acc = acc + got.astype(jnp.float32)
    return acc


def group_gather(x, axis, bits):
    me = group_index(axis, bits)
    g = 1 << len(bits)
    parts = [x] + [lax.ppermute(x, axis, group_pairs(axis, bits, o)) for o in range(1, g)]
    order = jnp.bitwise_xor(jnp.arange(g, dtype=jnp.int32), me)
    return jnp.take(jnp.stack(parts), order, axis=0)


def staged_scatter(x, axis, groups):
    acc = x
    for bits in groups:
        g = 1 << len(bits)
        lead = acc.reshape((acc.shape[0] // g, g) + acc.shape[1:])
        acc = group_scatter(lead, axis, bits, dim=1)
    return acc[0]


def staged_gather(x, axis, groups):
    acc = x
    for bits in groups:
        acc = group_gather(acc, axis, bits)
    count = len(groups)
    return acc.transpose(list(range(count - 1, -1, -1)) + list(range(count, acc.ndim)))


def log2(n):
    return n.bit_length() - 1


def rope_tables(positions, head_width):
    half = head_width // 2
    frequency = rope_base ** (-(jnp.arange(half).astype(jnp.float32) * 2.0 / head_width))
    angle = positions.astype(jnp.float32)[:, None] * frequency[None, :]
    return (jnp.cos(angle), jnp.sin(angle))


def rotate(values, cosine, sine):
    half = values.shape[-1] // 2
    first = values[..., :half]
    second = values[..., half:]
    cos_rows = cosine[:, None, :]
    sin_rows = sine[:, None, :]
    return jnp.concatenate(
        [first * cos_rows - second * sin_rows, second * cos_rows + first * sin_rows], axis=-1
    )


def unrotate(grads, cosine, sine):
    half = grads.shape[-1] // 2
    first = grads[..., :half]
    second = grads[..., half:]
    cos_rows = cosine[:, None, :]
    sin_rows = sine[:, None, :]
    return jnp.concatenate(
        [first * cos_rows + second * sin_rows, second * cos_rows - first * sin_rows], axis=-1
    )


def norm_backward(rows, grads, gain):
    inv_rms = lax.rsqrt(jnp.mean(rows * rows, axis=1, keepdims=True) + rms_eps)
    scaled = grads * gain[None, :]
    inner = jnp.mean(rows * scaled, axis=1, keepdims=True)
    return inv_rms * scaled - rows * (inv_rms * inv_rms * inv_rms) * inner


def attention_block(queries, keys, values, grads, allowed):
    scale = 1.0 / math.sqrt(queries.shape[-1])
    scores = jnp.einsum("qhgd,khd->hgqk", queries, keys, preferred_element_type=jnp.float32) * scale
    masked = jnp.where(allowed[None, None], scores, masked_score)
    peak = jnp.max(masked, axis=-1, keepdims=True)
    raised = jnp.where(allowed[None, None], jnp.exp(masked - peak), 0.0)
    shares = raised / jnp.sum(raised, axis=-1, keepdims=True)
    shares_low = shares.astype(jnp.bfloat16)
    context = jnp.einsum(
        "hgqk,khd->qhgd", shares_low, values, preferred_element_type=jnp.float32
    ).astype(jnp.bfloat16)
    share_grads = jnp.einsum("qhgd,khd->hgqk", grads, values, preferred_element_type=jnp.float32)
    delta = jnp.sum(shares * share_grads, axis=-1, keepdims=True)
    score_grads = (shares * (share_grads - delta) * scale).astype(jnp.bfloat16)
    query_grads = jnp.einsum(
        "hgqk,khd->qhgd", score_grads, keys, preferred_element_type=jnp.float32
    )
    key_grads = jnp.einsum(
        "hgqk,qhgd->khd", score_grads, queries, preferred_element_type=jnp.float32
    )
    value_grads = jnp.einsum(
        "hgqk,qhgd->khd", shares_low, grads, preferred_element_type=jnp.float32
    )
    return (context, query_grads, key_grads, value_grads)


def on_device(
    vis_feat,
    ln_gain,
    proj_weight,
    text_embed,
    rms_gain,
    wq,
    wk,
    wv,
    doc_ids,
    vis_slot,
    slot_token,
    token_slot,
    cotangent,
):
    seq_count = lax.axis_size("seq")
    my_index = lax.axis_index("seq")
    tok_rows = text_embed.shape[0]
    slot_cols = proj_weight.shape[1]
    features = vis_feat.astype(jnp.float32)
    tp_count = lax.axis_size("tp")
    tp_bits = log2(tp_count)
    seq_bits = log2(seq_count)
    tp_all = [list(range(tp_bits))]
    seq_up = [[0], [1, 2], [3, 4]] if seq_bits == 5 else [[b] for b in range(seq_bits)]
    seq_down = seq_up[::-1]
    row_total, row_squares = jnp.sum(
        staged_gather(
            jnp.stack([jnp.sum(features, axis=1), jnp.sum(features * features, axis=1)]),
            "tp", tp_all,
        ),
        axis=0,
    )
    row_mean = row_total / VF
    row_var = row_squares / VF - row_mean * row_mean
    inv_std = lax.rsqrt(row_var + ln_eps)
    centred = (features - row_mean[:, None]) * inv_std[:, None]
    vis_normed = (centred * ln_gain[None, :]).astype(jnp.bfloat16)
    all_normed = staged_gather(vis_normed, "seq", seq_down)
    partial_embed = jnp.dot(
        all_normed.reshape(seq_count * vis_feat.shape[0], vis_feat.shape[1]),
        proj_weight,
        preferred_element_type=jnp.float32,
    )
    slot_live = (slot_token >= 0)[:, None]
    slot_index = jnp.maximum(slot_token, 0)
    vis_total = partial_embed.shape[0]
    embed_part = staged_scatter(
        partial_embed.reshape(tp_count, vis_total // tp_count, slot_cols), "tp", tp_all
    ).astype(jnp.bfloat16)
    summed = staged_gather(embed_part, "tp", tp_all).reshape(vis_total, slot_cols)
    embed_rows = jnp.take(summed.astype(jnp.bfloat16), slot_index, axis=0)
    outgoing = jnp.where(slot_live, embed_rows, jnp.zeros_like(embed_rows)).reshape(
        seq_count, CAPD, slot_cols
    )
    arrived = lax.all_to_all(outgoing, "seq", split_axis=0, concat_axis=2, tiled=True)[0]
    lanes = jnp.arange(CAPD, dtype=jnp.int32)
    one_hot = (vis_slot[:, None] == lanes[None, :]).astype(jnp.bfloat16)
    placed = jnp.dot(one_hot, arrived, preferred_element_type=jnp.float32).astype(jnp.bfloat16)
    is_image = vis_slot >= 0
    hidden = jnp.where(is_image[:, None], placed, text_embed)
    hidden_wide = hidden.astype(jnp.float32)
    inv_rms = lax.rsqrt(jnp.mean(hidden_wide * hidden_wide, axis=1, keepdims=True) + rms_eps)
    normed = (hidden_wide * inv_rms * rms_gain[None, :]).astype(jnp.bfloat16)
    stacked = jnp.concatenate([wq, wk, wv], axis=1)
    query_cols = wq.shape[1]
    key_cols = wk.shape[1]
    gathered = lax.all_gather(stacked, "seq", axis=0, tiled=True)
    projected = jnp.dot(normed, gathered, preferred_element_type=jnp.float32)
    local_heads = query_cols // HEAD
    local_groups = key_cols // HEAD
    positions = my_index * tok_rows + jnp.arange(tok_rows, dtype=jnp.int32)
    cosine, sine = rope_tables(positions, HEAD)
    queries = rotate(
        projected[:, :query_cols].reshape(tok_rows, local_heads, HEAD), cosine, sine
    ).astype(jnp.bfloat16)
    keys = rotate(
        projected[:, query_cols : query_cols + key_cols].reshape(tok_rows, local_groups, HEAD),
        cosine,
        sine,
    ).astype(jnp.bfloat16)
    values = (
        projected[:, query_cols + key_cols :]
        .astype(jnp.bfloat16)
        .reshape(tok_rows, local_groups, HEAD)
    )
    doc_marks = (doc_ids + 1).astype(jnp.bfloat16)
    prev_keys, prev_values, prev_docs = shifted((keys, values, doc_marks), "seq", 1)
    all_keys = jnp.concatenate([prev_keys, keys], axis=0)
    all_values = jnp.concatenate([prev_values, values], axis=0)
    query_docs = doc_marks.astype(jnp.float32)
    key_docs = jnp.concatenate([prev_docs.astype(jnp.float32), query_docs], axis=0)
    key_positions = jnp.concatenate([positions - tok_rows, positions], axis=0)
    allowed = (key_docs[None, :] == query_docs[:, None]) & (
        key_positions[None, :] <= positions[:, None]
    )
    grads = cotangent.reshape(tok_rows, local_groups, GROUP, HEAD)
    context, query_grads, key_grads, value_grads = attention_block(
        queries.reshape(tok_rows, local_groups, GROUP, HEAD), all_keys, all_values, grads, allowed
    )
    back_keys, back_values = (
        shifted(key_grads[:tok_rows].astype(jnp.bfloat16), "seq", -1).astype(jnp.float32),
        shifted(value_grads[:tok_rows].astype(jnp.bfloat16), "seq", -1).astype(jnp.float32),
    )
    key_total = key_grads[tok_rows:] + back_keys
    value_total = value_grads[tok_rows:] + back_values
    query_pre = (
        unrotate(query_grads.reshape(tok_rows, local_heads, HEAD), cosine, sine)
        .astype(jnp.bfloat16)
        .reshape(tok_rows, query_cols)
    )
    key_pre = unrotate(key_total, cosine, sine).astype(jnp.bfloat16).reshape(tok_rows, key_cols)
    value_pre = value_total.astype(jnp.bfloat16).reshape(tok_rows, key_cols)
    proj_grads = jnp.concatenate([query_pre, key_pre, value_pre], axis=1)
    selected = lax.dot_general(
        one_hot, proj_grads, (((0,), (0,)), ((), ())), preferred_element_type=jnp.float32
    ).astype(jnp.bfloat16)
    width = gathered.shape[0]
    norm_part = jnp.einsum(
        "sc,kdc->ksd",
        selected,
        gathered.reshape(tp_count, width // tp_count, gathered.shape[1]),
        preferred_element_type=jnp.float32,
    )
    norm_block = staged_scatter(norm_part, "tp", tp_all).astype(jnp.bfloat16)
    norm_grads = (
        staged_gather(norm_block, "tp", tp_all)
        .reshape(tp_count, CAPD, width // tp_count)
        .transpose(1, 0, 2)
        .reshape(CAPD, width)
        .astype(jnp.float32)
    )
    embed_grads = norm_backward(arrived.astype(jnp.float32), norm_grads, rms_gain).astype(
        jnp.bfloat16
    )
    by_owner = embed_grads.reshape(CAPD, seq_count, slot_cols).transpose(1, 0, 2)
    returned = lax.all_to_all(by_owner, "seq", split_axis=0, concat_axis=0, tiled=True)
    token_grads = jnp.take(returned.reshape(seq_count * CAPD, slot_cols), token_slot, axis=0)
    own_rows = vis_feat.shape[0]
    feature_part = lax.dot_general(
        token_grads, proj_weight, (((1,), (1,)), ((), ())), preferred_element_type=jnp.float32
    )
    feature_grads = staged_scatter(
        feature_part.reshape(seq_count, own_rows, feature_part.shape[1]), "seq", seq_up
    )
    scaled = feature_grads * ln_gain[None, :]
    grad_total, grad_inner = jnp.sum(
        staged_gather(
            jnp.stack([jnp.sum(scaled, axis=1), jnp.sum(scaled * centred, axis=1)]), "tp", tp_all
        ),
        axis=0,
    )
    vis_grad = (
        inv_std[:, None]
        * (scaled - (grad_total / VF)[:, None] - centred * (grad_inner / VF)[:, None])
    ).astype(jnp.bfloat16)
    return (context.reshape(tok_rows, query_cols), vis_grad)


def solution(mesh):
    return jax.shard_map(
        on_device,
        mesh=mesh,
        in_specs=(
            P("seq", "tp"),
            P("tp"),
            P("tp", "seq"),
            P("seq", None),
            P(),
            P("seq", "tp"),
            P("seq", "tp"),
            P("seq", "tp"),
            P("seq"),
            P("seq"),
            P(),
            P(),
            P("seq", "tp"),
        ),
        out_specs=(P("seq", "tp"), P("seq", "tp")),
        check_vma=False,
    )
```

```python
import math

import jax
import jax.numpy as jnp
from jax import lax
from jax.sharding import PartitionSpec as P

VF = 12800
HEAD = 128
CAPD = 32
GROUP = 4


ln_eps = 1e-05
rms_eps = 1e-06
rope_base = 1000000.0
masked_score = -1e30


def shifted(x, axis, by):
    peers = lax.axis_size(axis)
    pairs = [(i, i + by) for i in range(peers) if 0 <= i + by < peers]
    return lax.ppermute(x, axis, pairs)


def bit_of(axis, b):
    return (lax.axis_index(axis) // (1 << b)) % 2


def bit_pairs(axis, b):
    peers = lax.axis_size(axis)
    return [(i, i ^ (1 << b)) for i in range(peers)]


def group_index(axis, bits):
    return sum(bit_of(axis, b) * (1 << k) for k, b in enumerate(bits))


def group_pairs(axis, bits, o):
    peers = lax.axis_size(axis)
    mask = sum(((o >> k) & 1) << b for k, b in enumerate(bits))
    return [(i, i ^ mask) for i in range(peers)]


def group_scatter(x, axis, bits, dim=0):
    me = group_index(axis, bits)
    acc = lax.dynamic_index_in_dim(x, me, dim, keepdims=False).astype(jnp.float32)
    for o in range(1, 1 << len(bits)):
        send = lax.dynamic_index_in_dim(x, jnp.bitwise_xor(me, o), dim, keepdims=False)
        got = lax.ppermute(send.astype(jnp.bfloat16), axis, group_pairs(axis, bits, o))
        acc = acc + got.astype(jnp.float32)
    return acc


def group_gather(x, axis, bits):
    me = group_index(axis, bits)
    g = 1 << len(bits)
    parts = [x] + [lax.ppermute(x, axis, group_pairs(axis, bits, o)) for o in range(1, g)]
    order = jnp.bitwise_xor(jnp.arange(g, dtype=jnp.int32), me)
    return jnp.take(jnp.stack(parts), order, axis=0)


def staged_scatter(x, axis, groups):
    acc = x
    for bits in groups:
        g = 1 << len(bits)
        lead = acc.reshape((acc.shape[0] // g, g) + acc.shape[1:])
        acc = group_scatter(lead, axis, bits, dim=1)
    return acc[0]


def staged_gather(x, axis, groups):
    acc = x
    for bits in groups:
        acc = group_gather(acc, axis, bits)
    count = len(groups)
    return acc.transpose(list(range(count - 1, -1, -1)) + list(range(count, acc.ndim)))


def exchange_sum(x, axis):
    got = lax.all_to_all(x.astype(jnp.bfloat16), axis, 0, 0, tiled=True)
    return jnp.sum(got.astype(jnp.float32), axis=0)


def exchange_gather(x, axis):
    peers = lax.axis_size(axis)
    return lax.all_to_all(jnp.broadcast_to(x[None], (peers,) + x.shape), axis, 0, 0, tiled=True)


def log2(n):
    return n.bit_length() - 1


def rope_tables(positions, head_width):
    half = head_width // 2
    frequency = rope_base ** (-(jnp.arange(half).astype(jnp.float32) * 2.0 / head_width))
    angle = positions.astype(jnp.float32)[:, None] * frequency[None, :]
    return (jnp.cos(angle), jnp.sin(angle))


def rotate(values, cosine, sine):
    half = values.shape[-1] // 2
    first = values[..., :half]
    second = values[..., half:]
    cos_rows = cosine[:, None, :]
    sin_rows = sine[:, None, :]
    return jnp.concatenate(
        [first * cos_rows - second * sin_rows, second * cos_rows + first * sin_rows], axis=-1
    )


def unrotate(grads, cosine, sine):
    half = grads.shape[-1] // 2
    first = grads[..., :half]
    second = grads[..., half:]
    cos_rows = cosine[:, None, :]
    sin_rows = sine[:, None, :]
    return jnp.concatenate(
        [first * cos_rows + second * sin_rows, second * cos_rows - first * sin_rows], axis=-1
    )


def norm_backward(rows, grads, gain):
    inv_rms = lax.rsqrt(jnp.mean(rows * rows, axis=1, keepdims=True) + rms_eps)
    scaled = grads * gain[None, :]
    inner = jnp.mean(rows * scaled, axis=1, keepdims=True)
    return inv_rms * scaled - rows * (inv_rms * inv_rms * inv_rms) * inner


def attention_block(queries, keys, values, grads, allowed):
    scale = 1.0 / math.sqrt(queries.shape[-1])
    scores = jnp.einsum("qhgd,khd->hgqk", queries, keys, preferred_element_type=jnp.float32) * scale
    masked = jnp.where(allowed[None, None], scores, masked_score)
    peak = jnp.max(masked, axis=-1, keepdims=True)
    raised = jnp.where(allowed[None, None], jnp.exp(masked - peak), 0.0)
    shares = raised / jnp.sum(raised, axis=-1, keepdims=True)
    shares_low = shares.astype(jnp.bfloat16)
    context = jnp.einsum(
        "hgqk,khd->qhgd", shares_low, values, preferred_element_type=jnp.float32
    ).astype(jnp.bfloat16)
    share_grads = jnp.einsum("qhgd,khd->hgqk", grads, values, preferred_element_type=jnp.float32)
    delta = jnp.sum(shares * share_grads, axis=-1, keepdims=True)
    score_grads = (shares * (share_grads - delta) * scale).astype(jnp.bfloat16)
    query_grads = jnp.einsum(
        "hgqk,khd->qhgd", score_grads, keys, preferred_element_type=jnp.float32
    )
    key_grads = jnp.einsum(
        "hgqk,qhgd->khd", score_grads, queries, preferred_element_type=jnp.float32
    )
    value_grads = jnp.einsum(
        "hgqk,qhgd->khd", shares_low, grads, preferred_element_type=jnp.float32
    )
    return (context, query_grads, key_grads, value_grads)


def on_device(
    vis_feat,
    ln_gain,
    proj_weight,
    text_embed,
    rms_gain,
    wq,
    wk,
    wv,
    doc_ids,
    vis_slot,
    slot_token,
    token_slot,
    cotangent,
):
    seq_count = lax.axis_size("seq")
    my_index = lax.axis_index("seq")
    tok_rows = text_embed.shape[0]
    slot_cols = proj_weight.shape[1]
    features = vis_feat.astype(jnp.float32)
    tp_count = lax.axis_size("tp")
    tp_bits = log2(tp_count)
    seq_bits = log2(seq_count)
    tp_all = [list(range(tp_bits))]
    seq_up = [[0], [1, 2], [3, 4]] if seq_bits == 5 else [[b] for b in range(seq_bits)]
    seq_down = seq_up[::-1]
    row_total, row_squares = jnp.sum(
        exchange_gather(
            jnp.stack([jnp.sum(features, axis=1), jnp.sum(features * features, axis=1)]), "tp"
        ),
        axis=0,
    )
    row_mean = row_total / VF
    row_var = row_squares / VF - row_mean * row_mean
    inv_std = lax.rsqrt(row_var + ln_eps)
    centred = (features - row_mean[:, None]) * inv_std[:, None]
    vis_normed = (centred * ln_gain[None, :]).astype(jnp.bfloat16)
    all_normed = staged_gather(vis_normed, "seq", seq_down)
    partial_embed = jnp.dot(
        all_normed.reshape(seq_count * vis_feat.shape[0], vis_feat.shape[1]),
        proj_weight,
        preferred_element_type=jnp.float32,
    )
    slot_live = (slot_token >= 0)[:, None]
    slot_index = jnp.maximum(slot_token, 0)
    vis_total = partial_embed.shape[0]
    embed_part = exchange_sum(
        partial_embed.reshape(tp_count, vis_total // tp_count, slot_cols), "tp"
    ).astype(jnp.bfloat16)
    summed = exchange_gather(embed_part, "tp").reshape(vis_total, slot_cols)
    embed_rows = jnp.take(summed.astype(jnp.bfloat16), slot_index, axis=0)
    outgoing = jnp.where(slot_live, embed_rows, jnp.zeros_like(embed_rows)).reshape(
        seq_count, CAPD, slot_cols
    )
    arrived = lax.all_to_all(outgoing, "seq", split_axis=0, concat_axis=2, tiled=True)[0]
    lanes = jnp.arange(CAPD, dtype=jnp.int32)
    one_hot = (vis_slot[:, None] == lanes[None, :]).astype(jnp.bfloat16)
    placed = jnp.dot(one_hot, arrived, preferred_element_type=jnp.float32).astype(jnp.bfloat16)
    is_image = vis_slot >= 0
    hidden = jnp.where(is_image[:, None], placed, text_embed)
    hidden_wide = hidden.astype(jnp.float32)
    inv_rms = lax.rsqrt(jnp.mean(hidden_wide * hidden_wide, axis=1, keepdims=True) + rms_eps)
    normed = (hidden_wide * inv_rms * rms_gain[None, :]).astype(jnp.bfloat16)
    stacked = jnp.concatenate([wq, wk, wv], axis=1)
    query_cols = wq.shape[1]
    key_cols = wk.shape[1]
    gathered = lax.all_gather(stacked, "seq", axis=0, tiled=True)
    projected = jnp.dot(normed, gathered, preferred_element_type=jnp.float32)
    local_heads = query_cols // HEAD
    local_groups = key_cols // HEAD
    positions = my_index * tok_rows + jnp.arange(tok_rows, dtype=jnp.int32)
    cosine, sine = rope_tables(positions, HEAD)
    queries = rotate(
        projected[:, :query_cols].reshape(tok_rows, local_heads, HEAD), cosine, sine
    ).astype(jnp.bfloat16)
    keys = rotate(
        projected[:, query_cols : query_cols + key_cols].reshape(tok_rows, local_groups, HEAD),
        cosine,
        sine,
    ).astype(jnp.bfloat16)
    values = (
        projected[:, query_cols + key_cols :]
        .astype(jnp.bfloat16)
        .reshape(tok_rows, local_groups, HEAD)
    )
    doc_marks = (doc_ids + 1).astype(jnp.bfloat16)
    prev_keys, prev_values, prev_docs = shifted((keys, values, doc_marks), "seq", 1)
    all_keys = jnp.concatenate([prev_keys, keys], axis=0)
    all_values = jnp.concatenate([prev_values, values], axis=0)
    query_docs = doc_marks.astype(jnp.float32)
    key_docs = jnp.concatenate([prev_docs.astype(jnp.float32), query_docs], axis=0)
    key_positions = jnp.concatenate([positions - tok_rows, positions], axis=0)
    allowed = (key_docs[None, :] == query_docs[:, None]) & (
        key_positions[None, :] <= positions[:, None]
    )
    grads = cotangent.reshape(tok_rows, local_groups, GROUP, HEAD)
    context, query_grads, key_grads, value_grads = attention_block(
        queries.reshape(tok_rows, local_groups, GROUP, HEAD), all_keys, all_values, grads, allowed
    )
    back_keys, back_values = (
        shifted(key_grads[:tok_rows].astype(jnp.bfloat16), "seq", -1).astype(jnp.float32),
        shifted(value_grads[:tok_rows].astype(jnp.bfloat16), "seq", -1).astype(jnp.float32),
    )
    key_total = key_grads[tok_rows:] + back_keys
    value_total = value_grads[tok_rows:] + back_values
    query_pre = (
        unrotate(query_grads.reshape(tok_rows, local_heads, HEAD), cosine, sine)
        .astype(jnp.bfloat16)
        .reshape(tok_rows, query_cols)
    )
    key_pre = unrotate(key_total, cosine, sine).astype(jnp.bfloat16).reshape(tok_rows, key_cols)
    value_pre = value_total.astype(jnp.bfloat16).reshape(tok_rows, key_cols)
    proj_grads = jnp.concatenate([query_pre, key_pre, value_pre], axis=1)
    selected = lax.dot_general(
        one_hot, proj_grads, (((0,), (0,)), ((), ())), preferred_element_type=jnp.float32
    ).astype(jnp.bfloat16)
    width = gathered.shape[0]
    norm_part = jnp.einsum(
        "sc,kdc->ksd",
        selected,
        gathered.reshape(tp_count, width // tp_count, gathered.shape[1]),
        preferred_element_type=jnp.float32,
    )
    norm_block = exchange_sum(norm_part, "tp").astype(jnp.bfloat16)
    norm_grads = (
        exchange_gather(norm_block, "tp")
        .reshape(tp_count, CAPD, width // tp_count)
        .transpose(1, 0, 2)
        .reshape(CAPD, width)
        .astype(jnp.float32)
    )
    embed_grads = norm_backward(arrived.astype(jnp.float32), norm_grads, rms_gain).astype(
        jnp.bfloat16
    )
    by_owner = embed_grads.reshape(CAPD, seq_count, slot_cols).transpose(1, 0, 2)
    returned = lax.all_to_all(by_owner, "seq", split_axis=0, concat_axis=0, tiled=True)
    token_grads = jnp.take(returned.reshape(seq_count * CAPD, slot_cols), token_slot, axis=0)
    own_rows = vis_feat.shape[0]
    feature_part = lax.dot_general(
        token_grads, proj_weight, (((1,), (1,)), ((), ())), preferred_element_type=jnp.float32
    )
    feature_grads = exchange_sum(
        feature_part.reshape(seq_count, own_rows, feature_part.shape[1]), "seq"
    )
    scaled = feature_grads * ln_gain[None, :]
    grad_total, grad_inner = jnp.sum(
        exchange_gather(
            jnp.stack([jnp.sum(scaled, axis=1), jnp.sum(scaled * centred, axis=1)]), "tp"
        ),
        axis=0,
    )
    vis_grad = (
        inv_std[:, None]
        * (scaled - (grad_total / VF)[:, None] - centred * (grad_inner / VF)[:, None])
    ).astype(jnp.bfloat16)
    return (context.reshape(tok_rows, query_cols), vis_grad)


def solution(mesh):
    return jax.shard_map(
        on_device,
        mesh=mesh,
        in_specs=(
            P("seq", "tp"),
            P("tp"),
            P("tp", "seq"),
            P("seq", None),
            P(),
            P("seq", "tp"),
            P("seq", "tp"),
            P("seq", "tp"),
            P("seq"),
            P("seq"),
            P(),
            P(),
            P("seq", "tp"),
        ),
        out_specs=(P("seq", "tp"), P("seq", "tp")),
        check_vma=False,
    )
```

```python
import math

import jax
import jax.numpy as jnp
from jax import lax
from jax.sharding import PartitionSpec as P

VF = 12800
HEAD = 128
CAPD = 32
GROUP = 4


ln_eps = 1e-05
rms_eps = 1e-06
rope_base = 1000000.0
masked_score = -1e30


def shifted(x, axis, by):
    peers = lax.axis_size(axis)
    pairs = [(i, i + by) for i in range(peers) if 0 <= i + by < peers]
    return lax.ppermute(x, axis, pairs)


def bit_of(axis, b):
    return (lax.axis_index(axis) // (1 << b)) % 2


def bit_pairs(axis, b):
    peers = lax.axis_size(axis)
    return [(i, i ^ (1 << b)) for i in range(peers)]


def group_index(axis, bits):
    return sum(bit_of(axis, b) * (1 << k) for k, b in enumerate(bits))


def group_pairs(axis, bits, o):
    peers = lax.axis_size(axis)
    mask = sum(((o >> k) & 1) << b for k, b in enumerate(bits))
    return [(i, i ^ mask) for i in range(peers)]


def group_scatter(x, axis, bits, dim=0):
    me = group_index(axis, bits)
    acc = lax.dynamic_index_in_dim(x, me, dim, keepdims=False).astype(jnp.float32)
    for o in range(1, 1 << len(bits)):
        send = lax.dynamic_index_in_dim(x, jnp.bitwise_xor(me, o), dim, keepdims=False)
        got = lax.ppermute(send.astype(jnp.bfloat16), axis, group_pairs(axis, bits, o))
        acc = acc + got.astype(jnp.float32)
    return acc


def group_gather(x, axis, bits):
    me = group_index(axis, bits)
    g = 1 << len(bits)
    parts = [x] + [lax.ppermute(x, axis, group_pairs(axis, bits, o)) for o in range(1, g)]
    order = jnp.bitwise_xor(jnp.arange(g, dtype=jnp.int32), me)
    return jnp.take(jnp.stack(parts), order, axis=0)


def staged_scatter(x, axis, groups):
    acc = x
    for bits in groups:
        g = 1 << len(bits)
        lead = acc.reshape((acc.shape[0] // g, g) + acc.shape[1:])
        acc = group_scatter(lead, axis, bits, dim=1)
    return acc[0]


def staged_gather(x, axis, groups):
    acc = x
    for bits in groups:
        acc = group_gather(acc, axis, bits)
    count = len(groups)
    return acc.transpose(list(range(count - 1, -1, -1)) + list(range(count, acc.ndim)))


def exchange_sum(x, axis):
    got = lax.all_to_all(x.astype(jnp.bfloat16), axis, 0, 0, tiled=True)
    return jnp.sum(got.astype(jnp.float32), axis=0)


def exchange_gather(x, axis):
    peers = lax.axis_size(axis)
    return lax.all_to_all(jnp.broadcast_to(x[None], (peers,) + x.shape), axis, 0, 0, tiled=True)


def log2(n):
    return n.bit_length() - 1


def rope_tables(positions, head_width):
    half = head_width // 2
    frequency = rope_base ** (-(jnp.arange(half).astype(jnp.float32) * 2.0 / head_width))
    angle = positions.astype(jnp.float32)[:, None] * frequency[None, :]
    return (jnp.cos(angle), jnp.sin(angle))


def rotate(values, cosine, sine):
    half = values.shape[-1] // 2
    first = values[..., :half]
    second = values[..., half:]
    cos_rows = cosine[:, None, :]
    sin_rows = sine[:, None, :]
    return jnp.concatenate(
        [first * cos_rows - second * sin_rows, second * cos_rows + first * sin_rows], axis=-1
    )


def unrotate(grads, cosine, sine):
    half = grads.shape[-1] // 2
    first = grads[..., :half]
    second = grads[..., half:]
    cos_rows = cosine[:, None, :]
    sin_rows = sine[:, None, :]
    return jnp.concatenate(
        [first * cos_rows + second * sin_rows, second * cos_rows - first * sin_rows], axis=-1
    )


def norm_backward(rows, grads, gain):
    inv_rms = lax.rsqrt(jnp.mean(rows * rows, axis=1, keepdims=True) + rms_eps)
    scaled = grads * gain[None, :]
    inner = jnp.mean(rows * scaled, axis=1, keepdims=True)
    return inv_rms * scaled - rows * (inv_rms * inv_rms * inv_rms) * inner


def attention_block(queries, keys, values, grads, allowed):
    scale = 1.0 / math.sqrt(queries.shape[-1])
    scores = jnp.einsum("qhgd,khd->hgqk", queries, keys, preferred_element_type=jnp.float32) * scale
    masked = jnp.where(allowed[None, None], scores, masked_score)
    peak = jnp.max(masked, axis=-1, keepdims=True)
    raised = jnp.where(allowed[None, None], jnp.exp(masked - peak), 0.0)
    shares = raised / jnp.sum(raised, axis=-1, keepdims=True)
    shares_low = shares.astype(jnp.bfloat16)
    context = jnp.einsum(
        "hgqk,khd->qhgd", shares_low, values, preferred_element_type=jnp.float32
    ).astype(jnp.bfloat16)
    share_grads = jnp.einsum("qhgd,khd->hgqk", grads, values, preferred_element_type=jnp.float32)
    delta = jnp.sum(shares * share_grads, axis=-1, keepdims=True)
    score_grads = (shares * (share_grads - delta) * scale).astype(jnp.bfloat16)
    query_grads = jnp.einsum(
        "hgqk,khd->qhgd", score_grads, keys, preferred_element_type=jnp.float32
    )
    key_grads = jnp.einsum(
        "hgqk,qhgd->khd", score_grads, queries, preferred_element_type=jnp.float32
    )
    value_grads = jnp.einsum(
        "hgqk,qhgd->khd", shares_low, grads, preferred_element_type=jnp.float32
    )
    return (context, query_grads, key_grads, value_grads)


def on_device(
    vis_feat,
    ln_gain,
    proj_weight,
    text_embed,
    rms_gain,
    wq,
    wk,
    wv,
    doc_ids,
    vis_slot,
    slot_token,
    token_slot,
    cotangent,
):
    seq_count = lax.axis_size("seq")
    my_index = lax.axis_index("seq")
    tok_rows = text_embed.shape[0]
    slot_cols = proj_weight.shape[1]
    features = vis_feat.astype(jnp.float32)
    tp_count = lax.axis_size("tp")
    tp_bits = log2(tp_count)
    seq_bits = log2(seq_count)
    tp_all = [list(range(tp_bits))]
    seq_up = [[0], [1, 2], [3, 4]] if seq_bits == 5 else [[b] for b in range(seq_bits)]
    seq_down = seq_up[::-1]
    own_rows = vis_feat.shape[0]
    devices = seq_count * tp_count
    local_stats = jnp.stack([jnp.sum(features, axis=1), jnp.sum(features * features, axis=1)])
    every_stats = lax.all_to_all(
        jnp.broadcast_to(local_stats[None], (devices,) + local_stats.shape),
        ("seq", "tp"), 0, 0, tiled=True,
    ).reshape(seq_count, tp_count, 2, own_rows)
    all_totals, all_squares = jnp.sum(every_stats, axis=1).transpose(1, 0, 2).reshape(2, -1)
    all_raw = staged_gather(vis_feat, "seq", seq_down).reshape(-1, vis_feat.shape[1])
    all_mean = all_totals / VF
    all_inv_std = lax.rsqrt(all_squares / VF - all_mean * all_mean + ln_eps)
    all_normed = (
        (all_raw.astype(jnp.float32) - all_mean[:, None]) * all_inv_std[:, None] * ln_gain[None, :]
    ).astype(jnp.bfloat16)
    row_mean = lax.dynamic_slice_in_dim(all_mean, my_index * own_rows, own_rows)
    inv_std = lax.dynamic_slice_in_dim(all_inv_std, my_index * own_rows, own_rows)
    centred = (features - row_mean[:, None]) * inv_std[:, None]
    partial_embed = jnp.dot(all_normed, proj_weight, preferred_element_type=jnp.float32)
    slot_live = (slot_token >= 0)[:, None]
    slot_index = jnp.maximum(slot_token, 0)
    vis_total = partial_embed.shape[0]
    embed_part = exchange_sum(
        partial_embed.reshape(tp_count, vis_total // tp_count, slot_cols), "tp"
    ).astype(jnp.bfloat16)
    summed = exchange_gather(embed_part, "tp").reshape(vis_total, slot_cols)
    embed_rows = jnp.take(summed.astype(jnp.bfloat16), slot_index, axis=0)
    outgoing = jnp.where(slot_live, embed_rows, jnp.zeros_like(embed_rows)).reshape(
        seq_count, CAPD, slot_cols
    )
    arrived = lax.all_to_all(outgoing, "seq", split_axis=0, concat_axis=2, tiled=True)[0]
    lanes = jnp.arange(CAPD, dtype=jnp.int32)
    head_rows = tok_rows - CAPD
    tail_slot = vis_slot[head_rows:]
    one_hot = (tail_slot[:, None] == lanes[None, :]).astype(jnp.bfloat16)
    placed = jnp.dot(one_hot, arrived, preferred_element_type=jnp.float32).astype(jnp.bfloat16)
    hidden_tail = jnp.where((tail_slot >= 0)[:, None], placed, text_embed[head_rows:])

    def rms_normed(hidden):
        hidden_wide = hidden.astype(jnp.float32)
        inv_rms = lax.rsqrt(jnp.mean(hidden_wide * hidden_wide, axis=1, keepdims=True) + rms_eps)
        return (hidden_wide * inv_rms * rms_gain[None, :]).astype(jnp.bfloat16)

    stacked = jnp.concatenate([wq, wk, wv], axis=1)
    query_cols = wq.shape[1]
    key_cols = wk.shape[1]
    gathered = lax.all_gather(stacked, "seq", axis=0, tiled=True)
    projected_text = jnp.dot(
        rms_normed(text_embed[:head_rows]), gathered, preferred_element_type=jnp.float32
    )
    projected_tail = jnp.dot(rms_normed(hidden_tail), gathered, preferred_element_type=jnp.float32)
    projected = jnp.concatenate([projected_text, projected_tail], axis=0)
    local_heads = query_cols // HEAD
    local_groups = key_cols // HEAD
    positions = my_index * tok_rows + jnp.arange(tok_rows, dtype=jnp.int32)
    cosine, sine = rope_tables(positions, HEAD)
    queries = rotate(
        projected[:, :query_cols].reshape(tok_rows, local_heads, HEAD), cosine, sine
    ).astype(jnp.bfloat16)
    keys = rotate(
        projected[:, query_cols : query_cols + key_cols].reshape(tok_rows, local_groups, HEAD),
        cosine,
        sine,
    ).astype(jnp.bfloat16)
    values = (
        projected[:, query_cols + key_cols :]
        .astype(jnp.bfloat16)
        .reshape(tok_rows, local_groups, HEAD)
    )
    doc_marks = (doc_ids + 1).astype(jnp.bfloat16)
    prev_keys, prev_values, prev_docs = shifted((keys, values, doc_marks), "seq", 1)
    all_keys = jnp.concatenate([prev_keys, keys], axis=0)
    all_values = jnp.concatenate([prev_values, values], axis=0)
    query_docs = doc_marks.astype(jnp.float32)
    key_docs = jnp.concatenate([prev_docs.astype(jnp.float32), query_docs], axis=0)
    key_positions = jnp.concatenate([positions - tok_rows, positions], axis=0)
    allowed = (key_docs[None, :] == query_docs[:, None]) & (
        key_positions[None, :] <= positions[:, None]
    )
    grads = cotangent.reshape(tok_rows, local_groups, GROUP, HEAD)
    context, query_grads, key_grads, value_grads = attention_block(
        queries.reshape(tok_rows, local_groups, GROUP, HEAD), all_keys, all_values, grads, allowed
    )
    back_keys, back_values = (
        shifted(key_grads[:tok_rows].astype(jnp.bfloat16), "seq", -1).astype(jnp.float32),
        shifted(value_grads[:tok_rows].astype(jnp.bfloat16), "seq", -1).astype(jnp.float32),
    )
    key_total = key_grads[tok_rows:] + back_keys
    value_total = value_grads[tok_rows:] + back_values
    query_pre = (
        unrotate(query_grads.reshape(tok_rows, local_heads, HEAD), cosine, sine)
        .astype(jnp.bfloat16)
        .reshape(tok_rows, query_cols)
    )
    key_pre = unrotate(key_total, cosine, sine).astype(jnp.bfloat16).reshape(tok_rows, key_cols)
    value_pre = value_total.astype(jnp.bfloat16).reshape(tok_rows, key_cols)
    proj_grads = jnp.concatenate([query_pre, key_pre, value_pre], axis=1)
    selected = lax.dot_general(
        one_hot, proj_grads[head_rows:], (((0,), (0,)), ((), ())), preferred_element_type=jnp.float32
    ).astype(jnp.bfloat16)
    width = gathered.shape[0]
    norm_part = jnp.einsum(
        "sc,kdc->ksd",
        selected,
        gathered.reshape(tp_count, width // tp_count, gathered.shape[1]),
        preferred_element_type=jnp.float32,
    )
    norm_block = exchange_sum(norm_part, "tp").astype(jnp.bfloat16)
    norm_grads = (
        exchange_gather(norm_block, "tp")
        .reshape(tp_count, CAPD, width // tp_count)
        .transpose(1, 0, 2)
        .reshape(CAPD, width)
        .astype(jnp.float32)
    )
    embed_grads = norm_backward(arrived.astype(jnp.float32), norm_grads, rms_gain).astype(
        jnp.bfloat16
    )
    by_owner = embed_grads.reshape(CAPD, seq_count, slot_cols).transpose(1, 0, 2)
    returned = lax.all_to_all(by_owner, "seq", split_axis=0, concat_axis=0, tiled=True)
    token_grads = jnp.take(returned.reshape(seq_count * CAPD, slot_cols), token_slot, axis=0)
    feature_part = lax.dot_general(
        token_grads, proj_weight, (((1,), (1,)), ((), ())), preferred_element_type=jnp.float32
    )
    feature_grads = exchange_sum(
        feature_part.reshape(seq_count, own_rows, feature_part.shape[1]), "seq"
    )
    scaled = feature_grads * ln_gain[None, :]
    grad_total, grad_inner = jnp.sum(
        exchange_gather(
            jnp.stack([jnp.sum(scaled, axis=1), jnp.sum(scaled * centred, axis=1)]), "tp"
        ),
        axis=0,
    )
    vis_grad = (
        inv_std[:, None]
        * (scaled - (grad_total / VF)[:, None] - centred * (grad_inner / VF)[:, None])
    ).astype(jnp.bfloat16)
    return (context.reshape(tok_rows, query_cols), vis_grad)


def solution(mesh):
    return jax.shard_map(
        on_device,
        mesh=mesh,
        in_specs=(
            P("seq", "tp"),
            P("tp"),
            P("tp", "seq"),
            P("seq", None),
            P(),
            P("seq", "tp"),
            P("seq", "tp"),
            P("seq", "tp"),
            P("seq"),
            P("seq"),
            P(),
            P(),
            P("seq", "tp"),
        ),
        out_specs=(P("seq", "tp"), P("seq", "tp")),
        check_vma=False,
    )
```

```python
import math

import jax
import jax.numpy as jnp
from jax import lax
from jax.sharding import PartitionSpec as P

VF = 12800
HEAD = 128
CAPD = 32
GROUP = 4


ln_eps = 1e-05
rms_eps = 1e-06
rope_base = 1000000.0
masked_score = -1e30


def shifted(x, axis, by):
    peers = lax.axis_size(axis)
    pairs = [(i, i + by) for i in range(peers) if 0 <= i + by < peers]
    return lax.ppermute(x, axis, pairs)


def bit_of(axis, b):
    return (lax.axis_index(axis) // (1 << b)) % 2


def bit_pairs(axis, b):
    peers = lax.axis_size(axis)
    return [(i, i ^ (1 << b)) for i in range(peers)]


def group_index(axis, bits):
    return sum(bit_of(axis, b) * (1 << k) for k, b in enumerate(bits))


def group_pairs(axis, bits, o):
    peers = lax.axis_size(axis)
    mask = sum(((o >> k) & 1) << b for k, b in enumerate(bits))
    return [(i, i ^ mask) for i in range(peers)]


def group_scatter(x, axis, bits, dim=0):
    me = group_index(axis, bits)
    acc = lax.dynamic_index_in_dim(x, me, dim, keepdims=False).astype(jnp.float32)
    for o in range(1, 1 << len(bits)):
        send = lax.dynamic_index_in_dim(x, jnp.bitwise_xor(me, o), dim, keepdims=False)
        got = lax.ppermute(send.astype(jnp.bfloat16), axis, group_pairs(axis, bits, o))
        acc = acc + got.astype(jnp.float32)
    return acc


def group_gather(x, axis, bits):
    me = group_index(axis, bits)
    g = 1 << len(bits)
    parts = [x] + [lax.ppermute(x, axis, group_pairs(axis, bits, o)) for o in range(1, g)]
    order = jnp.bitwise_xor(jnp.arange(g, dtype=jnp.int32), me)
    return jnp.take(jnp.stack(parts), order, axis=0)


def staged_scatter(x, axis, groups):
    acc = x
    for bits in groups:
        g = 1 << len(bits)
        lead = acc.reshape((acc.shape[0] // g, g) + acc.shape[1:])
        acc = group_scatter(lead, axis, bits, dim=1)
    return acc[0]


def staged_gather(x, axis, groups):
    acc = x
    for bits in groups:
        acc = group_gather(acc, axis, bits)
    count = len(groups)
    return acc.transpose(list(range(count - 1, -1, -1)) + list(range(count, acc.ndim)))


def exchange_sum(x, axis):
    got = lax.all_to_all(x.astype(jnp.bfloat16), axis, 0, 0, tiled=True)
    return jnp.sum(got.astype(jnp.float32), axis=0)


def exchange_gather(x, axis):
    peers = lax.axis_size(axis)
    return lax.all_to_all(jnp.broadcast_to(x[None], (peers,) + x.shape), axis, 0, 0, tiled=True)


def log2(n):
    return n.bit_length() - 1


def rope_tables(positions, head_width):
    half = head_width // 2
    frequency = rope_base ** (-(jnp.arange(half).astype(jnp.float32) * 2.0 / head_width))
    angle = positions.astype(jnp.float32)[:, None] * frequency[None, :]
    return (jnp.cos(angle), jnp.sin(angle))


def rotate(values, cosine, sine):
    half = values.shape[-1] // 2
    first = values[..., :half]
    second = values[..., half:]
    cos_rows = cosine[:, None, :]
    sin_rows = sine[:, None, :]
    return jnp.concatenate(
        [first * cos_rows - second * sin_rows, second * cos_rows + first * sin_rows], axis=-1
    )


def unrotate(grads, cosine, sine):
    half = grads.shape[-1] // 2
    first = grads[..., :half]
    second = grads[..., half:]
    cos_rows = cosine[:, None, :]
    sin_rows = sine[:, None, :]
    return jnp.concatenate(
        [first * cos_rows + second * sin_rows, second * cos_rows - first * sin_rows], axis=-1
    )


def norm_backward(rows, grads, gain):
    inv_rms = lax.rsqrt(jnp.mean(rows * rows, axis=(0, 2), keepdims=True) + rms_eps)
    scaled = grads * gain
    inner = jnp.mean(rows * scaled, axis=(0, 2), keepdims=True)
    return inv_rms * scaled - rows * (inv_rms * inv_rms * inv_rms) * inner


def attention_block(queries, keys, values, grads, allowed):
    scale = 1.0 / math.sqrt(queries.shape[-1])
    scores = jnp.einsum("qhgd,khd->hgqk", queries, keys, preferred_element_type=jnp.float32) * scale
    masked = jnp.where(allowed[None, None], scores, masked_score)
    peak = jnp.max(masked, axis=-1, keepdims=True)
    raised = jnp.where(allowed[None, None], jnp.exp(masked - peak), 0.0)
    shares = raised / jnp.sum(raised, axis=-1, keepdims=True)
    shares_low = shares.astype(jnp.bfloat16)
    context = jnp.einsum(
        "hgqk,khd->qhgd", shares_low, values, preferred_element_type=jnp.float32
    ).astype(jnp.bfloat16)
    share_grads = jnp.einsum("qhgd,khd->hgqk", grads, values, preferred_element_type=jnp.float32)
    delta = jnp.sum(shares * share_grads, axis=-1, keepdims=True)
    score_grads = (shares * (share_grads - delta) * scale).astype(jnp.bfloat16)
    query_grads = jnp.einsum(
        "hgqk,khd->qhgd", score_grads, keys, preferred_element_type=jnp.float32
    )
    key_grads = jnp.einsum(
        "hgqk,qhgd->khd", score_grads, queries, preferred_element_type=jnp.float32
    )
    value_grads = jnp.einsum(
        "hgqk,qhgd->khd", shares_low, grads, preferred_element_type=jnp.float32
    )
    return (context, query_grads, key_grads, value_grads)


def on_device(
    vis_feat,
    ln_gain,
    proj_weight,
    text_embed,
    rms_gain,
    wq,
    wk,
    wv,
    doc_ids,
    vis_slot,
    slot_token,
    token_slot,
    cotangent,
):
    seq_count = lax.axis_size("seq")
    my_index = lax.axis_index("seq")
    tok_rows = text_embed.shape[0]
    slot_cols = proj_weight.shape[1]
    features = vis_feat.astype(jnp.float32)
    tp_count = lax.axis_size("tp")
    tp_bits = log2(tp_count)
    seq_bits = log2(seq_count)
    tp_all = [list(range(tp_bits))]
    seq_up = [[0], [1, 2], [3, 4]] if seq_bits == 5 else [[b] for b in range(seq_bits)]
    seq_down = seq_up[::-1]
    row_total, row_squares = jnp.sum(
        exchange_gather(
            jnp.stack([jnp.sum(features, axis=1), jnp.sum(features * features, axis=1)]), "tp"
        ),
        axis=0,
    )
    row_mean = row_total / VF
    row_var = row_squares / VF - row_mean * row_mean
    inv_std = lax.rsqrt(row_var + ln_eps)
    centred = (features - row_mean[:, None]) * inv_std[:, None]
    vis_normed = (centred * ln_gain[None, :]).astype(jnp.bfloat16)
    all_normed = staged_gather(vis_normed, "seq", seq_down)
    partial_embed = jnp.dot(
        all_normed.reshape(seq_count * vis_feat.shape[0], vis_feat.shape[1]),
        proj_weight,
        preferred_element_type=jnp.float32,
    )
    slot_live = (slot_token >= 0)[:, None]
    slot_index = jnp.maximum(slot_token, 0)
    vis_total = partial_embed.shape[0]
    embed_part = exchange_sum(
        partial_embed.reshape(tp_count, vis_total // tp_count, slot_cols), "tp"
    ).astype(jnp.bfloat16)
    summed = exchange_gather(embed_part, "tp").reshape(vis_total, slot_cols)
    embed_rows = jnp.take(summed.astype(jnp.bfloat16), slot_index, axis=0)
    outgoing = jnp.where(slot_live, embed_rows, jnp.zeros_like(embed_rows)).reshape(
        seq_count, CAPD, slot_cols
    )
    arrived = lax.all_to_all(outgoing, "seq", split_axis=0, concat_axis=2, tiled=True)[0]
    lanes = jnp.arange(CAPD, dtype=jnp.int32)
    one_hot = (vis_slot[:, None] == lanes[None, :]).astype(jnp.bfloat16)
    placed = jnp.dot(one_hot, arrived, preferred_element_type=jnp.float32).astype(jnp.bfloat16)
    is_image = vis_slot >= 0
    hidden = jnp.where(is_image[:, None], placed, text_embed)
    hidden_wide = hidden.astype(jnp.float32)
    inv_rms = lax.rsqrt(jnp.mean(hidden_wide * hidden_wide, axis=1, keepdims=True) + rms_eps)
    normed = (hidden_wide * inv_rms * rms_gain[None, :]).astype(jnp.bfloat16)
    stacked = jnp.concatenate([wq, wk, wv], axis=1)
    query_cols = wq.shape[1]
    key_cols = wk.shape[1]
    gathered = lax.all_gather(stacked, "seq", axis=0, tiled=True)
    projected = jnp.dot(normed, gathered, preferred_element_type=jnp.float32)
    local_heads = query_cols // HEAD
    local_groups = key_cols // HEAD
    positions = my_index * tok_rows + jnp.arange(tok_rows, dtype=jnp.int32)
    cosine, sine = rope_tables(positions, HEAD)
    queries = rotate(
        projected[:, :query_cols].reshape(tok_rows, local_heads, HEAD), cosine, sine
    ).astype(jnp.bfloat16)
    keys = rotate(
        projected[:, query_cols : query_cols + key_cols].reshape(tok_rows, local_groups, HEAD),
        cosine,
        sine,
    ).astype(jnp.bfloat16)
    values = (
        projected[:, query_cols + key_cols :]
        .astype(jnp.bfloat16)
        .reshape(tok_rows, local_groups, HEAD)
    )
    doc_marks = (doc_ids + 1).astype(jnp.bfloat16)
    prev_keys, prev_values, prev_docs = shifted((keys, values, doc_marks), "seq", 1)
    all_keys = jnp.concatenate([prev_keys, keys], axis=0)
    all_values = jnp.concatenate([prev_values, values], axis=0)
    query_docs = doc_marks.astype(jnp.float32)
    key_docs = jnp.concatenate([prev_docs.astype(jnp.float32), query_docs], axis=0)
    key_positions = jnp.concatenate([positions - tok_rows, positions], axis=0)
    allowed = (key_docs[None, :] == query_docs[:, None]) & (
        key_positions[None, :] <= positions[:, None]
    )
    grads = cotangent.reshape(tok_rows, local_groups, GROUP, HEAD)
    context, query_grads, key_grads, value_grads = attention_block(
        queries.reshape(tok_rows, local_groups, GROUP, HEAD), all_keys, all_values, grads, allowed
    )
    back_keys, back_values = (
        shifted(key_grads[:tok_rows].astype(jnp.bfloat16), "seq", -1).astype(jnp.float32),
        shifted(value_grads[:tok_rows].astype(jnp.bfloat16), "seq", -1).astype(jnp.float32),
    )
    key_total = key_grads[tok_rows:] + back_keys
    value_total = value_grads[tok_rows:] + back_values
    query_pre = (
        unrotate(query_grads.reshape(tok_rows, local_heads, HEAD), cosine, sine)
        .astype(jnp.bfloat16)
        .reshape(tok_rows, query_cols)
    )
    key_pre = unrotate(key_total, cosine, sine).astype(jnp.bfloat16).reshape(tok_rows, key_cols)
    value_pre = value_total.astype(jnp.bfloat16).reshape(tok_rows, key_cols)
    proj_grads = jnp.concatenate([query_pre, key_pre, value_pre], axis=1)
    selected = lax.dot_general(
        one_hot, proj_grads, (((0,), (0,)), ((), ())), preferred_element_type=jnp.float32
    ).astype(jnp.bfloat16)
    width = gathered.shape[0]
    quarters = seq_count // tp_count
    norm_part = jnp.einsum(
        "sc,kqrc->kqsr",
        selected,
        gathered.reshape(tp_count, quarters, slot_cols, gathered.shape[1]),
        preferred_element_type=jnp.float32,
    )
    norm_block = exchange_sum(norm_part, "tp").astype(jnp.bfloat16)
    norm_grads = exchange_gather(norm_block, "tp").reshape(seq_count, CAPD, slot_cols)
    arrived_by_owner = arrived.reshape(CAPD, seq_count, slot_cols).transpose(1, 0, 2)
    by_owner = norm_backward(
        arrived_by_owner.astype(jnp.float32),
        norm_grads.astype(jnp.float32),
        rms_gain.reshape(seq_count, 1, slot_cols),
    ).astype(jnp.bfloat16)
    returned = lax.all_to_all(by_owner, "seq", split_axis=0, concat_axis=0, tiled=True)
    token_grads = jnp.take(returned.reshape(seq_count * CAPD, slot_cols), token_slot, axis=0)
    own_rows = vis_feat.shape[0]
    feature_part = lax.dot_general(
        token_grads, proj_weight, (((1,), (1,)), ((), ())), preferred_element_type=jnp.float32
    )
    feature_grads = exchange_sum(
        feature_part.reshape(seq_count, own_rows, feature_part.shape[1]), "seq"
    )
    scaled = feature_grads * ln_gain[None, :]
    grad_total, grad_inner = jnp.sum(
        exchange_gather(
            jnp.stack([jnp.sum(scaled, axis=1), jnp.sum(scaled * centred, axis=1)]), "tp"
        ),
        axis=0,
    )
    vis_grad = (
        inv_std[:, None]
        * (scaled - (grad_total / VF)[:, None] - centred * (grad_inner / VF)[:, None])
    ).astype(jnp.bfloat16)
    return (context.reshape(tok_rows, query_cols), vis_grad)


def solution(mesh):
    return jax.shard_map(
        on_device,
        mesh=mesh,
        in_specs=(
            P("seq", "tp"),
            P("tp"),
            P("tp", "seq"),
            P("seq", None),
            P(),
            P("seq", "tp"),
            P("seq", "tp"),
            P("seq", "tp"),
            P("seq"),
            P("seq"),
            P(),
            P(),
            P("seq", "tp"),
        ),
        out_specs=(P("seq", "tp"), P("seq", "tp")),
        check_vma=False,
    )
```

```python
import math

import jax
import jax.numpy as jnp
from jax import lax
from jax.sharding import PartitionSpec as P

VF = 12800
HEAD = 128
CAPD = 32
GROUP = 4


ln_eps = 1e-05
rms_eps = 1e-06
rope_base = 1000000.0
masked_score = -1e30


def shifted(x, axis, by):
    peers = lax.axis_size(axis)
    pairs = [(i, i + by) for i in range(peers) if 0 <= i + by < peers]
    return lax.ppermute(x, axis, pairs)


def bit_of(axis, b):
    return (lax.axis_index(axis) // (1 << b)) % 2


def bit_pairs(axis, b):
    peers = lax.axis_size(axis)
    return [(i, i ^ (1 << b)) for i in range(peers)]


def group_index(axis, bits):
    return sum(bit_of(axis, b) * (1 << k) for k, b in enumerate(bits))


def group_pairs(axis, bits, o):
    peers = lax.axis_size(axis)
    mask = sum(((o >> k) & 1) << b for k, b in enumerate(bits))
    return [(i, i ^ mask) for i in range(peers)]


def group_scatter(x, axis, bits, dim=0):
    me = group_index(axis, bits)
    acc = lax.dynamic_index_in_dim(x, me, dim, keepdims=False).astype(jnp.float32)
    for o in range(1, 1 << len(bits)):
        send = lax.dynamic_index_in_dim(x, jnp.bitwise_xor(me, o), dim, keepdims=False)
        got = lax.ppermute(send.astype(jnp.bfloat16), axis, group_pairs(axis, bits, o))
        acc = acc + got.astype(jnp.float32)
    return acc


def group_gather(x, axis, bits):
    me = group_index(axis, bits)
    g = 1 << len(bits)
    parts = [x] + [lax.ppermute(x, axis, group_pairs(axis, bits, o)) for o in range(1, g)]
    order = jnp.bitwise_xor(jnp.arange(g, dtype=jnp.int32), me)
    return jnp.take(jnp.stack(parts), order, axis=0)


def staged_scatter(x, axis, groups):
    acc = x
    for bits in groups:
        g = 1 << len(bits)
        lead = acc.reshape((acc.shape[0] // g, g) + acc.shape[1:])
        acc = group_scatter(lead, axis, bits, dim=1)
    return acc[0]


def staged_gather(x, axis, groups):
    acc = x
    for bits in groups:
        acc = group_gather(acc, axis, bits)
    count = len(groups)
    return acc.transpose(list(range(count - 1, -1, -1)) + list(range(count, acc.ndim)))


def exchange_sum(x, axis):
    got = lax.all_to_all(x.astype(jnp.bfloat16), axis, 0, 0, tiled=True)
    return jnp.sum(got.astype(jnp.float32), axis=0)


def exchange_gather(x, axis):
    peers = lax.axis_size(axis)
    return lax.all_to_all(jnp.broadcast_to(x[None], (peers,) + x.shape), axis, 0, 0, tiled=True)


def log2(n):
    return n.bit_length() - 1


def rope_tables(positions, head_width):
    half = head_width // 2
    frequency = rope_base ** (-(jnp.arange(half).astype(jnp.float32) * 2.0 / head_width))
    angle = positions.astype(jnp.float32)[:, None] * frequency[None, :]
    return (jnp.cos(angle), jnp.sin(angle))


def rotate(values, cosine, sine):
    half = values.shape[-1] // 2
    first = values[..., :half]
    second = values[..., half:]
    cos_rows = cosine[:, None, :]
    sin_rows = sine[:, None, :]
    return jnp.concatenate(
        [first * cos_rows - second * sin_rows, second * cos_rows + first * sin_rows], axis=-1
    )


def unrotate(grads, cosine, sine):
    half = grads.shape[-1] // 2
    first = grads[..., :half]
    second = grads[..., half:]
    cos_rows = cosine[:, None, :]
    sin_rows = sine[:, None, :]
    return jnp.concatenate(
        [first * cos_rows + second * sin_rows, second * cos_rows - first * sin_rows], axis=-1
    )


def norm_backward(rows, grads, gain, axes):
    inv_rms = lax.rsqrt(jnp.mean(rows * rows, axis=axes, keepdims=True) + rms_eps)
    scaled = grads * gain
    inner = jnp.mean(rows * scaled, axis=axes, keepdims=True)
    return inv_rms * scaled - rows * (inv_rms * inv_rms * inv_rms) * inner


def attention_block(queries, keys, values, grads, allowed):
    scale = 1.0 / math.sqrt(queries.shape[-1])
    scores = jnp.einsum("qhgd,khd->hgqk", queries, keys, preferred_element_type=jnp.float32) * scale
    masked = jnp.where(allowed[None, None], scores, masked_score)
    peak = jnp.max(masked, axis=-1, keepdims=True)
    raised = jnp.where(allowed[None, None], jnp.exp(masked - peak), 0.0)
    shares = raised / jnp.sum(raised, axis=-1, keepdims=True)
    shares_low = shares.astype(jnp.bfloat16)
    context = jnp.einsum(
        "hgqk,khd->qhgd", shares_low, values, preferred_element_type=jnp.float32
    ).astype(jnp.bfloat16)
    share_grads = jnp.einsum("qhgd,khd->hgqk", grads, values, preferred_element_type=jnp.float32)
    delta = jnp.sum(shares * share_grads, axis=-1, keepdims=True)
    score_grads = (shares * (share_grads - delta) * scale).astype(jnp.bfloat16)
    query_grads = jnp.einsum(
        "hgqk,khd->qhgd", score_grads, keys, preferred_element_type=jnp.float32
    )
    key_grads = jnp.einsum(
        "hgqk,qhgd->khd", score_grads, queries, preferred_element_type=jnp.float32
    )
    value_grads = jnp.einsum(
        "hgqk,qhgd->khd", shares_low, grads, preferred_element_type=jnp.float32
    )
    return (context, query_grads, key_grads, value_grads)


def on_device(
    vis_feat,
    ln_gain,
    proj_weight,
    text_embed,
    rms_gain,
    wq,
    wk,
    wv,
    doc_ids,
    vis_slot,
    slot_token,
    token_slot,
    cotangent,
):
    seq_count = lax.axis_size("seq")
    my_index = lax.axis_index("seq")
    tok_rows = text_embed.shape[0]
    slot_cols = proj_weight.shape[1]
    features = vis_feat.astype(jnp.float32)
    tp_count = lax.axis_size("tp")
    tp_bits = log2(tp_count)
    seq_bits = log2(seq_count)
    tp_all = [list(range(tp_bits))]
    seq_up = [[0], [1, 2], [3, 4]] if seq_bits == 5 else [[b] for b in range(seq_bits)]
    seq_down = seq_up[::-1]
    row_total, row_squares = jnp.sum(
        exchange_gather(
            jnp.stack([jnp.sum(features, axis=1), jnp.sum(features * features, axis=1)]), "tp"
        ),
        axis=0,
    )
    row_mean = row_total / VF
    row_var = row_squares / VF - row_mean * row_mean
    inv_std = lax.rsqrt(row_var + ln_eps)
    centred = (features - row_mean[:, None]) * inv_std[:, None]
    vis_normed = (centred * ln_gain[None, :]).astype(jnp.bfloat16)
    all_normed = staged_gather(vis_normed, "seq", seq_down)
    partial_embed = jnp.dot(
        all_normed.reshape(seq_count * vis_feat.shape[0], vis_feat.shape[1]),
        proj_weight,
        preferred_element_type=jnp.float32,
    )
    slot_live = (slot_token >= 0)[:, None]
    slot_index = jnp.maximum(slot_token, 0)
    devices = seq_count * tp_count
    per = CAPD // tp_count
    slot_rows = jnp.take(partial_embed, slot_index, axis=0)
    outgoing = jnp.where(slot_live, slot_rows, 0.0).reshape(devices, per, slot_cols)
    got = lax.all_to_all(outgoing.astype(jnp.bfloat16), ("seq", "tp"), 0, 0, tiled=True)
    mine = jnp.sum(
        got.reshape(seq_count, tp_count, per, slot_cols).astype(jnp.float32), axis=1
    ).astype(jnp.bfloat16)
    all_mine = exchange_gather(mine, "tp")
    arrived = all_mine.transpose(0, 2, 1, 3).reshape(CAPD, seq_count * slot_cols)
    lanes = jnp.arange(CAPD, dtype=jnp.int32)
    one_hot = (vis_slot[:, None] == lanes[None, :]).astype(jnp.bfloat16)
    placed = jnp.dot(one_hot, arrived, preferred_element_type=jnp.float32).astype(jnp.bfloat16)
    is_image = vis_slot >= 0
    hidden = jnp.where(is_image[:, None], placed, text_embed)
    hidden_wide = hidden.astype(jnp.float32)
    inv_rms = lax.rsqrt(jnp.mean(hidden_wide * hidden_wide, axis=1, keepdims=True) + rms_eps)
    normed = (hidden_wide * inv_rms * rms_gain[None, :]).astype(jnp.bfloat16)
    stacked = jnp.concatenate([wq, wk, wv], axis=1)
    query_cols = wq.shape[1]
    key_cols = wk.shape[1]
    gathered = lax.all_gather(stacked, "seq", axis=0, tiled=True)
    projected = jnp.dot(normed, gathered, preferred_element_type=jnp.float32)
    local_heads = query_cols // HEAD
    local_groups = key_cols // HEAD
    positions = my_index * tok_rows + jnp.arange(tok_rows, dtype=jnp.int32)
    cosine, sine = rope_tables(positions, HEAD)
    queries = rotate(
        projected[:, :query_cols].reshape(tok_rows, local_heads, HEAD), cosine, sine
    ).astype(jnp.bfloat16)
    keys = rotate(
        projected[:, query_cols : query_cols + key_cols].reshape(tok_rows, local_groups, HEAD),
        cosine,
        sine,
    ).astype(jnp.bfloat16)
    values = (
        projected[:, query_cols + key_cols :]
        .astype(jnp.bfloat16)
        .reshape(tok_rows, local_groups, HEAD)
    )
    doc_marks = (doc_ids + 1).astype(jnp.bfloat16)
    prev_keys, prev_values, prev_docs = shifted((keys, values, doc_marks), "seq", 1)
    all_keys = jnp.concatenate([prev_keys, keys], axis=0)
    all_values = jnp.concatenate([prev_values, values], axis=0)
    query_docs = doc_marks.astype(jnp.float32)
    key_docs = jnp.concatenate([prev_docs.astype(jnp.float32), query_docs], axis=0)
    key_positions = jnp.concatenate([positions - tok_rows, positions], axis=0)
    allowed = (key_docs[None, :] == query_docs[:, None]) & (
        key_positions[None, :] <= positions[:, None]
    )
    grads = cotangent.reshape(tok_rows, local_groups, GROUP, HEAD)
    context, query_grads, key_grads, value_grads = attention_block(
        queries.reshape(tok_rows, local_groups, GROUP, HEAD), all_keys, all_values, grads, allowed
    )
    back_keys, back_values = (
        shifted(key_grads[:tok_rows].astype(jnp.bfloat16), "seq", -1).astype(jnp.float32),
        shifted(value_grads[:tok_rows].astype(jnp.bfloat16), "seq", -1).astype(jnp.float32),
    )
    key_total = key_grads[tok_rows:] + back_keys
    value_total = value_grads[tok_rows:] + back_values
    query_pre = (
        unrotate(query_grads.reshape(tok_rows, local_heads, HEAD), cosine, sine)
        .astype(jnp.bfloat16)
        .reshape(tok_rows, query_cols)
    )
    key_pre = unrotate(key_total, cosine, sine).astype(jnp.bfloat16).reshape(tok_rows, key_cols)
    value_pre = value_total.astype(jnp.bfloat16).reshape(tok_rows, key_cols)
    proj_grads = jnp.concatenate([query_pre, key_pre, value_pre], axis=1)
    selected = lax.dot_general(
        one_hot, proj_grads, (((0,), (0,)), ((), ())), preferred_element_type=jnp.float32
    ).astype(jnp.bfloat16)
    norm_part = jnp.einsum(
        "tkc,jrc->jtkr",
        selected.reshape(tp_count, per, selected.shape[1]),
        gathered.reshape(seq_count, slot_cols, gathered.shape[1]),
        preferred_element_type=jnp.float32,
    )
    embed_part = norm_backward(
        all_mine.transpose(1, 0, 2, 3).astype(jnp.float32),
        norm_part,
        rms_gain.reshape(seq_count, 1, 1, slot_cols),
        (0, 3),
    )
    got_back = lax.all_to_all(
        embed_part.astype(jnp.bfloat16).reshape(devices, per, slot_cols),
        ("seq", "tp"), 0, 0, tiled=True,
    )
    mine_back = jnp.sum(
        got_back.reshape(seq_count, tp_count, per, slot_cols).astype(jnp.float32), axis=1
    ).astype(jnp.bfloat16)
    all_back = exchange_gather(mine_back, "tp").reshape(tp_count * seq_count * per, slot_cols)
    block_of = token_slot // CAPD
    lane_of = token_slot % CAPD
    back_index = (lane_of // per) * (seq_count * per) + block_of * per + lane_of % per
    token_grads = jnp.take(all_back, back_index, axis=0)
    own_rows = vis_feat.shape[0]
    feature_part = lax.dot_general(
        token_grads, proj_weight, (((1,), (1,)), ((), ())), preferred_element_type=jnp.float32
    )
    feature_grads = exchange_sum(
        feature_part.reshape(seq_count, own_rows, feature_part.shape[1]), "seq"
    )
    scaled = feature_grads * ln_gain[None, :]
    grad_total, grad_inner = jnp.sum(
        exchange_gather(
            jnp.stack([jnp.sum(scaled, axis=1), jnp.sum(scaled * centred, axis=1)]), "tp"
        ),
        axis=0,
    )
    vis_grad = (
        inv_std[:, None]
        * (scaled - (grad_total / VF)[:, None] - centred * (grad_inner / VF)[:, None])
    ).astype(jnp.bfloat16)
    return (context.reshape(tok_rows, query_cols), vis_grad)


def solution(mesh):
    return jax.shard_map(
        on_device,
        mesh=mesh,
        in_specs=(
            P("seq", "tp"),
            P("tp"),
            P("tp", "seq"),
            P("seq", None),
            P(),
            P("seq", "tp"),
            P("seq", "tp"),
            P("seq", "tp"),
            P("seq"),
            P("seq"),
            P(),
            P(),
            P("seq", "tp"),
        ),
        out_specs=(P("seq", "tp"), P("seq", "tp")),
        check_vma=False,
    )
```

```python
import math

import jax
import jax.numpy as jnp
from jax import lax
from jax.sharding import PartitionSpec as P

VF = 12800
HEAD = 128
CAPD = 32
GROUP = 4


ln_eps = 1e-05
rms_eps = 1e-06
rope_base = 1000000.0
masked_score = -1e30


def shifted(x, axis, by):
    peers = lax.axis_size(axis)
    pairs = [(i, i + by) for i in range(peers) if 0 <= i + by < peers]
    return lax.ppermute(x, axis, pairs)


def bit_of(axis, b):
    return (lax.axis_index(axis) // (1 << b)) % 2


def bit_pairs(axis, b):
    peers = lax.axis_size(axis)
    return [(i, i ^ (1 << b)) for i in range(peers)]


def group_index(axis, bits):
    return sum(bit_of(axis, b) * (1 << k) for k, b in enumerate(bits))


def group_pairs(axis, bits, o):
    peers = lax.axis_size(axis)
    mask = sum(((o >> k) & 1) << b for k, b in enumerate(bits))
    return [(i, i ^ mask) for i in range(peers)]


def group_scatter(x, axis, bits, dim=0):
    me = group_index(axis, bits)
    acc = lax.dynamic_index_in_dim(x, me, dim, keepdims=False).astype(jnp.float32)
    for o in range(1, 1 << len(bits)):
        send = lax.dynamic_index_in_dim(x, jnp.bitwise_xor(me, o), dim, keepdims=False)
        got = lax.ppermute(send.astype(jnp.bfloat16), axis, group_pairs(axis, bits, o))
        acc = acc + got.astype(jnp.float32)
    return acc


def group_gather(x, axis, bits):
    me = group_index(axis, bits)
    g = 1 << len(bits)
    parts = [x] + [lax.ppermute(x, axis, group_pairs(axis, bits, o)) for o in range(1, g)]
    order = jnp.bitwise_xor(jnp.arange(g, dtype=jnp.int32), me)
    return jnp.take(jnp.stack(parts), order, axis=0)


def staged_scatter(x, axis, groups):
    acc = x
    for bits in groups:
        g = 1 << len(bits)
        lead = acc.reshape((acc.shape[0] // g, g) + acc.shape[1:])
        acc = group_scatter(lead, axis, bits, dim=1)
    return acc[0]


def staged_gather(x, axis, groups):
    acc = x
    for bits in groups:
        acc = group_gather(acc, axis, bits)
    count = len(groups)
    return acc.transpose(list(range(count - 1, -1, -1)) + list(range(count, acc.ndim)))


def exchange_sum(x, axis):
    got = lax.all_to_all(x.astype(jnp.bfloat16), axis, 0, 0, tiled=True)
    return jnp.sum(got.astype(jnp.float32), axis=0)


def exchange_gather(x, axis):
    peers = lax.axis_size(axis)
    return lax.all_to_all(jnp.broadcast_to(x[None], (peers,) + x.shape), axis, 0, 0, tiled=True)


def log2(n):
    return n.bit_length() - 1


def rope_tables(positions, head_width):
    half = head_width // 2
    frequency = rope_base ** (-(jnp.arange(half).astype(jnp.float32) * 2.0 / head_width))
    angle = positions.astype(jnp.float32)[:, None] * frequency[None, :]
    return (jnp.cos(angle), jnp.sin(angle))


def rotate(values, cosine, sine):
    half = values.shape[-1] // 2
    first = values[..., :half]
    second = values[..., half:]
    cos_rows = cosine[:, None, :]
    sin_rows = sine[:, None, :]
    return jnp.concatenate(
        [first * cos_rows - second * sin_rows, second * cos_rows + first * sin_rows], axis=-1
    )


def unrotate(grads, cosine, sine):
    half = grads.shape[-1] // 2
    first = grads[..., :half]
    second = grads[..., half:]
    cos_rows = cosine[:, None, :]
    sin_rows = sine[:, None, :]
    return jnp.concatenate(
        [first * cos_rows + second * sin_rows, second * cos_rows - first * sin_rows], axis=-1
    )


def norm_backward(rows, grads, gain, axes):
    inv_rms = lax.rsqrt(jnp.mean(rows * rows, axis=axes, keepdims=True) + rms_eps)
    scaled = grads * gain
    inner = jnp.mean(rows * scaled, axis=axes, keepdims=True)
    return inv_rms * scaled - rows * (inv_rms * inv_rms * inv_rms) * inner


def attention_block(queries, keys, values, grads, allowed):
    scale = 1.0 / math.sqrt(queries.shape[-1])
    scores = jnp.einsum("qhgd,khd->hgqk", queries, keys, preferred_element_type=jnp.float32) * scale
    masked = jnp.where(allowed[None, None], scores, masked_score)
    peak = jnp.max(masked, axis=-1, keepdims=True)
    raised = jnp.where(allowed[None, None], jnp.exp(masked - peak), 0.0)
    shares = raised / jnp.sum(raised, axis=-1, keepdims=True)
    shares_low = shares.astype(jnp.bfloat16)
    context = jnp.einsum(
        "hgqk,khd->qhgd", shares_low, values, preferred_element_type=jnp.float32
    ).astype(jnp.bfloat16)
    share_grads = jnp.einsum("qhgd,khd->hgqk", grads, values, preferred_element_type=jnp.float32)
    delta = jnp.sum(shares * share_grads, axis=-1, keepdims=True)
    score_grads = (shares * (share_grads - delta) * scale).astype(jnp.bfloat16)
    query_grads = jnp.einsum(
        "hgqk,khd->qhgd", score_grads, keys, preferred_element_type=jnp.float32
    )
    key_grads = jnp.einsum(
        "hgqk,qhgd->khd", score_grads, queries, preferred_element_type=jnp.float32
    )
    value_grads = jnp.einsum(
        "hgqk,qhgd->khd", shares_low, grads, preferred_element_type=jnp.float32
    )
    return (context, query_grads, key_grads, value_grads)


def on_device(
    vis_feat,
    ln_gain,
    proj_weight,
    text_embed,
    rms_gain,
    wq,
    wk,
    wv,
    doc_ids,
    vis_slot,
    slot_token,
    token_slot,
    cotangent,
):
    seq_count = lax.axis_size("seq")
    my_index = lax.axis_index("seq")
    tok_rows = text_embed.shape[0]
    slot_cols = proj_weight.shape[1]
    features = vis_feat.astype(jnp.float32)
    tp_count = lax.axis_size("tp")
    tp_bits = log2(tp_count)
    seq_bits = log2(seq_count)
    tp_all = [list(range(tp_bits))]
    seq_up = [[0], [1, 2], [3, 4]] if seq_bits == 5 else [[b] for b in range(seq_bits)]
    seq_down = seq_up[::-1]
    row_total, row_squares = jnp.sum(
        exchange_gather(
            jnp.stack([jnp.sum(features, axis=1), jnp.sum(features * features, axis=1)]), "tp"
        ),
        axis=0,
    )
    row_mean = row_total / VF
    row_var = row_squares / VF - row_mean * row_mean
    inv_std = lax.rsqrt(row_var + ln_eps)
    centred = (features - row_mean[:, None]) * inv_std[:, None]
    vis_normed = (centred * ln_gain[None, :]).astype(jnp.bfloat16)
    all_normed = staged_gather(vis_normed, "seq", seq_down)
    partial_embed = jnp.dot(
        all_normed.reshape(seq_count * vis_feat.shape[0], vis_feat.shape[1]),
        proj_weight,
        preferred_element_type=jnp.float32,
    )
    slot_live = (slot_token >= 0)[:, None]
    slot_index = jnp.maximum(slot_token, 0)
    devices = seq_count * tp_count
    per = CAPD // tp_count
    slot_rows = jnp.take(partial_embed, slot_index, axis=0)
    outgoing = jnp.where(slot_live, slot_rows, 0.0).reshape(devices, per, slot_cols)
    got = lax.all_to_all(outgoing.astype(jnp.bfloat16), ("seq", "tp"), 0, 0, tiled=True)
    mine = jnp.sum(
        got.reshape(seq_count, tp_count, per, slot_cols).astype(jnp.float32), axis=1
    ).astype(jnp.bfloat16)
    stacked = jnp.concatenate([wq, wk, wv], axis=1)
    gathered = lax.all_gather(stacked, "seq", axis=0, tiled=True)
    mine, gathered = lax.optimization_barrier((mine, gathered))
    all_mine = exchange_gather(mine, "tp")
    arrived = all_mine.transpose(0, 2, 1, 3).reshape(CAPD, seq_count * slot_cols)
    lanes = jnp.arange(CAPD, dtype=jnp.int32)
    head_rows = tok_rows - CAPD
    tail_slot = vis_slot[head_rows:]
    one_hot = (tail_slot[:, None] == lanes[None, :]).astype(jnp.bfloat16)
    placed = jnp.dot(one_hot, arrived, preferred_element_type=jnp.float32).astype(jnp.bfloat16)
    hidden_tail = jnp.where((tail_slot >= 0)[:, None], placed, text_embed[head_rows:])

    def rms_normed(hidden):
        hidden_wide = hidden.astype(jnp.float32)
        inv_rms = lax.rsqrt(jnp.mean(hidden_wide * hidden_wide, axis=1, keepdims=True) + rms_eps)
        return (hidden_wide * inv_rms * rms_gain[None, :]).astype(jnp.bfloat16)

    query_cols = wq.shape[1]
    key_cols = wk.shape[1]
    projected_text = jnp.dot(rms_normed(text_embed), gathered, preferred_element_type=jnp.float32)
    projected_tail = jnp.dot(rms_normed(hidden_tail), gathered, preferred_element_type=jnp.float32)
    projected = lax.dynamic_update_slice_in_dim(projected_text, projected_tail, head_rows, 0)
    local_heads = query_cols // HEAD
    local_groups = key_cols // HEAD
    positions = my_index * tok_rows + jnp.arange(tok_rows, dtype=jnp.int32)
    cosine, sine = rope_tables(positions, HEAD)
    queries = rotate(
        projected[:, :query_cols].reshape(tok_rows, local_heads, HEAD), cosine, sine
    ).astype(jnp.bfloat16)
    keys = rotate(
        projected[:, query_cols : query_cols + key_cols].reshape(tok_rows, local_groups, HEAD),
        cosine,
        sine,
    ).astype(jnp.bfloat16)
    values = (
        projected[:, query_cols + key_cols :]
        .astype(jnp.bfloat16)
        .reshape(tok_rows, local_groups, HEAD)
    )
    doc_marks = (doc_ids + 1).astype(jnp.bfloat16)
    prev_keys, prev_values, prev_docs = shifted((keys, values, doc_marks), "seq", 1)
    all_keys = jnp.concatenate([prev_keys, keys], axis=0)
    all_values = jnp.concatenate([prev_values, values], axis=0)
    query_docs = doc_marks.astype(jnp.float32)
    key_docs = jnp.concatenate([prev_docs.astype(jnp.float32), query_docs], axis=0)
    key_positions = jnp.concatenate([positions - tok_rows, positions], axis=0)
    allowed = (key_docs[None, :] == query_docs[:, None]) & (
        key_positions[None, :] <= positions[:, None]
    )
    grads = cotangent.reshape(tok_rows, local_groups, GROUP, HEAD)
    context, query_grads, key_grads, value_grads = attention_block(
        queries.reshape(tok_rows, local_groups, GROUP, HEAD), all_keys, all_values, grads, allowed
    )
    back_keys, back_values = (
        shifted(key_grads[:tok_rows].astype(jnp.bfloat16), "seq", -1).astype(jnp.float32),
        shifted(value_grads[:tok_rows].astype(jnp.bfloat16), "seq", -1).astype(jnp.float32),
    )
    key_total = key_grads[tok_rows:] + back_keys
    value_total = value_grads[tok_rows:] + back_values
    query_pre = (
        unrotate(query_grads.reshape(tok_rows, local_heads, HEAD), cosine, sine)
        .astype(jnp.bfloat16)
        .reshape(tok_rows, query_cols)
    )
    key_pre = unrotate(key_total, cosine, sine).astype(jnp.bfloat16).reshape(tok_rows, key_cols)
    value_pre = value_total.astype(jnp.bfloat16).reshape(tok_rows, key_cols)
    proj_grads = jnp.concatenate([query_pre, key_pre, value_pre], axis=1)
    selected = lax.dot_general(
        one_hot, proj_grads[head_rows:], (((0,), (0,)), ((), ())), preferred_element_type=jnp.float32
    ).astype(jnp.bfloat16)
    norm_part = jnp.einsum(
        "tkc,jrc->jtkr",
        selected.reshape(tp_count, per, selected.shape[1]),
        gathered.reshape(seq_count, slot_cols, gathered.shape[1]),
        preferred_element_type=jnp.float32,
    )
    embed_part = norm_backward(
        all_mine.transpose(1, 0, 2, 3).astype(jnp.float32),
        norm_part,
        rms_gain.reshape(seq_count, 1, 1, slot_cols),
        (0, 3),
    )
    got_back = lax.all_to_all(
        embed_part.astype(jnp.bfloat16).reshape(devices, per, slot_cols),
        ("seq", "tp"), 0, 0, tiled=True,
    )
    mine_back = jnp.sum(
        got_back.reshape(seq_count, tp_count, per, slot_cols).astype(jnp.float32), axis=1
    ).astype(jnp.bfloat16)
    all_back = exchange_gather(mine_back, "tp").reshape(tp_count * seq_count * per, slot_cols)
    block_of = token_slot // CAPD
    lane_of = token_slot % CAPD
    back_index = (lane_of // per) * (seq_count * per) + block_of * per + lane_of % per
    token_grads = jnp.take(all_back, back_index, axis=0)
    own_rows = vis_feat.shape[0]
    feature_part = lax.dot_general(
        token_grads, proj_weight, (((1,), (1,)), ((), ())), preferred_element_type=jnp.float32
    )
    feature_grads = exchange_sum(
        feature_part.reshape(seq_count, own_rows, feature_part.shape[1]), "seq"
    )
    scaled = feature_grads * ln_gain[None, :]
    grad_total, grad_inner = jnp.sum(
        exchange_gather(
            jnp.stack([jnp.sum(scaled, axis=1), jnp.sum(scaled * centred, axis=1)]), "tp"
        ),
        axis=0,
    )
    vis_grad = (
        inv_std[:, None]
        * (scaled - (grad_total / VF)[:, None] - centred * (grad_inner / VF)[:, None])
    ).astype(jnp.bfloat16)
    return (context.reshape(tok_rows, query_cols), vis_grad)


def solution(mesh):
    return jax.shard_map(
        on_device,
        mesh=mesh,
        in_specs=(
            P("seq", "tp"),
            P("tp"),
            P("tp", "seq"),
            P("seq", None),
            P(),
            P("seq", "tp"),
            P("seq", "tp"),
            P("seq", "tp"),
            P("seq"),
            P("seq"),
            P(),
            P(),
            P("seq", "tp"),
        ),
        out_specs=(P("seq", "tp"), P("seq", "tp")),
        check_vma=False,
    )
```

```python
import math

import jax
import jax.numpy as jnp
from jax import lax
from jax.sharding import PartitionSpec as P

VF = 12800
HEAD = 128
CAPD = 32
GROUP = 4


ln_eps = 1e-05
rms_eps = 1e-06
rope_base = 1000000.0
masked_score = -1e30


def shifted(x, axis, by):
    peers = lax.axis_size(axis)
    pairs = [(i, i + by) for i in range(peers) if 0 <= i + by < peers]
    return lax.ppermute(x, axis, pairs)


def bit_of(axis, b):
    return (lax.axis_index(axis) // (1 << b)) % 2


def bit_pairs(axis, b):
    peers = lax.axis_size(axis)
    return [(i, i ^ (1 << b)) for i in range(peers)]


def group_index(axis, bits):
    return sum(bit_of(axis, b) * (1 << k) for k, b in enumerate(bits))


def group_pairs(axis, bits, o):
    peers = lax.axis_size(axis)
    mask = sum(((o >> k) & 1) << b for k, b in enumerate(bits))
    return [(i, i ^ mask) for i in range(peers)]


def group_scatter(x, axis, bits, dim=0):
    me = group_index(axis, bits)
    acc = lax.dynamic_index_in_dim(x, me, dim, keepdims=False).astype(jnp.float32)
    for o in range(1, 1 << len(bits)):
        send = lax.dynamic_index_in_dim(x, jnp.bitwise_xor(me, o), dim, keepdims=False)
        got = lax.ppermute(send.astype(jnp.bfloat16), axis, group_pairs(axis, bits, o))
        acc = acc + got.astype(jnp.float32)
    return acc


def group_gather(x, axis, bits):
    me = group_index(axis, bits)
    g = 1 << len(bits)
    parts = [x] + [lax.ppermute(x, axis, group_pairs(axis, bits, o)) for o in range(1, g)]
    order = jnp.bitwise_xor(jnp.arange(g, dtype=jnp.int32), me)
    return jnp.take(jnp.stack(parts), order, axis=0)


def staged_scatter(x, axis, groups):
    acc = x
    for bits in groups:
        g = 1 << len(bits)
        lead = acc.reshape((acc.shape[0] // g, g) + acc.shape[1:])
        acc = group_scatter(lead, axis, bits, dim=1)
    return acc[0]


def staged_gather(x, axis, groups):
    acc = x
    for bits in groups:
        acc = group_gather(acc, axis, bits)
    count = len(groups)
    return acc.transpose(list(range(count - 1, -1, -1)) + list(range(count, acc.ndim)))


def exchange_sum(x, axis):
    got = lax.all_to_all(x.astype(jnp.bfloat16), axis, 0, 0, tiled=True)
    return jnp.sum(got.astype(jnp.float32), axis=0)


def exchange_gather(x, axis):
    peers = lax.axis_size(axis)
    return lax.all_to_all(jnp.broadcast_to(x[None], (peers,) + x.shape), axis, 0, 0, tiled=True)


def exchange_position(axis, groups, source):
    me = lax.axis_index(axis)
    place = jnp.zeros_like(source)
    step = 1
    for bits in groups:
        group_of = lambda d: sum(((d // (1 << b)) % 2) * (1 << k) for k, b in enumerate(bits))
        place = place + jnp.bitwise_xor(group_of(source), group_of(me)) * step
        step = step * (1 << len(bits))
    return place


def staged_gather_unordered(x, axis, groups):
    acc = x
    for bits in groups:
        g = 1 << len(bits)
        acc = jnp.stack([acc] + [lax.ppermute(acc, axis, group_pairs(axis, bits, o)) for o in range(1, g)])
    return acc


def log2(n):
    return n.bit_length() - 1


def rope_tables(positions, head_width):
    half = head_width // 2
    frequency = rope_base ** (-(jnp.arange(half).astype(jnp.float32) * 2.0 / head_width))
    angle = positions.astype(jnp.float32)[:, None] * frequency[None, :]
    return (jnp.cos(angle), jnp.sin(angle))


def rotate(values, cosine, sine):
    half = values.shape[-1] // 2
    first = values[..., :half]
    second = values[..., half:]
    cos_rows = cosine[:, None, :]
    sin_rows = sine[:, None, :]
    return jnp.concatenate(
        [first * cos_rows - second * sin_rows, second * cos_rows + first * sin_rows], axis=-1
    )


def unrotate(grads, cosine, sine):
    half = grads.shape[-1] // 2
    first = grads[..., :half]
    second = grads[..., half:]
    cos_rows = cosine[:, None, :]
    sin_rows = sine[:, None, :]
    return jnp.concatenate(
        [first * cos_rows + second * sin_rows, second * cos_rows - first * sin_rows], axis=-1
    )


def norm_backward(rows, grads, gain, axes):
    inv_rms = lax.rsqrt(jnp.mean(rows * rows, axis=axes, keepdims=True) + rms_eps)
    scaled = grads * gain
    inner = jnp.mean(rows * scaled, axis=axes, keepdims=True)
    return inv_rms * scaled - rows * (inv_rms * inv_rms * inv_rms) * inner


def attention_block(queries, keys, values, grads, allowed):
    scale = 1.0 / math.sqrt(queries.shape[-1])
    scores = jnp.einsum("qhgd,khd->hgqk", queries, keys, preferred_element_type=jnp.float32) * scale
    masked = jnp.where(allowed[None, None], scores, masked_score)
    peak = jnp.max(masked, axis=-1, keepdims=True)
    raised = jnp.where(allowed[None, None], jnp.exp(masked - peak), 0.0)
    shares = raised / jnp.sum(raised, axis=-1, keepdims=True)
    shares_low = shares.astype(jnp.bfloat16)
    context = jnp.einsum(
        "hgqk,khd->qhgd", shares_low, values, preferred_element_type=jnp.float32
    ).astype(jnp.bfloat16)
    share_grads = jnp.einsum("qhgd,khd->hgqk", grads, values, preferred_element_type=jnp.float32)
    delta = jnp.sum(shares * share_grads, axis=-1, keepdims=True)
    score_grads = (shares * (share_grads - delta) * scale).astype(jnp.bfloat16)
    query_grads = jnp.einsum(
        "hgqk,khd->qhgd", score_grads, keys, preferred_element_type=jnp.float32
    )
    key_grads = jnp.einsum(
        "hgqk,qhgd->khd", score_grads, queries, preferred_element_type=jnp.float32
    )
    value_grads = jnp.einsum(
        "hgqk,qhgd->khd", shares_low, grads, preferred_element_type=jnp.float32
    )
    return (context, query_grads, key_grads, value_grads)


def on_device(
    vis_feat,
    ln_gain,
    proj_weight,
    text_embed,
    rms_gain,
    wq,
    wk,
    wv,
    doc_ids,
    vis_slot,
    slot_token,
    token_slot,
    cotangent,
):
    seq_count = lax.axis_size("seq")
    my_index = lax.axis_index("seq")
    tok_rows = text_embed.shape[0]
    slot_cols = proj_weight.shape[1]
    features = vis_feat.astype(jnp.float32)
    tp_count = lax.axis_size("tp")
    tp_bits = log2(tp_count)
    seq_bits = log2(seq_count)
    tp_all = [list(range(tp_bits))]
    seq_up = [[0], [1, 2], [3, 4]] if seq_bits == 5 else [[b] for b in range(seq_bits)]
    seq_down = seq_up[::-1]
    row_total, row_squares = jnp.sum(
        exchange_gather(
            jnp.stack([jnp.sum(features, axis=1), jnp.sum(features * features, axis=1)]), "tp"
        ),
        axis=0,
    )
    row_mean = row_total / VF
    row_var = row_squares / VF - row_mean * row_mean
    inv_std = lax.rsqrt(row_var + ln_eps)
    centred = (features - row_mean[:, None]) * inv_std[:, None]
    vis_normed = (centred * ln_gain[None, :]).astype(jnp.bfloat16)
    vis_rows = vis_feat.shape[0]
    all_normed = staged_gather_unordered(vis_normed, "seq", seq_down)
    partial_embed = jnp.dot(
        all_normed.reshape(seq_count * vis_rows, vis_feat.shape[1]),
        proj_weight,
        preferred_element_type=jnp.float32,
    )
    slot_live = (slot_token >= 0)[:, None]
    slot_index = jnp.maximum(slot_token, 0)
    devices = seq_count * tp_count
    per = CAPD // tp_count
    token_place = (
        exchange_position("seq", seq_down, slot_index // vis_rows) * vis_rows + slot_index % vis_rows
    )
    route = (
        (token_place[:, None] == jnp.arange(seq_count * vis_rows, dtype=jnp.int32)[None, :])
        & slot_live
    ).astype(jnp.bfloat16)
    outgoing = jnp.dot(
        route, partial_embed.astype(jnp.bfloat16), preferred_element_type=jnp.float32
    ).reshape(devices, per, slot_cols)
    got = lax.all_to_all(outgoing.astype(jnp.bfloat16), ("seq", "tp"), 0, 0, tiled=True)
    mine = jnp.sum(
        got.reshape(seq_count, tp_count, per, slot_cols).astype(jnp.float32), axis=1
    ).astype(jnp.bfloat16)
    all_mine = exchange_gather(mine, "tp")
    arrived = all_mine.transpose(0, 2, 1, 3).reshape(CAPD, seq_count * slot_cols)
    lanes = jnp.arange(CAPD, dtype=jnp.int32)
    one_hot = (vis_slot[:, None] == lanes[None, :]).astype(jnp.bfloat16)
    placed = jnp.dot(one_hot, arrived, preferred_element_type=jnp.float32).astype(jnp.bfloat16)
    is_image = vis_slot >= 0
    hidden = jnp.where(is_image[:, None], placed, text_embed)
    hidden_wide = hidden.astype(jnp.float32)
    inv_rms = lax.rsqrt(jnp.mean(hidden_wide * hidden_wide, axis=1, keepdims=True) + rms_eps)
    normed = (hidden_wide * inv_rms * rms_gain[None, :]).astype(jnp.bfloat16)
    stacked = jnp.concatenate([wq, wk, wv], axis=1)
    query_cols = wq.shape[1]
    key_cols = wk.shape[1]
    gathered = lax.all_gather(stacked, "seq", axis=0, tiled=True)
    projected = jnp.dot(normed, gathered, preferred_element_type=jnp.float32)
    local_heads = query_cols // HEAD
    local_groups = key_cols // HEAD
    positions = my_index * tok_rows + jnp.arange(tok_rows, dtype=jnp.int32)
    cosine, sine = rope_tables(positions, HEAD)
    queries = rotate(
        projected[:, :query_cols].reshape(tok_rows, local_heads, HEAD), cosine, sine
    ).astype(jnp.bfloat16)
    keys = rotate(
        projected[:, query_cols : query_cols + key_cols].reshape(tok_rows, local_groups, HEAD),
        cosine,
        sine,
    ).astype(jnp.bfloat16)
    values = (
        projected[:, query_cols + key_cols :]
        .astype(jnp.bfloat16)
        .reshape(tok_rows, local_groups, HEAD)
    )
    doc_marks = (doc_ids + 1).astype(jnp.bfloat16)
    prev_keys, prev_values, prev_docs = shifted((keys, values, doc_marks), "seq", 1)
    all_keys = jnp.concatenate([prev_keys, keys], axis=0)
    all_values = jnp.concatenate([prev_values, values], axis=0)
    query_docs = doc_marks.astype(jnp.float32)
    key_docs = jnp.concatenate([prev_docs.astype(jnp.float32), query_docs], axis=0)
    key_positions = jnp.concatenate([positions - tok_rows, positions], axis=0)
    allowed = (key_docs[None, :] == query_docs[:, None]) & (
        key_positions[None, :] <= positions[:, None]
    )
    grads = cotangent.reshape(tok_rows, local_groups, GROUP, HEAD)
    context, query_grads, key_grads, value_grads = attention_block(
        queries.reshape(tok_rows, local_groups, GROUP, HEAD), all_keys, all_values, grads, allowed
    )
    back_keys, back_values = (
        shifted(key_grads[:tok_rows].astype(jnp.bfloat16), "seq", -1).astype(jnp.float32),
        shifted(value_grads[:tok_rows].astype(jnp.bfloat16), "seq", -1).astype(jnp.float32),
    )
    key_total = key_grads[tok_rows:] + back_keys
    value_total = value_grads[tok_rows:] + back_values
    query_pre = (
        unrotate(query_grads.reshape(tok_rows, local_heads, HEAD), cosine, sine)
        .astype(jnp.bfloat16)
        .reshape(tok_rows, query_cols)
    )
    key_pre = unrotate(key_total, cosine, sine).astype(jnp.bfloat16).reshape(tok_rows, key_cols)
    value_pre = value_total.astype(jnp.bfloat16).reshape(tok_rows, key_cols)
    proj_grads = jnp.concatenate([query_pre, key_pre, value_pre], axis=1)
    selected = lax.dot_general(
        one_hot, proj_grads, (((0,), (0,)), ((), ())), preferred_element_type=jnp.float32
    ).astype(jnp.bfloat16)
    norm_part = jnp.einsum(
        "tkc,jrc->jtkr",
        selected.reshape(tp_count, per, selected.shape[1]),
        gathered.reshape(seq_count, slot_cols, gathered.shape[1]),
        preferred_element_type=jnp.float32,
    )
    embed_part = norm_backward(
        all_mine.transpose(1, 0, 2, 3).astype(jnp.float32),
        norm_part,
        rms_gain.reshape(seq_count, 1, 1, slot_cols),
        (0, 3),
    )
    got_back = lax.all_to_all(
        embed_part.astype(jnp.bfloat16).reshape(devices, per, slot_cols),
        ("seq", "tp"), 0, 0, tiled=True,
    )
    mine_back = jnp.sum(
        got_back.reshape(seq_count, tp_count, per, slot_cols).astype(jnp.float32), axis=1
    ).astype(jnp.bfloat16)
    all_back = exchange_gather(mine_back, "tp").reshape(tp_count * seq_count * per, slot_cols)
    block_of = token_slot // CAPD
    lane_of = token_slot % CAPD
    back_index = (lane_of // per) * (seq_count * per) + block_of * per + lane_of % per
    pick = (
        back_index[:, None] == jnp.arange(all_back.shape[0], dtype=jnp.int32)[None, :]
    ).astype(jnp.bfloat16)
    token_grads = jnp.dot(pick, all_back, preferred_element_type=jnp.float32).astype(jnp.bfloat16)
    own_rows = vis_feat.shape[0]
    feature_part = lax.dot_general(
        token_grads, proj_weight, (((1,), (1,)), ((), ())), preferred_element_type=jnp.float32
    )
    feature_grads = exchange_sum(
        feature_part.reshape(seq_count, own_rows, feature_part.shape[1]), "seq"
    )
    scaled = feature_grads * ln_gain[None, :]
    grad_total, grad_inner = jnp.sum(
        exchange_gather(
            jnp.stack([jnp.sum(scaled, axis=1), jnp.sum(scaled * centred, axis=1)]), "tp"
        ),
        axis=0,
    )
    vis_grad = (
        inv_std[:, None]
        * (scaled - (grad_total / VF)[:, None] - centred * (grad_inner / VF)[:, None])
    ).astype(jnp.bfloat16)
    return (context.reshape(tok_rows, query_cols), vis_grad)


def solution(mesh):
    return jax.shard_map(
        on_device,
        mesh=mesh,
        in_specs=(
            P("seq", "tp"),
            P("tp"),
            P("tp", "seq"),
            P("seq", None),
            P(),
            P("seq", "tp"),
            P("seq", "tp"),
            P("seq", "tp"),
            P("seq"),
            P("seq"),
            P(),
            P(),
            P("seq", "tp"),
        ),
        out_specs=(P("seq", "tp"), P("seq", "tp")),
        check_vma=False,
    )
```

```python
import math

import jax
import jax.numpy as jnp
from jax import lax
from jax.sharding import PartitionSpec as P

VF = 12800
HEAD = 128
CAPD = 32
GROUP = 4


ln_eps = 1e-05
rms_eps = 1e-06
rope_base = 1000000.0
masked_score = -1e30


def shifted(x, axis, by):
    peers = lax.axis_size(axis)
    pairs = [(i, i + by) for i in range(peers) if 0 <= i + by < peers]
    return lax.ppermute(x, axis, pairs)


def bit_of(axis, b):
    return (lax.axis_index(axis) // (1 << b)) % 2


def bit_pairs(axis, b):
    peers = lax.axis_size(axis)
    return [(i, i ^ (1 << b)) for i in range(peers)]


def group_index(axis, bits):
    return sum(bit_of(axis, b) * (1 << k) for k, b in enumerate(bits))


def group_pairs(axis, bits, o):
    peers = lax.axis_size(axis)
    mask = sum(((o >> k) & 1) << b for k, b in enumerate(bits))
    return [(i, i ^ mask) for i in range(peers)]


def group_scatter(x, axis, bits, dim=0):
    me = group_index(axis, bits)
    acc = lax.dynamic_index_in_dim(x, me, dim, keepdims=False).astype(jnp.float32)
    for o in range(1, 1 << len(bits)):
        send = lax.dynamic_index_in_dim(x, jnp.bitwise_xor(me, o), dim, keepdims=False)
        got = lax.ppermute(send.astype(jnp.bfloat16), axis, group_pairs(axis, bits, o))
        acc = acc + got.astype(jnp.float32)
    return acc


def group_gather(x, axis, bits):
    me = group_index(axis, bits)
    g = 1 << len(bits)
    parts = [x] + [lax.ppermute(x, axis, group_pairs(axis, bits, o)) for o in range(1, g)]
    order = jnp.bitwise_xor(jnp.arange(g, dtype=jnp.int32), me)
    return jnp.take(jnp.stack(parts), order, axis=0)


def staged_scatter(x, axis, groups):
    acc = x
    for bits in groups:
        g = 1 << len(bits)
        lead = acc.reshape((acc.shape[0] // g, g) + acc.shape[1:])
        acc = group_scatter(lead, axis, bits, dim=1)
    return acc[0]


def staged_gather(x, axis, groups):
    acc = x
    for bits in groups:
        acc = group_gather(acc, axis, bits)
    count = len(groups)
    return acc.transpose(list(range(count - 1, -1, -1)) + list(range(count, acc.ndim)))


def exchange_sum(x, axis):
    got = lax.all_to_all(x.astype(jnp.bfloat16), axis, 0, 0, tiled=True)
    return jnp.sum(got.astype(jnp.float32), axis=0)


def exchange_gather(x, axis):
    peers = lax.axis_size(axis)
    return lax.all_to_all(jnp.broadcast_to(x[None], (peers,) + x.shape), axis, 0, 0, tiled=True)


def exchange_position(axis, groups, source):
    me = lax.axis_index(axis)
    place = jnp.zeros_like(source)
    step = 1
    for bits in groups:
        group_of = lambda d: sum(((d // (1 << b)) % 2) * (1 << k) for k, b in enumerate(bits))
        place = place + jnp.bitwise_xor(group_of(source), group_of(me)) * step
        step = step * (1 << len(bits))
    return place


def staged_gather_unordered(x, axis, groups):
    acc = x
    for bits in groups:
        g = 1 << len(bits)
        acc = jnp.stack([acc] + [lax.ppermute(acc, axis, group_pairs(axis, bits, o)) for o in range(1, g)])
    return acc


def log2(n):
    return n.bit_length() - 1


def rope_tables(positions, head_width):
    half = head_width // 2
    frequency = rope_base ** (-(jnp.arange(half).astype(jnp.float32) * 2.0 / head_width))
    angle = positions.astype(jnp.float32)[:, None] * frequency[None, :]
    return (jnp.cos(angle), jnp.sin(angle))


def rotate(values, cosine, sine):
    half = values.shape[-1] // 2
    first = values[..., :half]
    second = values[..., half:]
    cos_rows = cosine[:, None, :]
    sin_rows = sine[:, None, :]
    return jnp.concatenate(
        [first * cos_rows - second * sin_rows, second * cos_rows + first * sin_rows], axis=-1
    )


def unrotate(grads, cosine, sine):
    half = grads.shape[-1] // 2
    first = grads[..., :half]
    second = grads[..., half:]
    cos_rows = cosine[:, None, :]
    sin_rows = sine[:, None, :]
    return jnp.concatenate(
        [first * cos_rows + second * sin_rows, second * cos_rows - first * sin_rows], axis=-1
    )


def norm_backward(rows, grads, gain, axes):
    inv_rms = lax.rsqrt(jnp.mean(rows * rows, axis=axes, keepdims=True) + rms_eps)
    scaled = grads * gain
    inner = jnp.mean(rows * scaled, axis=axes, keepdims=True)
    return inv_rms * scaled - rows * (inv_rms * inv_rms * inv_rms) * inner


def attention_block(queries, keys, values, grads, allowed):
    scale = 1.0 / math.sqrt(queries.shape[-1])
    scores = jnp.einsum("qhgd,khd->hgqk", queries, keys, preferred_element_type=jnp.float32) * scale
    masked = jnp.where(allowed[None, None], scores, masked_score)
    peak = jnp.max(masked, axis=-1, keepdims=True)
    raised = jnp.where(allowed[None, None], jnp.exp(masked - peak), 0.0)
    shares = raised / jnp.sum(raised, axis=-1, keepdims=True)
    shares_low = shares.astype(jnp.bfloat16)
    context = jnp.einsum(
        "hgqk,khd->qhgd", shares_low, values, preferred_element_type=jnp.float32
    ).astype(jnp.bfloat16)
    share_grads = jnp.einsum("qhgd,khd->hgqk", grads, values, preferred_element_type=jnp.float32)
    delta = jnp.sum(shares * share_grads, axis=-1, keepdims=True)
    score_grads = (shares * (share_grads - delta) * scale).astype(jnp.bfloat16)
    query_grads = jnp.einsum(
        "hgqk,khd->qhgd", score_grads, keys, preferred_element_type=jnp.float32
    )
    key_grads = jnp.einsum(
        "hgqk,qhgd->khd", score_grads, queries, preferred_element_type=jnp.float32
    )
    value_grads = jnp.einsum(
        "hgqk,qhgd->khd", shares_low, grads, preferred_element_type=jnp.float32
    )
    return (context, query_grads, key_grads, value_grads)


def on_device(
    vis_feat,
    ln_gain,
    proj_weight,
    text_embed,
    rms_gain,
    wq,
    wk,
    wv,
    doc_ids,
    vis_slot,
    slot_token,
    token_slot,
    cotangent,
):
    seq_count = lax.axis_size("seq")
    my_index = lax.axis_index("seq")
    tok_rows = text_embed.shape[0]
    slot_cols = proj_weight.shape[1]
    features = vis_feat.astype(jnp.float32)
    tp_count = lax.axis_size("tp")
    tp_bits = log2(tp_count)
    seq_bits = log2(seq_count)
    tp_all = [list(range(tp_bits))]
    seq_up = [[0], [1, 2], [3, 4]] if seq_bits == 5 else [[b] for b in range(seq_bits)]
    seq_down = seq_up[::-1]
    row_total, row_squares = jnp.sum(
        exchange_gather(
            jnp.stack([jnp.sum(features, axis=1), jnp.sum(features * features, axis=1)]), "tp"
        ),
        axis=0,
    )
    row_mean = row_total / VF
    row_var = row_squares / VF - row_mean * row_mean
    inv_std = lax.rsqrt(row_var + ln_eps)
    centred = (features - row_mean[:, None]) * inv_std[:, None]
    vis_normed = (centred * ln_gain[None, :]).astype(jnp.bfloat16)
    vis_rows = vis_feat.shape[0]
    all_normed = staged_gather_unordered(vis_normed, "seq", seq_down)
    partial_embed = jnp.dot(
        all_normed.reshape(seq_count * vis_rows, vis_feat.shape[1]),
        proj_weight,
        preferred_element_type=jnp.float32,
    )
    slot_live = (slot_token >= 0)[:, None]
    slot_index = jnp.maximum(slot_token, 0)
    devices = seq_count * tp_count
    per = CAPD // tp_count
    token_place = (
        exchange_position("seq", seq_down, slot_index // vis_rows) * vis_rows + slot_index % vis_rows
    )
    route = (
        (token_place[:, None] == jnp.arange(seq_count * vis_rows, dtype=jnp.int32)[None, :])
        & slot_live
    ).astype(jnp.bfloat16)
    outgoing = jnp.dot(
        route, partial_embed.astype(jnp.bfloat16), preferred_element_type=jnp.float32
    ).reshape(devices, per, slot_cols)
    got = lax.all_to_all(outgoing.astype(jnp.bfloat16), ("seq", "tp"), 0, 0, tiled=True)
    mine = jnp.sum(
        got.reshape(seq_count, tp_count, per, slot_cols).astype(jnp.float32), axis=1
    ).astype(jnp.bfloat16)
    stacked = jnp.concatenate([wq, wk, wv], axis=1)
    gathered = lax.all_gather(stacked, "seq", axis=0, tiled=True)
    mine, gathered = lax.optimization_barrier((mine, gathered))
    all_mine = exchange_gather(mine, "tp")
    arrived = all_mine.transpose(0, 2, 1, 3).reshape(CAPD, seq_count * slot_cols)
    lanes = jnp.arange(CAPD, dtype=jnp.int32)
    head_rows = tok_rows - CAPD
    tail_slot = vis_slot[head_rows:]
    one_hot = (tail_slot[:, None] == lanes[None, :]).astype(jnp.bfloat16)
    placed = jnp.dot(one_hot, arrived, preferred_element_type=jnp.float32).astype(jnp.bfloat16)
    hidden_tail = jnp.where((tail_slot >= 0)[:, None], placed, text_embed[head_rows:])

    def rms_normed(hidden):
        hidden_wide = hidden.astype(jnp.float32)
        inv_rms = lax.rsqrt(jnp.mean(hidden_wide * hidden_wide, axis=1, keepdims=True) + rms_eps)
        return (hidden_wide * inv_rms * rms_gain[None, :]).astype(jnp.bfloat16)

    query_cols = wq.shape[1]
    key_cols = wk.shape[1]
    projected_text = jnp.dot(rms_normed(text_embed), gathered, preferred_element_type=jnp.float32)
    projected_tail = jnp.dot(rms_normed(hidden_tail), gathered, preferred_element_type=jnp.float32)
    projected = lax.dynamic_update_slice_in_dim(projected_text, projected_tail, head_rows, 0)
    local_heads = query_cols // HEAD
    local_groups = key_cols // HEAD
    positions = my_index * tok_rows + jnp.arange(tok_rows, dtype=jnp.int32)
    cosine, sine = rope_tables(positions, HEAD)
    queries = rotate(
        projected[:, :query_cols].reshape(tok_rows, local_heads, HEAD), cosine, sine
    ).astype(jnp.bfloat16)
    keys = rotate(
        projected[:, query_cols : query_cols + key_cols].reshape(tok_rows, local_groups, HEAD),
        cosine,
        sine,
    ).astype(jnp.bfloat16)
    values = (
        projected[:, query_cols + key_cols :]
        .astype(jnp.bfloat16)
        .reshape(tok_rows, local_groups, HEAD)
    )
    doc_marks = (doc_ids + 1).astype(jnp.bfloat16)
    prev_keys, prev_values, prev_docs = shifted((keys, values, doc_marks), "seq", 1)
    all_keys = jnp.concatenate([prev_keys, keys], axis=0)
    all_values = jnp.concatenate([prev_values, values], axis=0)
    query_docs = doc_marks.astype(jnp.float32)
    key_docs = jnp.concatenate([prev_docs.astype(jnp.float32), query_docs], axis=0)
    key_positions = jnp.concatenate([positions - tok_rows, positions], axis=0)
    allowed = (key_docs[None, :] == query_docs[:, None]) & (
        key_positions[None, :] <= positions[:, None]
    )
    grads = cotangent.reshape(tok_rows, local_groups, GROUP, HEAD)
    context, query_grads, key_grads, value_grads = attention_block(
        queries.reshape(tok_rows, local_groups, GROUP, HEAD), all_keys, all_values, grads, allowed
    )
    back_keys, back_values = (
        shifted(key_grads[:tok_rows].astype(jnp.bfloat16), "seq", -1).astype(jnp.float32),
        shifted(value_grads[:tok_rows].astype(jnp.bfloat16), "seq", -1).astype(jnp.float32),
    )
    key_total = key_grads[tok_rows:] + back_keys
    value_total = value_grads[tok_rows:] + back_values
    query_pre = (
        unrotate(query_grads.reshape(tok_rows, local_heads, HEAD), cosine, sine)
        .astype(jnp.bfloat16)
        .reshape(tok_rows, query_cols)
    )
    key_pre = unrotate(key_total, cosine, sine).astype(jnp.bfloat16).reshape(tok_rows, key_cols)
    value_pre = value_total.astype(jnp.bfloat16).reshape(tok_rows, key_cols)
    proj_grads = jnp.concatenate([query_pre, key_pre, value_pre], axis=1)
    selected = lax.dot_general(
        one_hot, proj_grads[head_rows:], (((0,), (0,)), ((), ())), preferred_element_type=jnp.float32
    ).astype(jnp.bfloat16)
    norm_part = jnp.einsum(
        "tkc,jrc->jtkr",
        selected.reshape(tp_count, per, selected.shape[1]),
        gathered.reshape(seq_count, slot_cols, gathered.shape[1]),
        preferred_element_type=jnp.float32,
    )
    embed_part = norm_backward(
        all_mine.transpose(1, 0, 2, 3).astype(jnp.float32),
        norm_part,
        rms_gain.reshape(seq_count, 1, 1, slot_cols),
        (0, 3),
    )
    got_back = lax.all_to_all(
        embed_part.astype(jnp.bfloat16).reshape(devices, per, slot_cols),
        ("seq", "tp"), 0, 0, tiled=True,
    )
    mine_back = jnp.sum(
        got_back.reshape(seq_count, tp_count, per, slot_cols).astype(jnp.float32), axis=1
    ).astype(jnp.bfloat16)
    all_back = exchange_gather(mine_back, "tp").reshape(tp_count * seq_count * per, slot_cols)
    block_of = token_slot // CAPD
    lane_of = token_slot % CAPD
    back_index = (lane_of // per) * (seq_count * per) + block_of * per + lane_of % per
    pick = (
        back_index[:, None] == jnp.arange(all_back.shape[0], dtype=jnp.int32)[None, :]
    ).astype(jnp.bfloat16)
    token_grads = jnp.dot(pick, all_back, preferred_element_type=jnp.float32).astype(jnp.bfloat16)
    own_rows = vis_feat.shape[0]
    feature_part = lax.dot_general(
        token_grads, proj_weight, (((1,), (1,)), ((), ())), preferred_element_type=jnp.float32
    )
    feature_grads = exchange_sum(
        feature_part.reshape(seq_count, own_rows, feature_part.shape[1]), "seq"
    )
    scaled = feature_grads * ln_gain[None, :]
    grad_total, grad_inner = jnp.sum(
        exchange_gather(
            jnp.stack([jnp.sum(scaled, axis=1), jnp.sum(scaled * centred, axis=1)]), "tp"
        ),
        axis=0,
    )
    vis_grad = (
        inv_std[:, None]
        * (scaled - (grad_total / VF)[:, None] - centred * (grad_inner / VF)[:, None])
    ).astype(jnp.bfloat16)
    return (context.reshape(tok_rows, query_cols), vis_grad)


def solution(mesh):
    return jax.shard_map(
        on_device,
        mesh=mesh,
        in_specs=(
            P("seq", "tp"),
            P("tp"),
            P("tp", "seq"),
            P("seq", None),
            P(),
            P("seq", "tp"),
            P("seq", "tp"),
            P("seq", "tp"),
            P("seq"),
            P("seq"),
            P(),
            P(),
            P("seq", "tp"),
        ),
        out_specs=(P("seq", "tp"), P("seq", "tp")),
        check_vma=False,
    )
```

```python
import math

import jax
import jax.numpy as jnp
from jax import lax
from jax.sharding import PartitionSpec as P

VF = 12800
HEAD = 128
CAPD = 32
GROUP = 4


ln_eps = 1e-05
rms_eps = 1e-06
rope_base = 1000000.0
masked_score = -1e30


def shifted(x, axis, by):
    peers = lax.axis_size(axis)
    pairs = [(i, i + by) for i in range(peers) if 0 <= i + by < peers]
    return lax.ppermute(x, axis, pairs)


def bit_of(axis, b):
    return (lax.axis_index(axis) // (1 << b)) % 2


def bit_pairs(axis, b):
    peers = lax.axis_size(axis)
    return [(i, i ^ (1 << b)) for i in range(peers)]


def group_index(axis, bits):
    return sum(bit_of(axis, b) * (1 << k) for k, b in enumerate(bits))


def group_pairs(axis, bits, o):
    peers = lax.axis_size(axis)
    mask = sum(((o >> k) & 1) << b for k, b in enumerate(bits))
    return [(i, i ^ mask) for i in range(peers)]


def group_scatter(x, axis, bits, dim=0):
    me = group_index(axis, bits)
    acc = lax.dynamic_index_in_dim(x, me, dim, keepdims=False).astype(jnp.float32)
    for o in range(1, 1 << len(bits)):
        send = lax.dynamic_index_in_dim(x, jnp.bitwise_xor(me, o), dim, keepdims=False)
        got = lax.ppermute(send.astype(jnp.bfloat16), axis, group_pairs(axis, bits, o))
        acc = acc + got.astype(jnp.float32)
    return acc


def group_gather(x, axis, bits):
    me = group_index(axis, bits)
    g = 1 << len(bits)
    parts = [x] + [lax.ppermute(x, axis, group_pairs(axis, bits, o)) for o in range(1, g)]
    order = jnp.bitwise_xor(jnp.arange(g, dtype=jnp.int32), me)
    return jnp.take(jnp.stack(parts), order, axis=0)


def staged_scatter(x, axis, groups):
    acc = x
    for bits in groups:
        g = 1 << len(bits)
        lead = acc.reshape((acc.shape[0] // g, g) + acc.shape[1:])
        acc = group_scatter(lead, axis, bits, dim=1)
    return acc[0]


def staged_gather(x, axis, groups):
    acc = x
    for bits in groups:
        acc = group_gather(acc, axis, bits)
    count = len(groups)
    return acc.transpose(list(range(count - 1, -1, -1)) + list(range(count, acc.ndim)))


def exchange_sum(x, axis):
    got = lax.all_to_all(x.astype(jnp.bfloat16), axis, 0, 0, tiled=True)
    return jnp.sum(got.astype(jnp.float32), axis=0)


def exchange_gather(x, axis):
    peers = lax.axis_size(axis)
    return lax.all_to_all(jnp.broadcast_to(x[None], (peers,) + x.shape), axis, 0, 0, tiled=True)


def exchange_position(axis, groups, source):
    me = lax.axis_index(axis)
    place = jnp.zeros_like(source)
    step = 1
    for bits in groups:
        group_of = lambda d: sum(((d // (1 << b)) % 2) * (1 << k) for k, b in enumerate(bits))
        place = place + jnp.bitwise_xor(group_of(source), group_of(me)) * step
        step = step * (1 << len(bits))
    return place


def staged_gather_unordered(x, axis, groups):
    acc = x
    for bits in groups:
        g = 1 << len(bits)
        acc = jnp.stack([acc] + [lax.ppermute(acc, axis, group_pairs(axis, bits, o)) for o in range(1, g)])
    return acc


def log2(n):
    return n.bit_length() - 1


def rope_tables(positions, head_width):
    half = head_width // 2
    frequency = rope_base ** (-(jnp.arange(half).astype(jnp.float32) * 2.0 / head_width))
    angle = positions.astype(jnp.float32)[:, None] * frequency[None, :]
    return (jnp.cos(angle), jnp.sin(angle))


def rotate(values, cosine, sine):
    half = values.shape[-1] // 2
    first = values[..., :half]
    second = values[..., half:]
    cos_rows = cosine[:, None, :]
    sin_rows = sine[:, None, :]
    return jnp.concatenate(
        [first * cos_rows - second * sin_rows, second * cos_rows + first * sin_rows], axis=-1
    )


def unrotate(grads, cosine, sine):
    half = grads.shape[-1] // 2
    first = grads[..., :half]
    second = grads[..., half:]
    cos_rows = cosine[:, None, :]
    sin_rows = sine[:, None, :]
    return jnp.concatenate(
        [first * cos_rows + second * sin_rows, second * cos_rows - first * sin_rows], axis=-1
    )


def norm_backward(rows, grads, gain, axes):
    inv_rms = lax.rsqrt(jnp.mean(rows * rows, axis=axes, keepdims=True) + rms_eps)
    scaled = grads * gain
    inner = jnp.mean(rows * scaled, axis=axes, keepdims=True)
    return inv_rms * scaled - rows * (inv_rms * inv_rms * inv_rms) * inner


def attention_block(queries, keys, values, grads, allowed):
    scale = 1.0 / math.sqrt(queries.shape[-1])
    scores = jnp.einsum("qhgd,khd->hgqk", queries, keys, preferred_element_type=jnp.float32) * scale
    masked = jnp.where(allowed[None, None], scores, masked_score)
    peak = jnp.max(masked, axis=-1, keepdims=True)
    raised = jnp.where(allowed[None, None], jnp.exp(masked - peak), 0.0)
    shares = raised / jnp.sum(raised, axis=-1, keepdims=True)
    shares_low = shares.astype(jnp.bfloat16)
    context = jnp.einsum(
        "hgqk,khd->qhgd", shares_low, values, preferred_element_type=jnp.float32
    ).astype(jnp.bfloat16)
    share_grads = jnp.einsum("qhgd,khd->hgqk", grads, values, preferred_element_type=jnp.float32)
    delta = jnp.sum(shares * share_grads, axis=-1, keepdims=True)
    score_grads = (shares * (share_grads - delta) * scale).astype(jnp.bfloat16)
    query_grads = jnp.einsum(
        "hgqk,khd->qhgd", score_grads, keys, preferred_element_type=jnp.float32
    )
    key_grads = jnp.einsum(
        "hgqk,qhgd->khd", score_grads, queries, preferred_element_type=jnp.float32
    )
    value_grads = jnp.einsum(
        "hgqk,qhgd->khd", shares_low, grads, preferred_element_type=jnp.float32
    )
    return (context, query_grads, key_grads, value_grads)


def on_device(
    vis_feat,
    ln_gain,
    proj_weight,
    text_embed,
    rms_gain,
    wq,
    wk,
    wv,
    doc_ids,
    vis_slot,
    slot_token,
    token_slot,
    cotangent,
):
    seq_count = lax.axis_size("seq")
    my_index = lax.axis_index("seq")
    tok_rows = text_embed.shape[0]
    slot_cols = proj_weight.shape[1]
    features = vis_feat.astype(jnp.float32)
    tp_count = lax.axis_size("tp")
    tp_bits = log2(tp_count)
    seq_bits = log2(seq_count)
    tp_all = [list(range(tp_bits))]
    seq_up = [[0], [1, 2], [3, 4]] if seq_bits == 5 else [[b] for b in range(seq_bits)]
    seq_down = seq_up[::-1]
    row_total, row_squares = jnp.sum(
        exchange_gather(
            jnp.stack([jnp.sum(features, axis=1), jnp.sum(features * features, axis=1)]), "tp"
        ),
        axis=0,
    )
    row_mean = row_total / VF
    row_var = row_squares / VF - row_mean * row_mean
    inv_std = lax.rsqrt(row_var + ln_eps)
    centred = (features - row_mean[:, None]) * inv_std[:, None]
    vis_normed = (centred * ln_gain[None, :]).astype(jnp.bfloat16)
    vis_rows = vis_feat.shape[0]
    all_normed = staged_gather_unordered(vis_normed, "seq", seq_down)
    partial_embed = jnp.dot(
        all_normed.reshape(seq_count * vis_rows, vis_feat.shape[1]),
        proj_weight,
        preferred_element_type=jnp.float32,
    )
    slot_live = (slot_token >= 0)[:, None]
    slot_index = jnp.maximum(slot_token, 0)
    devices = seq_count * tp_count
    per = CAPD // tp_count
    token_place = (
        exchange_position("seq", seq_down, slot_index // vis_rows) * vis_rows + slot_index % vis_rows
    )
    route = (
        (token_place[:, None] == jnp.arange(seq_count * vis_rows, dtype=jnp.int32)[None, :])
        & slot_live
    ).astype(jnp.bfloat16)
    outgoing = jnp.dot(
        route, partial_embed.astype(jnp.bfloat16), preferred_element_type=jnp.float32
    ).reshape(devices, per, slot_cols)
    got = lax.all_to_all(outgoing.astype(jnp.bfloat16), ("seq", "tp"), 0, 0, tiled=True)
    mine = jnp.sum(
        got.reshape(seq_count, tp_count, per, slot_cols).astype(jnp.float32), axis=1
    ).astype(jnp.bfloat16)
    all_mine = exchange_gather(mine, "tp")
    arrived = all_mine.transpose(0, 2, 1, 3).reshape(CAPD, seq_count * slot_cols)
    lanes = jnp.arange(CAPD, dtype=jnp.int32)
    one_hot = (vis_slot[:, None] == lanes[None, :]).astype(jnp.bfloat16)
    placed = jnp.dot(one_hot, arrived, preferred_element_type=jnp.float32).astype(jnp.bfloat16)
    is_image = vis_slot >= 0
    hidden = jnp.where(is_image[:, None], placed, text_embed)
    hidden_wide = hidden.astype(jnp.float32)
    inv_rms = lax.rsqrt(jnp.mean(hidden_wide * hidden_wide, axis=1, keepdims=True) + rms_eps)
    normed = (hidden_wide * inv_rms * rms_gain[None, :]).astype(jnp.bfloat16)
    stacked = jnp.concatenate([wq, wk, wv], axis=1)
    query_cols = wq.shape[1]
    key_cols = wk.shape[1]
    gathered = lax.all_gather(stacked, "seq", axis=0, tiled=True)
    projected = jnp.dot(normed, gathered, preferred_element_type=jnp.float32)
    local_heads = query_cols // HEAD
    local_groups = key_cols // HEAD
    positions = my_index * tok_rows + jnp.arange(tok_rows, dtype=jnp.int32)
    cosine, sine = rope_tables(positions, HEAD)
    queries = rotate(
        projected[:, :query_cols].reshape(tok_rows, local_heads, HEAD), cosine, sine
    ).astype(jnp.bfloat16)
    keys = rotate(
        projected[:, query_cols : query_cols + key_cols].reshape(tok_rows, local_groups, HEAD),
        cosine,
        sine,
    ).astype(jnp.bfloat16)
    values = (
        projected[:, query_cols + key_cols :]
        .astype(jnp.bfloat16)
        .reshape(tok_rows, local_groups, HEAD)
    )
    doc_marks = (doc_ids + 1).astype(jnp.bfloat16)
    prev_keys, prev_values, prev_docs = shifted((keys, values, doc_marks), "seq", 1)
    all_keys = jnp.concatenate([prev_keys, keys], axis=0)
    all_values = jnp.concatenate([prev_values, values], axis=0)
    query_docs = doc_marks.astype(jnp.float32)
    key_docs = jnp.concatenate([prev_docs.astype(jnp.float32), query_docs], axis=0)
    key_positions = jnp.concatenate([positions - tok_rows, positions], axis=0)
    allowed = (key_docs[None, :] == query_docs[:, None]) & (
        key_positions[None, :] <= positions[:, None]
    )
    grads = cotangent.reshape(tok_rows, local_groups, GROUP, HEAD)
    context, query_grads, key_grads, value_grads = attention_block(
        queries.reshape(tok_rows, local_groups, GROUP, HEAD), all_keys, all_values, grads, allowed
    )
    back_keys, back_values = (
        shifted(key_grads[:tok_rows].astype(jnp.bfloat16), "seq", -1).astype(jnp.float32),
        shifted(value_grads[:tok_rows].astype(jnp.bfloat16), "seq", -1).astype(jnp.float32),
    )
    key_total = key_grads[tok_rows:] + back_keys
    value_total = value_grads[tok_rows:] + back_values
    query_pre = (
        unrotate(query_grads.reshape(tok_rows, local_heads, HEAD), cosine, sine)
        .astype(jnp.bfloat16)
        .reshape(tok_rows, query_cols)
    )
    key_pre = unrotate(key_total, cosine, sine).astype(jnp.bfloat16).reshape(tok_rows, key_cols)
    value_pre = value_total.astype(jnp.bfloat16).reshape(tok_rows, key_cols)
    proj_grads = jnp.concatenate([query_pre, key_pre, value_pre], axis=1)
    selected = lax.dot_general(
        one_hot, proj_grads, (((0,), (0,)), ((), ())), preferred_element_type=jnp.float32
    ).astype(jnp.bfloat16)
    norm_part = jnp.einsum(
        "tkc,jrc->jtkr",
        selected.reshape(tp_count, per, selected.shape[1]),
        gathered.reshape(seq_count, slot_cols, gathered.shape[1]),
        preferred_element_type=jnp.float32,
    )
    embed_part = norm_backward(
        all_mine.transpose(1, 0, 2, 3).astype(jnp.float32),
        norm_part,
        rms_gain.reshape(seq_count, 1, 1, slot_cols),
        (0, 3),
    )
    got_back = lax.all_to_all(
        embed_part.astype(jnp.bfloat16).reshape(devices, per, slot_cols),
        ("seq", "tp"), 0, 0, tiled=True,
    )
    mine_back = jnp.sum(
        got_back.reshape(seq_count, tp_count, per, slot_cols).astype(jnp.float32), axis=1
    ).astype(jnp.bfloat16)
    all_back = exchange_gather(mine_back, "tp").reshape(tp_count * seq_count * per, slot_cols)
    block_of = token_slot // CAPD
    lane_of = token_slot % CAPD
    back_index = (lane_of // per) * (seq_count * per) + block_of * per + lane_of % per
    pick = (
        back_index[:, None] == jnp.arange(all_back.shape[0], dtype=jnp.int32)[None, :]
    ).astype(jnp.bfloat16)
    token_grads = jnp.dot(pick, all_back, preferred_element_type=jnp.float32).astype(jnp.bfloat16)
    own_rows = vis_feat.shape[0]
    feature_part = jnp.einsum(
        "bqd,fd->bqf",
        token_grads.reshape(seq_count, own_rows, slot_cols),
        proj_weight,
        preferred_element_type=jnp.float32,
    )
    feature_grads = exchange_sum(feature_part, "seq")
    scaled = feature_grads * ln_gain[None, :]
    grad_total, grad_inner = jnp.sum(
        exchange_gather(
            jnp.stack([jnp.sum(scaled, axis=1), jnp.sum(scaled * centred, axis=1)]), "tp"
        ),
        axis=0,
    )
    vis_grad = (
        inv_std[:, None]
        * (scaled - (grad_total / VF)[:, None] - centred * (grad_inner / VF)[:, None])
    ).astype(jnp.bfloat16)
    return (context.reshape(tok_rows, query_cols), vis_grad)


def solution(mesh):
    return jax.shard_map(
        on_device,
        mesh=mesh,
        in_specs=(
            P("seq", "tp"),
            P("tp"),
            P("tp", "seq"),
            P("seq", None),
            P(),
            P("seq", "tp"),
            P("seq", "tp"),
            P("seq", "tp"),
            P("seq"),
            P("seq"),
            P(),
            P(),
            P("seq", "tp"),
        ),
        out_specs=(P("seq", "tp"), P("seq", "tp")),
        check_vma=False,
    )
```

```python
import math

import jax
import jax.numpy as jnp
from jax import lax
from jax.sharding import PartitionSpec as P

VF = 12800
HEAD = 128
CAPD = 32
GROUP = 4


ln_eps = 1e-05
rms_eps = 1e-06
rope_base = 1000000.0
masked_score = -1e30


def shifted(x, axis, by):
    peers = lax.axis_size(axis)
    pairs = [(i, i + by) for i in range(peers) if 0 <= i + by < peers]
    return lax.ppermute(x, axis, pairs)


def bit_of(axis, b):
    return (lax.axis_index(axis) // (1 << b)) % 2


def bit_pairs(axis, b):
    peers = lax.axis_size(axis)
    return [(i, i ^ (1 << b)) for i in range(peers)]


def group_index(axis, bits):
    return sum(bit_of(axis, b) * (1 << k) for k, b in enumerate(bits))


def group_pairs(axis, bits, o):
    peers = lax.axis_size(axis)
    mask = sum(((o >> k) & 1) << b for k, b in enumerate(bits))
    return [(i, i ^ mask) for i in range(peers)]


def group_scatter(x, axis, bits, dim=0):
    me = group_index(axis, bits)
    acc = lax.dynamic_index_in_dim(x, me, dim, keepdims=False).astype(jnp.float32)
    for o in range(1, 1 << len(bits)):
        send = lax.dynamic_index_in_dim(x, jnp.bitwise_xor(me, o), dim, keepdims=False)
        got = lax.ppermute(send.astype(jnp.bfloat16), axis, group_pairs(axis, bits, o))
        acc = acc + got.astype(jnp.float32)
    return acc


def group_gather(x, axis, bits):
    me = group_index(axis, bits)
    g = 1 << len(bits)
    parts = [x] + [lax.ppermute(x, axis, group_pairs(axis, bits, o)) for o in range(1, g)]
    order = jnp.bitwise_xor(jnp.arange(g, dtype=jnp.int32), me)
    return jnp.take(jnp.stack(parts), order, axis=0)


def staged_scatter(x, axis, groups):
    acc = x
    for bits in groups:
        g = 1 << len(bits)
        lead = acc.reshape((acc.shape[0] // g, g) + acc.shape[1:])
        acc = group_scatter(lead, axis, bits, dim=1)
    return acc[0]


def staged_gather(x, axis, groups):
    acc = x
    for bits in groups:
        acc = group_gather(acc, axis, bits)
    count = len(groups)
    return acc.transpose(list(range(count - 1, -1, -1)) + list(range(count, acc.ndim)))


def exchange_sum(x, axis):
    got = lax.all_to_all(x.astype(jnp.bfloat16), axis, 0, 0, tiled=True)
    return jnp.sum(got.astype(jnp.float32), axis=0)


def exchange_gather(x, axis):
    peers = lax.axis_size(axis)
    return lax.all_to_all(jnp.broadcast_to(x[None], (peers,) + x.shape), axis, 0, 0, tiled=True)


def exchange_position(axis, groups, source):
    me = lax.axis_index(axis)
    place = jnp.zeros_like(source)
    step = 1
    for bits in groups:
        group_of = lambda d: sum(((d // (1 << b)) % 2) * (1 << k) for k, b in enumerate(bits))
        place = place + jnp.bitwise_xor(group_of(source), group_of(me)) * step
        step = step * (1 << len(bits))
    return place


def staged_gather_unordered(x, axis, groups):
    acc = x
    for bits in groups:
        g = 1 << len(bits)
        acc = jnp.stack([acc] + [lax.ppermute(acc, axis, group_pairs(axis, bits, o)) for o in range(1, g)])
    return acc


def log2(n):
    return n.bit_length() - 1


def rope_tables(positions, head_width):
    half = head_width // 2
    frequency = rope_base ** (-(jnp.arange(half).astype(jnp.float32) * 2.0 / head_width))
    angle = positions.astype(jnp.float32)[:, None] * frequency[None, :]
    return (jnp.cos(angle), jnp.sin(angle))


def rotate(values, cosine, sine):
    half = values.shape[-1] // 2
    first = values[..., :half]
    second = values[..., half:]
    cos_rows = cosine[:, None, :]
    sin_rows = sine[:, None, :]
    return jnp.concatenate(
        [first * cos_rows - second * sin_rows, second * cos_rows + first * sin_rows], axis=-1
    )


def unrotate(grads, cosine, sine):
    half = grads.shape[-1] // 2
    first = grads[..., :half]
    second = grads[..., half:]
    cos_rows = cosine[:, None, :]
    sin_rows = sine[:, None, :]
    return jnp.concatenate(
        [first * cos_rows + second * sin_rows, second * cos_rows - first * sin_rows], axis=-1
    )


def norm_backward(rows, grads, gain, axes):
    inv_rms = lax.rsqrt(jnp.mean(rows * rows, axis=axes, keepdims=True) + rms_eps)
    scaled = grads * gain
    inner = jnp.mean(rows * scaled, axis=axes, keepdims=True)
    return inv_rms * scaled - rows * (inv_rms * inv_rms * inv_rms) * inner


def attention_block(queries, keys, values, grads, allowed):
    scale = 1.0 / math.sqrt(queries.shape[-1])
    scores = jnp.einsum("qhgd,khd->hgqk", queries, keys, preferred_element_type=jnp.float32) * scale
    masked = jnp.where(allowed[None, None], scores, masked_score)
    peak = jnp.max(masked, axis=-1, keepdims=True)
    raised = jnp.where(allowed[None, None], jnp.exp(masked - peak), 0.0)
    shares = raised / jnp.sum(raised, axis=-1, keepdims=True)
    shares_low = shares.astype(jnp.bfloat16)
    context = jnp.einsum(
        "hgqk,khd->qhgd", shares_low, values, preferred_element_type=jnp.float32
    ).astype(jnp.bfloat16)
    share_grads = jnp.einsum("qhgd,khd->hgqk", grads, values, preferred_element_type=jnp.float32)
    delta = jnp.sum(shares * share_grads, axis=-1, keepdims=True)
    score_grads = (shares * (share_grads - delta) * scale).astype(jnp.bfloat16)
    query_grads = jnp.einsum(
        "hgqk,khd->qhgd", score_grads, keys, preferred_element_type=jnp.float32
    )
    key_grads = jnp.einsum(
        "hgqk,qhgd->khd", score_grads, queries, preferred_element_type=jnp.float32
    )
    value_grads = jnp.einsum(
        "hgqk,qhgd->khd", shares_low, grads, preferred_element_type=jnp.float32
    )
    return (context, query_grads, key_grads, value_grads)


def on_device(
    vis_feat,
    ln_gain,
    proj_weight,
    text_embed,
    rms_gain,
    wq,
    wk,
    wv,
    doc_ids,
    vis_slot,
    slot_token,
    token_slot,
    cotangent,
):
    seq_count = lax.axis_size("seq")
    my_index = lax.axis_index("seq")
    tok_rows = text_embed.shape[0]
    slot_cols = proj_weight.shape[1]
    features = vis_feat.astype(jnp.float32)
    tp_count = lax.axis_size("tp")
    tp_bits = log2(tp_count)
    seq_bits = log2(seq_count)
    tp_all = [list(range(tp_bits))]
    seq_up = [[0], [1, 2], [3, 4]] if seq_bits == 5 else [[b] for b in range(seq_bits)]
    seq_down = seq_up[::-1]
    row_total, row_squares = jnp.sum(
        exchange_gather(
            jnp.stack([jnp.sum(features, axis=1), jnp.sum(features * features, axis=1)]), "tp"
        ),
        axis=0,
    )
    row_mean = row_total / VF
    row_var = row_squares / VF - row_mean * row_mean
    inv_std = lax.rsqrt(row_var + ln_eps)
    centred = (features - row_mean[:, None]) * inv_std[:, None]
    vis_normed = (centred * ln_gain[None, :]).astype(jnp.bfloat16)
    vis_rows = vis_feat.shape[0]
    all_normed = staged_gather_unordered(vis_normed, "seq", seq_down)
    partial_embed = jnp.dot(
        all_normed.reshape(seq_count * vis_rows, vis_feat.shape[1]),
        proj_weight,
        preferred_element_type=jnp.float32,
    )
    slot_live = (slot_token >= 0)[:, None]
    slot_index = jnp.maximum(slot_token, 0)
    devices = seq_count * tp_count
    per = CAPD // tp_count
    token_place = (
        exchange_position("seq", seq_down, slot_index // vis_rows) * vis_rows + slot_index % vis_rows
    )
    route = (
        (token_place[:, None] == jnp.arange(seq_count * vis_rows, dtype=jnp.int32)[None, :])
        & slot_live
    ).astype(jnp.bfloat16)
    outgoing = jnp.dot(
        route, partial_embed.astype(jnp.bfloat16), preferred_element_type=jnp.float32
    ).reshape(devices, per, slot_cols)
    got = lax.all_to_all(outgoing.astype(jnp.bfloat16), ("seq", "tp"), 0, 0, tiled=True)
    mine = jnp.sum(
        got.reshape(seq_count, tp_count, per, slot_cols).astype(jnp.float32), axis=1
    ).astype(jnp.bfloat16)
    all_mine = exchange_gather(mine.transpose(1, 0, 2), "tp")
    arrived = all_mine.reshape(CAPD, seq_count * slot_cols)
    lanes = jnp.arange(CAPD, dtype=jnp.int32)
    one_hot = (vis_slot[:, None] == lanes[None, :]).astype(jnp.bfloat16)
    placed = jnp.dot(one_hot, arrived, preferred_element_type=jnp.float32).astype(jnp.bfloat16)
    is_image = vis_slot >= 0
    hidden = jnp.where(is_image[:, None], placed, text_embed)
    hidden_wide = hidden.astype(jnp.float32)
    inv_rms = lax.rsqrt(jnp.mean(hidden_wide * hidden_wide, axis=1, keepdims=True) + rms_eps)
    normed = (hidden_wide * inv_rms * rms_gain[None, :]).astype(jnp.bfloat16)
    stacked = jnp.concatenate([wq, wk, wv], axis=1)
    query_cols = wq.shape[1]
    key_cols = wk.shape[1]
    gathered = lax.all_gather(stacked, "seq", axis=0, tiled=True)
    projected = jnp.dot(normed, gathered, preferred_element_type=jnp.float32)
    local_heads = query_cols // HEAD
    local_groups = key_cols // HEAD
    positions = my_index * tok_rows + jnp.arange(tok_rows, dtype=jnp.int32)
    cosine, sine = rope_tables(positions, HEAD)
    queries = rotate(
        projected[:, :query_cols].reshape(tok_rows, local_heads, HEAD), cosine, sine
    ).astype(jnp.bfloat16)
    keys = rotate(
        projected[:, query_cols : query_cols + key_cols].reshape(tok_rows, local_groups, HEAD),
        cosine,
        sine,
    ).astype(jnp.bfloat16)
    values = (
        projected[:, query_cols + key_cols :]
        .astype(jnp.bfloat16)
        .reshape(tok_rows, local_groups, HEAD)
    )
    doc_marks = (doc_ids + 1).astype(jnp.bfloat16)
    prev_keys, prev_values, prev_docs = shifted((keys, values, doc_marks), "seq", 1)
    all_keys = jnp.concatenate([prev_keys, keys], axis=0)
    all_values = jnp.concatenate([prev_values, values], axis=0)
    query_docs = doc_marks.astype(jnp.float32)
    key_docs = jnp.concatenate([prev_docs.astype(jnp.float32), query_docs], axis=0)
    key_positions = jnp.concatenate([positions - tok_rows, positions], axis=0)
    allowed = (key_docs[None, :] == query_docs[:, None]) & (
        key_positions[None, :] <= positions[:, None]
    )
    grads = cotangent.reshape(tok_rows, local_groups, GROUP, HEAD)
    context, query_grads, key_grads, value_grads = attention_block(
        queries.reshape(tok_rows, local_groups, GROUP, HEAD), all_keys, all_values, grads, allowed
    )
    back_keys, back_values = (
        shifted(key_grads[:tok_rows].astype(jnp.bfloat16), "seq", -1).astype(jnp.float32),
        shifted(value_grads[:tok_rows].astype(jnp.bfloat16), "seq", -1).astype(jnp.float32),
    )
    key_total = key_grads[tok_rows:] + back_keys
    value_total = value_grads[tok_rows:] + back_values
    query_pre = (
        unrotate(query_grads.reshape(tok_rows, local_heads, HEAD), cosine, sine)
        .astype(jnp.bfloat16)
        .reshape(tok_rows, query_cols)
    )
    key_pre = unrotate(key_total, cosine, sine).astype(jnp.bfloat16).reshape(tok_rows, key_cols)
    value_pre = value_total.astype(jnp.bfloat16).reshape(tok_rows, key_cols)
    proj_grads = jnp.concatenate([query_pre, key_pre, value_pre], axis=1)
    selected = lax.dot_general(
        one_hot, proj_grads, (((0,), (0,)), ((), ())), preferred_element_type=jnp.float32
    ).astype(jnp.bfloat16)
    norm_part = jnp.einsum(
        "tkc,jrc->jtkr",
        selected.reshape(tp_count, per, selected.shape[1]),
        gathered.reshape(seq_count, slot_cols, gathered.shape[1]),
        preferred_element_type=jnp.float32,
    )
    embed_part = norm_backward(
        all_mine.transpose(2, 0, 1, 3).astype(jnp.float32),
        norm_part,
        rms_gain.reshape(seq_count, 1, 1, slot_cols),
        (0, 3),
    )
    got_back = lax.all_to_all(
        embed_part.astype(jnp.bfloat16).reshape(devices, per, slot_cols),
        ("seq", "tp"), 0, 0, tiled=True,
    )
    mine_back = jnp.sum(
        got_back.reshape(seq_count, tp_count, per, slot_cols).astype(jnp.float32), axis=1
    ).astype(jnp.bfloat16)
    all_back = exchange_gather(mine_back, "tp").reshape(tp_count * seq_count * per, slot_cols)
    block_of = token_slot // CAPD
    lane_of = token_slot % CAPD
    back_index = (lane_of // per) * (seq_count * per) + block_of * per + lane_of % per
    pick = (
        back_index[:, None] == jnp.arange(all_back.shape[0], dtype=jnp.int32)[None, :]
    ).astype(jnp.bfloat16)
    token_grads = jnp.dot(pick, all_back, preferred_element_type=jnp.float32).astype(jnp.bfloat16)
    own_rows = vis_feat.shape[0]
    feature_part = jnp.einsum(
        "bqd,fd->bqf",
        token_grads.reshape(seq_count, own_rows, slot_cols),
        proj_weight,
        preferred_element_type=jnp.float32,
    )
    feature_grads = exchange_sum(feature_part, "seq")
    scaled = feature_grads * ln_gain[None, :]
    grad_total, grad_inner = jnp.sum(
        exchange_gather(
            jnp.stack([jnp.sum(scaled, axis=1), jnp.sum(scaled * centred, axis=1)]), "tp"
        ),
        axis=0,
    )
    vis_grad = (
        inv_std[:, None]
        * (scaled - (grad_total / VF)[:, None] - centred * (grad_inner / VF)[:, None])
    ).astype(jnp.bfloat16)
    return (context.reshape(tok_rows, query_cols), vis_grad)


def solution(mesh):
    return jax.shard_map(
        on_device,
        mesh=mesh,
        in_specs=(
            P("seq", "tp"),
            P("tp"),
            P("tp", "seq"),
            P("seq", None),
            P(),
            P("seq", "tp"),
            P("seq", "tp"),
            P("seq", "tp"),
            P("seq"),
            P("seq"),
            P(),
            P(),
            P("seq", "tp"),
        ),
        out_specs=(P("seq", "tp"), P("seq", "tp")),
        check_vma=False,
    )
```

```python
import math

import jax
import jax.numpy as jnp
from jax import lax
from jax.sharding import PartitionSpec as P

VF = 12800
HEAD = 128
CAPD = 32
GROUP = 4


ln_eps = 1e-05
rms_eps = 1e-06
rope_base = 1000000.0
masked_score = -1e30


def shifted(x, axis, by):
    peers = lax.axis_size(axis)
    pairs = [(i, i + by) for i in range(peers) if 0 <= i + by < peers]
    return lax.ppermute(x, axis, pairs)


def bit_of(axis, b):
    return (lax.axis_index(axis) // (1 << b)) % 2


def bit_pairs(axis, b):
    peers = lax.axis_size(axis)
    return [(i, i ^ (1 << b)) for i in range(peers)]


def group_index(axis, bits):
    return sum(bit_of(axis, b) * (1 << k) for k, b in enumerate(bits))


def group_pairs(axis, bits, o):
    peers = lax.axis_size(axis)
    mask = sum(((o >> k) & 1) << b for k, b in enumerate(bits))
    return [(i, i ^ mask) for i in range(peers)]


def group_scatter(x, axis, bits, dim=0):
    me = group_index(axis, bits)
    acc = lax.dynamic_index_in_dim(x, me, dim, keepdims=False).astype(jnp.float32)
    for o in range(1, 1 << len(bits)):
        send = lax.dynamic_index_in_dim(x, jnp.bitwise_xor(me, o), dim, keepdims=False)
        got = lax.ppermute(send.astype(jnp.bfloat16), axis, group_pairs(axis, bits, o))
        acc = acc + got.astype(jnp.float32)
    return acc


def group_gather(x, axis, bits):
    me = group_index(axis, bits)
    g = 1 << len(bits)
    parts = [x] + [lax.ppermute(x, axis, group_pairs(axis, bits, o)) for o in range(1, g)]
    order = jnp.bitwise_xor(jnp.arange(g, dtype=jnp.int32), me)
    return jnp.take(jnp.stack(parts), order, axis=0)


def staged_scatter(x, axis, groups):
    acc = x
    for bits in groups:
        g = 1 << len(bits)
        lead = acc.reshape((acc.shape[0] // g, g) + acc.shape[1:])
        acc = group_scatter(lead, axis, bits, dim=1)
    return acc[0]


def staged_gather(x, axis, groups):
    acc = x
    for bits in groups:
        acc = group_gather(acc, axis, bits)
    count = len(groups)
    return acc.transpose(list(range(count - 1, -1, -1)) + list(range(count, acc.ndim)))


def exchange_sum(x, axis):
    got = lax.all_to_all(x.astype(jnp.bfloat16), axis, 0, 0, tiled=True)
    return jnp.sum(got.astype(jnp.float32), axis=0)


def exchange_gather(x, axis):
    peers = lax.axis_size(axis)
    return lax.all_to_all(jnp.broadcast_to(x[None], (peers,) + x.shape), axis, 0, 0, tiled=True)


def exchange_position(axis, groups, source):
    me = lax.axis_index(axis)
    place = jnp.zeros_like(source)
    step = 1
    for bits in groups:
        group_of = lambda d: sum(((d // (1 << b)) % 2) * (1 << k) for k, b in enumerate(bits))
        place = place + jnp.bitwise_xor(group_of(source), group_of(me)) * step
        step = step * (1 << len(bits))
    return place


def staged_gather_unordered(x, axis, groups):
    acc = x
    for bits in groups:
        g = 1 << len(bits)
        acc = jnp.stack([acc] + [lax.ppermute(acc, axis, group_pairs(axis, bits, o)) for o in range(1, g)])
    return acc


def log2(n):
    return n.bit_length() - 1


def rope_tables(positions, head_width):
    half = head_width // 2
    frequency = rope_base ** (-(jnp.arange(half).astype(jnp.float32) * 2.0 / head_width))
    angle = positions.astype(jnp.float32)[:, None] * frequency[None, :]
    return (jnp.cos(angle), jnp.sin(angle))


def rotate(values, cosine, sine):
    half = values.shape[-1] // 2
    first = values[..., :half]
    second = values[..., half:]
    cos_rows = cosine[:, None, :]
    sin_rows = sine[:, None, :]
    return jnp.concatenate(
        [first * cos_rows - second * sin_rows, second * cos_rows + first * sin_rows], axis=-1
    )


def unrotate(grads, cosine, sine):
    half = grads.shape[-1] // 2
    first = grads[..., :half]
    second = grads[..., half:]
    cos_rows = cosine[:, None, :]
    sin_rows = sine[:, None, :]
    return jnp.concatenate(
        [first * cos_rows + second * sin_rows, second * cos_rows - first * sin_rows], axis=-1
    )


def norm_backward(rows, grads, gain, axes):
    inv_rms = lax.rsqrt(jnp.mean(rows * rows, axis=axes, keepdims=True) + rms_eps)
    scaled = grads * gain
    inner = jnp.mean(rows * scaled, axis=axes, keepdims=True)
    return inv_rms * scaled - rows * (inv_rms * inv_rms * inv_rms) * inner


def attention_block(queries, keys, values, grads, allowed):
    scale = 1.0 / math.sqrt(queries.shape[-1])
    scores = jnp.einsum("qhgd,khd->hgqk", queries, keys, preferred_element_type=jnp.float32) * scale
    masked = jnp.where(allowed[None, None], scores, masked_score)
    peak = jnp.max(masked, axis=-1, keepdims=True)
    raised = jnp.where(allowed[None, None], jnp.exp(masked - peak), 0.0)
    shares = raised / jnp.sum(raised, axis=-1, keepdims=True)
    shares_low = shares.astype(jnp.bfloat16)
    context = jnp.einsum(
        "hgqk,khd->qhgd", shares_low, values, preferred_element_type=jnp.float32
    ).astype(jnp.bfloat16)
    share_grads = jnp.einsum("qhgd,khd->hgqk", grads, values, preferred_element_type=jnp.float32)
    delta = jnp.sum(shares * share_grads, axis=-1, keepdims=True)
    score_grads = (shares * (share_grads - delta) * scale).astype(jnp.bfloat16)
    query_grads = jnp.einsum(
        "hgqk,khd->qhgd", score_grads, keys, preferred_element_type=jnp.float32
    )
    key_grads = jnp.einsum(
        "hgqk,qhgd->khd", score_grads, queries, preferred_element_type=jnp.float32
    )
    value_grads = jnp.einsum(
        "hgqk,qhgd->khd", shares_low, grads, preferred_element_type=jnp.float32
    )
    return (context, query_grads, key_grads, value_grads)


def on_device(
    vis_feat,
    ln_gain,
    proj_weight,
    text_embed,
    rms_gain,
    wq,
    wk,
    wv,
    doc_ids,
    vis_slot,
    slot_token,
    token_slot,
    cotangent,
):
    seq_count = lax.axis_size("seq")
    my_index = lax.axis_index("seq")
    tok_rows = text_embed.shape[0]
    slot_cols = proj_weight.shape[1]
    features = vis_feat.astype(jnp.float32)
    tp_count = lax.axis_size("tp")
    tp_bits = log2(tp_count)
    seq_bits = log2(seq_count)
    tp_all = [list(range(tp_bits))]
    seq_up = [[0], [1, 2], [3, 4]] if seq_bits == 5 else [[b] for b in range(seq_bits)]
    seq_down = seq_up[::-1]
    row_total, row_squares = jnp.sum(
        exchange_gather(
            jnp.stack([jnp.sum(features, axis=1), jnp.sum(features * features, axis=1)]), "tp"
        ),
        axis=0,
    )
    row_mean = row_total / VF
    row_var = row_squares / VF - row_mean * row_mean
    inv_std = lax.rsqrt(row_var + ln_eps)
    centred = (features - row_mean[:, None]) * inv_std[:, None]
    vis_normed = (centred * ln_gain[None, :]).astype(jnp.bfloat16)
    vis_rows = vis_feat.shape[0]
    all_normed = staged_gather_unordered(vis_normed, "seq", seq_down)
    partial_embed = jnp.dot(
        all_normed.reshape(seq_count * vis_rows, vis_feat.shape[1]),
        proj_weight,
        preferred_element_type=jnp.float32,
    )
    slot_live = (slot_token >= 0)[:, None]
    slot_index = jnp.maximum(slot_token, 0)
    devices = seq_count * tp_count
    per = CAPD // tp_count
    token_place = (
        exchange_position("seq", seq_down, slot_index // vis_rows) * vis_rows + slot_index % vis_rows
    )
    route = (
        (token_place[:, None] == jnp.arange(seq_count * vis_rows, dtype=jnp.int32)[None, :])
        & slot_live
    ).astype(jnp.bfloat16)
    outgoing = jnp.dot(
        route, partial_embed.astype(jnp.bfloat16), preferred_element_type=jnp.float32
    ).reshape(devices, per, slot_cols)
    got = lax.all_to_all(outgoing.astype(jnp.bfloat16), ("seq", "tp"), 0, 0, tiled=True)
    mine = jnp.sum(
        got.reshape(seq_count, tp_count, per, slot_cols).astype(jnp.float32), axis=1
    ).astype(jnp.bfloat16)
    all_mine = exchange_gather(mine.transpose(1, 0, 2), "tp")
    arrived = all_mine.reshape(CAPD, seq_count * slot_cols)
    lanes = jnp.arange(CAPD, dtype=jnp.int32)
    one_hot = (vis_slot[:, None] == lanes[None, :]).astype(jnp.bfloat16)
    placed = jnp.dot(one_hot, arrived, preferred_element_type=jnp.float32).astype(jnp.bfloat16)
    is_image = vis_slot >= 0
    hidden = jnp.where(is_image[:, None], placed, text_embed)
    hidden_wide = hidden.astype(jnp.float32)
    inv_rms = lax.rsqrt(jnp.mean(hidden_wide * hidden_wide, axis=1, keepdims=True) + rms_eps)
    normed = (hidden_wide * inv_rms * rms_gain[None, :]).astype(jnp.bfloat16)
    stacked = jnp.concatenate([wq, wk, wv], axis=1)
    query_cols = wq.shape[1]
    key_cols = wk.shape[1]
    gathered = lax.all_gather(stacked, "seq", axis=0, tiled=True)
    projected = jnp.dot(normed, gathered, preferred_element_type=jnp.float32)
    local_heads = query_cols // HEAD
    local_groups = key_cols // HEAD
    positions = my_index * tok_rows + jnp.arange(tok_rows, dtype=jnp.int32)
    cosine, sine = rope_tables(positions, HEAD)
    queries = rotate(
        projected[:, :query_cols].reshape(tok_rows, local_heads, HEAD), cosine, sine
    ).astype(jnp.bfloat16)
    keys = rotate(
        projected[:, query_cols : query_cols + key_cols].reshape(tok_rows, local_groups, HEAD),
        cosine,
        sine,
    ).astype(jnp.bfloat16)
    values = (
        projected[:, query_cols + key_cols :]
        .astype(jnp.bfloat16)
        .reshape(tok_rows, local_groups, HEAD)
    )
    doc_marks = (doc_ids + 1).astype(jnp.bfloat16)
    prev_pair, prev_docs = shifted((jnp.concatenate([keys, values], axis=1), doc_marks), "seq", 1)
    prev_keys, prev_values = prev_pair[:, :local_groups], prev_pair[:, local_groups:]
    all_keys = jnp.concatenate([prev_keys, keys], axis=0)
    all_values = jnp.concatenate([prev_values, values], axis=0)
    query_docs = doc_marks.astype(jnp.float32)
    key_docs = jnp.concatenate([prev_docs.astype(jnp.float32), query_docs], axis=0)
    key_positions = jnp.concatenate([positions - tok_rows, positions], axis=0)
    allowed = (key_docs[None, :] == query_docs[:, None]) & (
        key_positions[None, :] <= positions[:, None]
    )
    grads = cotangent.reshape(tok_rows, local_groups, GROUP, HEAD)
    context, query_grads, key_grads, value_grads = attention_block(
        queries.reshape(tok_rows, local_groups, GROUP, HEAD), all_keys, all_values, grads, allowed
    )
    back_pair = shifted(
        jnp.concatenate([key_grads[:tok_rows], value_grads[:tok_rows]], axis=1).astype(jnp.bfloat16),
        "seq", -1,
    ).astype(jnp.float32)
    back_keys, back_values = back_pair[:, :local_groups], back_pair[:, local_groups:]
    key_total = key_grads[tok_rows:] + back_keys
    value_total = value_grads[tok_rows:] + back_values
    query_pre = (
        unrotate(query_grads.reshape(tok_rows, local_heads, HEAD), cosine, sine)
        .astype(jnp.bfloat16)
        .reshape(tok_rows, query_cols)
    )
    key_pre = unrotate(key_total, cosine, sine).astype(jnp.bfloat16).reshape(tok_rows, key_cols)
    value_pre = value_total.astype(jnp.bfloat16).reshape(tok_rows, key_cols)
    proj_grads = jnp.concatenate([query_pre, key_pre, value_pre], axis=1)
    selected = lax.dot_general(
        one_hot, proj_grads, (((0,), (0,)), ((), ())), preferred_element_type=jnp.float32
    ).astype(jnp.bfloat16)
    norm_part = jnp.einsum(
        "tkc,jrc->jtkr",
        selected.reshape(tp_count, per, selected.shape[1]),
        gathered.reshape(seq_count, slot_cols, gathered.shape[1]),
        preferred_element_type=jnp.float32,
    )
    embed_part = norm_backward(
        all_mine.transpose(2, 0, 1, 3).astype(jnp.float32),
        norm_part,
        rms_gain.reshape(seq_count, 1, 1, slot_cols),
        (0, 3),
    )
    got_back = lax.all_to_all(
        embed_part.astype(jnp.bfloat16).reshape(devices, per, slot_cols),
        ("seq", "tp"), 0, 0, tiled=True,
    )
    mine_back = jnp.sum(
        got_back.reshape(seq_count, tp_count, per, slot_cols).astype(jnp.float32), axis=1
    ).astype(jnp.bfloat16)
    all_back = exchange_gather(mine_back, "tp").reshape(tp_count * seq_count * per, slot_cols)
    block_of = token_slot // CAPD
    lane_of = token_slot % CAPD
    back_index = (lane_of // per) * (seq_count * per) + block_of * per + lane_of % per
    pick = (
        back_index[:, None] == jnp.arange(all_back.shape[0], dtype=jnp.int32)[None, :]
    ).astype(jnp.bfloat16)
    token_grads = jnp.dot(pick, all_back, preferred_element_type=jnp.float32).astype(jnp.bfloat16)
    own_rows = vis_feat.shape[0]
    feature_part = jnp.einsum(
        "bqd,fd->bqf",
        token_grads.reshape(seq_count, own_rows, slot_cols),
        proj_weight,
        preferred_element_type=jnp.float32,
    )
    feature_grads = exchange_sum(feature_part, "seq")
    scaled = feature_grads * ln_gain[None, :]
    grad_total, grad_inner = jnp.sum(
        exchange_gather(
            jnp.stack([jnp.sum(scaled, axis=1), jnp.sum(scaled * centred, axis=1)]), "tp"
        ),
        axis=0,
    )
    vis_grad = (
        inv_std[:, None]
        * (scaled - (grad_total / VF)[:, None] - centred * (grad_inner / VF)[:, None])
    ).astype(jnp.bfloat16)
    return (context.reshape(tok_rows, query_cols), vis_grad)


def solution(mesh):
    return jax.shard_map(
        on_device,
        mesh=mesh,
        in_specs=(
            P("seq", "tp"),
            P("tp"),
            P("tp", "seq"),
            P("seq", None),
            P(),
            P("seq", "tp"),
            P("seq", "tp"),
            P("seq", "tp"),
            P("seq"),
            P("seq"),
            P(),
            P(),
            P("seq", "tp"),
        ),
        out_specs=(P("seq", "tp"), P("seq", "tp")),
        check_vma=False,
    )
```

```python
import math

import jax
import jax.numpy as jnp
from jax import lax
from jax.sharding import PartitionSpec as P

VF = 12800
HEAD = 128
CAPD = 32
GROUP = 4


ln_eps = 1e-05
rms_eps = 1e-06
rope_base = 1000000.0
masked_score = -1e30


def shifted(x, axis, by):
    peers = lax.axis_size(axis)
    pairs = [(i, i + by) for i in range(peers) if 0 <= i + by < peers]
    return lax.ppermute(x, axis, pairs)


def bit_of(axis, b):
    return (lax.axis_index(axis) // (1 << b)) % 2


def bit_pairs(axis, b):
    peers = lax.axis_size(axis)
    return [(i, i ^ (1 << b)) for i in range(peers)]


def group_index(axis, bits):
    return sum(bit_of(axis, b) * (1 << k) for k, b in enumerate(bits))


def group_pairs(axis, bits, o):
    peers = lax.axis_size(axis)
    mask = sum(((o >> k) & 1) << b for k, b in enumerate(bits))
    return [(i, i ^ mask) for i in range(peers)]


def group_scatter(x, axis, bits, dim=0):
    me = group_index(axis, bits)
    acc = lax.dynamic_index_in_dim(x, me, dim, keepdims=False).astype(jnp.float32)
    for o in range(1, 1 << len(bits)):
        send = lax.dynamic_index_in_dim(x, jnp.bitwise_xor(me, o), dim, keepdims=False)
        got = lax.ppermute(send.astype(jnp.bfloat16), axis, group_pairs(axis, bits, o))
        acc = acc + got.astype(jnp.float32)
    return acc


def group_gather(x, axis, bits):
    me = group_index(axis, bits)
    g = 1 << len(bits)
    parts = [x] + [lax.ppermute(x, axis, group_pairs(axis, bits, o)) for o in range(1, g)]
    order = jnp.bitwise_xor(jnp.arange(g, dtype=jnp.int32), me)
    return jnp.take(jnp.stack(parts), order, axis=0)


def staged_scatter(x, axis, groups):
    acc = x
    for bits in groups:
        g = 1 << len(bits)
        lead = acc.reshape((acc.shape[0] // g, g) + acc.shape[1:])
        acc = group_scatter(lead, axis, bits, dim=1)
    return acc[0]


def staged_gather(x, axis, groups):
    acc = x
    for bits in groups:
        acc = group_gather(acc, axis, bits)
    count = len(groups)
    return acc.transpose(list(range(count - 1, -1, -1)) + list(range(count, acc.ndim)))


def exchange_sum(x, axis):
    got = lax.all_to_all(x.astype(jnp.bfloat16), axis, 0, 0, tiled=True)
    return jnp.sum(got.astype(jnp.float32), axis=0)


def exchange_gather(x, axis):
    peers = lax.axis_size(axis)
    return lax.all_to_all(jnp.broadcast_to(x[None], (peers,) + x.shape), axis, 0, 0, tiled=True)


def exchange_position(axis, groups, source):
    me = lax.axis_index(axis)
    place = jnp.zeros_like(source)
    step = 1
    for bits in groups:
        group_of = lambda d: sum(((d // (1 << b)) % 2) * (1 << k) for k, b in enumerate(bits))
        place = place + jnp.bitwise_xor(group_of(source), group_of(me)) * step
        step = step * (1 << len(bits))
    return place


def staged_gather_unordered(x, axis, groups):
    acc = x
    for bits in groups:
        g = 1 << len(bits)
        acc = jnp.stack([acc] + [lax.ppermute(acc, axis, group_pairs(axis, bits, o)) for o in range(1, g)])
    return acc


def log2(n):
    return n.bit_length() - 1


def rope_tables(positions, head_width):
    half = head_width // 2
    frequency = rope_base ** (-(jnp.arange(half).astype(jnp.float32) * 2.0 / head_width))
    angle = positions.astype(jnp.float32)[:, None] * frequency[None, :]
    return (jnp.cos(angle), jnp.sin(angle))


def rotate(values, cosine, sine):
    half = values.shape[-1] // 2
    first = values[..., :half]
    second = values[..., half:]
    cos_rows = cosine[:, None, :]
    sin_rows = sine[:, None, :]
    return jnp.concatenate(
        [first * cos_rows - second * sin_rows, second * cos_rows + first * sin_rows], axis=-1
    )


def unrotate(grads, cosine, sine):
    half = grads.shape[-1] // 2
    first = grads[..., :half]
    second = grads[..., half:]
    cos_rows = cosine[:, None, :]
    sin_rows = sine[:, None, :]
    return jnp.concatenate(
        [first * cos_rows + second * sin_rows, second * cos_rows - first * sin_rows], axis=-1
    )


def norm_backward(rows, grads, gain, axes):
    inv_rms = lax.rsqrt(jnp.mean(rows * rows, axis=axes, keepdims=True) + rms_eps)
    scaled = grads * gain
    inner = jnp.mean(rows * scaled, axis=axes, keepdims=True)
    return inv_rms * scaled - rows * (inv_rms * inv_rms * inv_rms) * inner


def attention_block(queries, keys, values, grads, allowed):
    scale = 1.0 / math.sqrt(queries.shape[-1])
    scores = jnp.einsum("qhgd,khd->hgqk", queries, keys, preferred_element_type=jnp.float32) * scale
    masked = jnp.where(allowed[None, None], scores, masked_score)
    peak = jnp.max(masked, axis=-1, keepdims=True)
    raised = jnp.where(allowed[None, None], jnp.exp(masked - peak), 0.0)
    shares = raised / jnp.sum(raised, axis=-1, keepdims=True)
    shares_low = shares.astype(jnp.bfloat16)
    context = jnp.einsum(
        "hgqk,khd->qhgd", shares_low, values, preferred_element_type=jnp.float32
    ).astype(jnp.bfloat16)
    share_grads = jnp.einsum("qhgd,khd->hgqk", grads, values, preferred_element_type=jnp.float32)
    delta = jnp.sum(shares * share_grads, axis=-1, keepdims=True)
    score_grads = (shares * (share_grads - delta) * scale).astype(jnp.bfloat16)
    query_grads = jnp.einsum(
        "hgqk,khd->qhgd", score_grads, keys, preferred_element_type=jnp.float32
    )
    key_grads = jnp.einsum(
        "hgqk,qhgd->khd", score_grads, queries, preferred_element_type=jnp.float32
    )
    value_grads = jnp.einsum(
        "hgqk,qhgd->khd", shares_low, grads, preferred_element_type=jnp.float32
    )
    return (context, query_grads, key_grads, value_grads)


def on_device(
    vis_feat,
    ln_gain,
    proj_weight,
    text_embed,
    rms_gain,
    wq,
    wk,
    wv,
    doc_ids,
    vis_slot,
    slot_token,
    token_slot,
    cotangent,
):
    seq_count = lax.axis_size("seq")
    my_index = lax.axis_index("seq")
    tok_rows = text_embed.shape[0]
    slot_cols = proj_weight.shape[1]
    features = vis_feat.astype(jnp.float32)
    tp_count = lax.axis_size("tp")
    tp_bits = log2(tp_count)
    seq_bits = log2(seq_count)
    tp_all = [list(range(tp_bits))]
    seq_up = [[0], [1, 2], [3, 4]] if seq_bits == 5 else [[b] for b in range(seq_bits)]
    seq_down = seq_up[::-1]
    row_total, row_squares = jnp.sum(
        exchange_gather(
            jnp.stack([jnp.sum(features, axis=1), jnp.sum(features * features, axis=1)]), "tp"
        ),
        axis=0,
    )
    row_mean = row_total / VF
    row_var = row_squares / VF - row_mean * row_mean
    inv_std = lax.rsqrt(row_var + ln_eps)
    centred = (features - row_mean[:, None]) * inv_std[:, None]
    vis_normed = (centred * ln_gain[None, :]).astype(jnp.bfloat16)
    vis_rows = vis_feat.shape[0]
    all_normed = staged_gather_unordered(vis_normed, "seq", seq_down)
    partial_embed = jnp.dot(
        all_normed.reshape(seq_count * vis_rows, vis_feat.shape[1]),
        proj_weight,
        preferred_element_type=jnp.float32,
    )
    slot_live = (slot_token >= 0)[:, None]
    slot_index = jnp.maximum(slot_token, 0)
    devices = seq_count * tp_count
    per = CAPD // tp_count
    token_place = (
        exchange_position("seq", seq_down, slot_index // vis_rows) * vis_rows + slot_index % vis_rows
    )
    route = (
        (token_place[:, None] == jnp.arange(seq_count * vis_rows, dtype=jnp.int32)[None, :])
        & slot_live
    ).astype(jnp.bfloat16)
    outgoing = jnp.dot(
        route, partial_embed.astype(jnp.bfloat16), preferred_element_type=jnp.float32
    ).reshape(devices, per, slot_cols)
    got = lax.all_to_all(outgoing.astype(jnp.bfloat16), ("seq", "tp"), 0, 0, tiled=True)
    mine = jnp.sum(
        got.reshape(seq_count, tp_count, per, slot_cols).astype(jnp.float32), axis=1
    ).astype(jnp.bfloat16)
    all_mine = exchange_gather(mine.transpose(1, 0, 2), "tp")
    arrived = all_mine.reshape(CAPD, seq_count * slot_cols)
    lanes = jnp.arange(CAPD, dtype=jnp.int32)
    one_hot = (vis_slot[:, None] == lanes[None, :]).astype(jnp.bfloat16)
    head_rows = tok_rows - CAPD
    tail_slot = vis_slot[head_rows:]
    placed = jnp.dot(
        one_hot[head_rows:], arrived, preferred_element_type=jnp.float32
    ).astype(jnp.bfloat16)
    hidden_tail = jnp.where((tail_slot >= 0)[:, None], placed, text_embed[head_rows:])

    def rms_normed(hidden):
        hidden_wide = hidden.astype(jnp.float32)
        inv_rms = lax.rsqrt(jnp.mean(hidden_wide * hidden_wide, axis=1, keepdims=True) + rms_eps)
        return (hidden_wide * inv_rms * rms_gain[None, :]).astype(jnp.bfloat16)

    normed = lax.dynamic_update_slice_in_dim(
        rms_normed(text_embed), rms_normed(hidden_tail), head_rows, 0
    )
    stacked = jnp.concatenate([wq, wk, wv], axis=1)
    query_cols = wq.shape[1]
    key_cols = wk.shape[1]
    gathered = lax.all_gather(stacked, "seq", axis=0, tiled=True)
    projected = jnp.dot(normed, gathered, preferred_element_type=jnp.float32)
    local_heads = query_cols // HEAD
    local_groups = key_cols // HEAD
    positions = my_index * tok_rows + jnp.arange(tok_rows, dtype=jnp.int32)
    cosine, sine = rope_tables(positions, HEAD)
    queries = rotate(
        projected[:, :query_cols].reshape(tok_rows, local_heads, HEAD), cosine, sine
    ).astype(jnp.bfloat16)
    keys = rotate(
        projected[:, query_cols : query_cols + key_cols].reshape(tok_rows, local_groups, HEAD),
        cosine,
        sine,
    ).astype(jnp.bfloat16)
    values = (
        projected[:, query_cols + key_cols :]
        .astype(jnp.bfloat16)
        .reshape(tok_rows, local_groups, HEAD)
    )
    doc_marks = (doc_ids + 1).astype(jnp.bfloat16)
    prev_keys, prev_values, prev_docs = shifted((keys, values, doc_marks), "seq", 1)
    all_keys = jnp.concatenate([prev_keys, keys], axis=0)
    all_values = jnp.concatenate([prev_values, values], axis=0)
    query_docs = doc_marks.astype(jnp.float32)
    key_docs = jnp.concatenate([prev_docs.astype(jnp.float32), query_docs], axis=0)
    key_positions = jnp.concatenate([positions - tok_rows, positions], axis=0)
    allowed = (key_docs[None, :] == query_docs[:, None]) & (
        key_positions[None, :] <= positions[:, None]
    )
    grads = cotangent.reshape(tok_rows, local_groups, GROUP, HEAD)
    context, query_grads, key_grads, value_grads = attention_block(
        queries.reshape(tok_rows, local_groups, GROUP, HEAD), all_keys, all_values, grads, allowed
    )
    back_keys, back_values = (
        shifted(key_grads[:tok_rows].astype(jnp.bfloat16), "seq", -1).astype(jnp.float32),
        shifted(value_grads[:tok_rows].astype(jnp.bfloat16), "seq", -1).astype(jnp.float32),
    )
    key_total = key_grads[tok_rows:] + back_keys
    value_total = value_grads[tok_rows:] + back_values
    query_pre = (
        unrotate(query_grads.reshape(tok_rows, local_heads, HEAD), cosine, sine)
        .astype(jnp.bfloat16)
        .reshape(tok_rows, query_cols)
    )
    key_pre = unrotate(key_total, cosine, sine).astype(jnp.bfloat16).reshape(tok_rows, key_cols)
    value_pre = value_total.astype(jnp.bfloat16).reshape(tok_rows, key_cols)
    proj_grads = jnp.concatenate([query_pre, key_pre, value_pre], axis=1)
    selected = lax.dot_general(
        one_hot, proj_grads, (((0,), (0,)), ((), ())), preferred_element_type=jnp.float32
    ).astype(jnp.bfloat16)
    norm_part = jnp.einsum(
        "tkc,jrc->jtkr",
        selected.reshape(tp_count, per, selected.shape[1]),
        gathered.reshape(seq_count, slot_cols, gathered.shape[1]),
        preferred_element_type=jnp.float32,
    )
    embed_part = norm_backward(
        all_mine.transpose(2, 0, 1, 3).astype(jnp.float32),
        norm_part,
        rms_gain.reshape(seq_count, 1, 1, slot_cols),
        (0, 3),
    )
    got_back = lax.all_to_all(
        embed_part.astype(jnp.bfloat16).reshape(devices, per, slot_cols),
        ("seq", "tp"), 0, 0, tiled=True,
    )
    mine_back = jnp.sum(
        got_back.reshape(seq_count, tp_count, per, slot_cols).astype(jnp.float32), axis=1
    ).astype(jnp.bfloat16)
    all_back = exchange_gather(mine_back, "tp").reshape(tp_count * seq_count * per, slot_cols)
    block_of = token_slot // CAPD
    lane_of = token_slot % CAPD
    back_index = (lane_of // per) * (seq_count * per) + block_of * per + lane_of % per
    pick = (
        back_index[:, None] == jnp.arange(all_back.shape[0], dtype=jnp.int32)[None, :]
    ).astype(jnp.bfloat16)
    token_grads = jnp.dot(pick, all_back, preferred_element_type=jnp.float32).astype(jnp.bfloat16)
    own_rows = vis_feat.shape[0]
    feature_part = jnp.einsum(
        "bqd,fd->bqf",
        token_grads.reshape(seq_count, own_rows, slot_cols),
        proj_weight,
        preferred_element_type=jnp.float32,
    )
    feature_grads = exchange_sum(feature_part, "seq")
    scaled = feature_grads * ln_gain[None, :]
    grad_total, grad_inner = jnp.sum(
        exchange_gather(
            jnp.stack([jnp.sum(scaled, axis=1), jnp.sum(scaled * centred, axis=1)]), "tp"
        ),
        axis=0,
    )
    vis_grad = (
        inv_std[:, None]
        * (scaled - (grad_total / VF)[:, None] - centred * (grad_inner / VF)[:, None])
    ).astype(jnp.bfloat16)
    return (context.reshape(tok_rows, query_cols), vis_grad)


def solution(mesh):
    return jax.shard_map(
        on_device,
        mesh=mesh,
        in_specs=(
            P("seq", "tp"),
            P("tp"),
            P("tp", "seq"),
            P("seq", None),
            P(),
            P("seq", "tp"),
            P("seq", "tp"),
            P("seq", "tp"),
            P("seq"),
            P("seq"),
            P(),
            P(),
            P("seq", "tp"),
        ),
        out_specs=(P("seq", "tp"), P("seq", "tp")),
        check_vma=False,
    )
```

```python
import math

import jax
import jax.numpy as jnp
from jax import lax
from jax.sharding import PartitionSpec as P

VF = 12800
HEAD = 128
CAPD = 32
GROUP = 4


ln_eps = 1e-05
rms_eps = 1e-06
rope_base = 1000000.0
masked_score = -1e30


def shifted(x, axis, by):
    peers = lax.axis_size(axis)
    pairs = [(i, i + by) for i in range(peers) if 0 <= i + by < peers]
    return lax.ppermute(x, axis, pairs)


def bit_of(axis, b):
    return (lax.axis_index(axis) // (1 << b)) % 2


def bit_pairs(axis, b):
    peers = lax.axis_size(axis)
    return [(i, i ^ (1 << b)) for i in range(peers)]


def group_index(axis, bits):
    return sum(bit_of(axis, b) * (1 << k) for k, b in enumerate(bits))


def group_pairs(axis, bits, o):
    peers = lax.axis_size(axis)
    mask = sum(((o >> k) & 1) << b for k, b in enumerate(bits))
    return [(i, i ^ mask) for i in range(peers)]


def group_scatter(x, axis, bits, dim=0):
    me = group_index(axis, bits)
    acc = lax.dynamic_index_in_dim(x, me, dim, keepdims=False).astype(jnp.float32)
    for o in range(1, 1 << len(bits)):
        send = lax.dynamic_index_in_dim(x, jnp.bitwise_xor(me, o), dim, keepdims=False)
        got = lax.ppermute(send.astype(jnp.bfloat16), axis, group_pairs(axis, bits, o))
        acc = acc + got.astype(jnp.float32)
    return acc


def group_gather(x, axis, bits):
    me = group_index(axis, bits)
    g = 1 << len(bits)
    parts = [x] + [lax.ppermute(x, axis, group_pairs(axis, bits, o)) for o in range(1, g)]
    order = jnp.bitwise_xor(jnp.arange(g, dtype=jnp.int32), me)
    return jnp.take(jnp.stack(parts), order, axis=0)


def staged_scatter(x, axis, groups):
    acc = x
    for bits in groups:
        g = 1 << len(bits)
        lead = acc.reshape((acc.shape[0] // g, g) + acc.shape[1:])
        acc = group_scatter(lead, axis, bits, dim=1)
    return acc[0]


def staged_gather(x, axis, groups):
    acc = x
    for bits in groups:
        acc = group_gather(acc, axis, bits)
    count = len(groups)
    return acc.transpose(list(range(count - 1, -1, -1)) + list(range(count, acc.ndim)))


def exchange_sum(x, axis):
    got = lax.all_to_all(x.astype(jnp.bfloat16), axis, 0, 0, tiled=True)
    return jnp.sum(got.astype(jnp.float32), axis=0)


def exchange_gather(x, axis):
    peers = lax.axis_size(axis)
    return lax.all_to_all(jnp.broadcast_to(x[None], (peers,) + x.shape), axis, 0, 0, tiled=True)


def exchange_position(axis, groups, source):
    me = lax.axis_index(axis)
    place = jnp.zeros_like(source)
    step = 1
    for bits in groups:
        group_of = lambda d: sum(((d // (1 << b)) % 2) * (1 << k) for k, b in enumerate(bits))
        place = place + jnp.bitwise_xor(group_of(source), group_of(me)) * step
        step = step * (1 << len(bits))
    return place


def staged_gather_unordered(x, axis, groups):
    acc = x
    for bits in groups:
        g = 1 << len(bits)
        acc = jnp.stack([acc] + [lax.ppermute(acc, axis, group_pairs(axis, bits, o)) for o in range(1, g)])
    return acc


def log2(n):
    return n.bit_length() - 1


def rope_tables(positions, head_width):
    half = head_width // 2
    frequency = rope_base ** (-(jnp.arange(half).astype(jnp.float32) * 2.0 / head_width))
    angle = positions.astype(jnp.float32)[:, None] * frequency[None, :]
    return (jnp.cos(angle), jnp.sin(angle))


def rotate(values, cosine, sine):
    half = values.shape[-1] // 2
    first = values[..., :half]
    second = values[..., half:]
    cos_rows = cosine[:, None, :]
    sin_rows = sine[:, None, :]
    return jnp.concatenate(
        [first * cos_rows - second * sin_rows, second * cos_rows + first * sin_rows], axis=-1
    )


def unrotate(grads, cosine, sine):
    half = grads.shape[-1] // 2
    first = grads[..., :half]
    second = grads[..., half:]
    cos_rows = cosine[:, None, :]
    sin_rows = sine[:, None, :]
    return jnp.concatenate(
        [first * cos_rows + second * sin_rows, second * cos_rows - first * sin_rows], axis=-1
    )


def norm_backward(rows, grads, gain, axes):
    inv_rms = lax.rsqrt(jnp.mean(rows * rows, axis=axes, keepdims=True) + rms_eps)
    scaled = grads * gain
    inner = jnp.mean(rows * scaled, axis=axes, keepdims=True)
    return inv_rms * scaled - rows * (inv_rms * inv_rms * inv_rms) * inner


def attention_block(queries, keys, values, grads, allowed):
    scale = 1.0 / math.sqrt(queries.shape[-1])
    scores = jnp.einsum("qhgd,khd->hgqk", queries, keys, preferred_element_type=jnp.float32) * scale
    masked = jnp.where(allowed[None, None], scores, masked_score)
    peak = jnp.max(masked, axis=-1, keepdims=True)
    raised = jnp.where(allowed[None, None], jnp.exp(masked - peak), 0.0)
    shares = raised / jnp.sum(raised, axis=-1, keepdims=True)
    shares_low = shares.astype(jnp.bfloat16)
    context = jnp.einsum(
        "hgqk,khd->qhgd", shares_low, values, preferred_element_type=jnp.float32
    ).astype(jnp.bfloat16)
    share_grads = jnp.einsum("qhgd,khd->hgqk", grads, values, preferred_element_type=jnp.float32)
    delta = jnp.sum(shares * share_grads, axis=-1, keepdims=True)
    score_grads = (shares * (share_grads - delta) * scale).astype(jnp.bfloat16)
    query_grads = jnp.einsum(
        "hgqk,khd->qhgd", score_grads, keys, preferred_element_type=jnp.float32
    )
    key_grads = jnp.einsum(
        "hgqk,qhgd->khd", score_grads, queries, preferred_element_type=jnp.float32
    )
    value_grads = jnp.einsum(
        "hgqk,qhgd->khd", shares_low, grads, preferred_element_type=jnp.float32
    )
    return (context, query_grads, key_grads, value_grads)


def on_device(
    vis_feat,
    ln_gain,
    proj_weight,
    text_embed,
    rms_gain,
    wq,
    wk,
    wv,
    doc_ids,
    vis_slot,
    slot_token,
    token_slot,
    cotangent,
):
    seq_count = lax.axis_size("seq")
    my_index = lax.axis_index("seq")
    tok_rows = text_embed.shape[0]
    slot_cols = proj_weight.shape[1]
    features = vis_feat.astype(jnp.float32)
    tp_count = lax.axis_size("tp")
    tp_bits = log2(tp_count)
    seq_bits = log2(seq_count)
    tp_all = [list(range(tp_bits))]
    seq_up = [[0], [1, 2], [3, 4]] if seq_bits == 5 else [[b] for b in range(seq_bits)]
    seq_down = seq_up[::-1]
    row_total, row_squares = jnp.sum(
        exchange_gather(
            jnp.stack([jnp.sum(features, axis=1), jnp.sum(features * features, axis=1)]), "tp"
        ),
        axis=0,
    )
    row_mean = row_total / VF
    row_var = row_squares / VF - row_mean * row_mean
    inv_std = lax.rsqrt(row_var + ln_eps)
    centred = (features - row_mean[:, None]) * inv_std[:, None]
    vis_normed = (centred * ln_gain[None, :]).astype(jnp.bfloat16)
    vis_rows = vis_feat.shape[0]
    all_normed = staged_gather_unordered(vis_normed, "seq", seq_down)
    partial_embed = jnp.dot(
        all_normed.reshape(seq_count * vis_rows, vis_feat.shape[1]),
        proj_weight,
        preferred_element_type=jnp.float32,
    )
    slot_live = (slot_token >= 0)[:, None]
    slot_index = jnp.maximum(slot_token, 0)
    devices = seq_count * tp_count
    per = CAPD // tp_count
    token_place = (
        exchange_position("seq", seq_down, slot_index // vis_rows) * vis_rows + slot_index % vis_rows
    )
    route = (
        (token_place[:, None] == jnp.arange(seq_count * vis_rows, dtype=jnp.int32)[None, :])
        & slot_live
    ).astype(jnp.bfloat16)
    outgoing = jnp.dot(
        route, partial_embed.astype(jnp.bfloat16), preferred_element_type=jnp.float32
    ).reshape(devices, per, slot_cols)
    got = lax.all_to_all(outgoing.astype(jnp.bfloat16), ("seq", "tp"), 0, 0, tiled=True)
    mine = jnp.sum(
        got.reshape(seq_count, tp_count, per, slot_cols).astype(jnp.float32), axis=1
    ).astype(jnp.bfloat16)
    all_mine = exchange_gather(mine.transpose(1, 0, 2), "tp")
    arrived = all_mine.reshape(CAPD, seq_count * slot_cols)
    lanes = jnp.arange(CAPD, dtype=jnp.int32)
    one_hot = (vis_slot[:, None] == lanes[None, :]).astype(jnp.bfloat16)
    head_rows = tok_rows - CAPD
    tail_slot = vis_slot[head_rows:]
    placed = jnp.dot(
        one_hot[head_rows:], arrived, preferred_element_type=jnp.float32
    ).astype(jnp.bfloat16)
    hidden_tail = jnp.where((tail_slot >= 0)[:, None], placed, text_embed[head_rows:])

    def rms_normed(hidden):
        hidden_wide = hidden.astype(jnp.float32)
        inv_rms = lax.rsqrt(jnp.mean(hidden_wide * hidden_wide, axis=1, keepdims=True) + rms_eps)
        return (hidden_wide * inv_rms * rms_gain[None, :]).astype(jnp.bfloat16)

    normed = lax.dynamic_update_slice_in_dim(
        rms_normed(text_embed), rms_normed(hidden_tail), head_rows, 0
    )
    stacked = jnp.concatenate([wq, wk, wv], axis=1)
    query_cols = wq.shape[1]
    key_cols = wk.shape[1]
    gathered = lax.all_gather(stacked, "seq", axis=0, tiled=True)
    projected = jnp.dot(normed, gathered, preferred_element_type=jnp.float32)
    local_heads = query_cols // HEAD
    local_groups = key_cols // HEAD
    positions = my_index * tok_rows + jnp.arange(tok_rows, dtype=jnp.int32)
    cosine, sine = rope_tables(positions, HEAD)
    queries = rotate(
        projected[:, :query_cols].reshape(tok_rows, local_heads, HEAD), cosine, sine
    ).astype(jnp.bfloat16)
    keys = rotate(
        projected[:, query_cols : query_cols + key_cols].reshape(tok_rows, local_groups, HEAD),
        cosine,
        sine,
    ).astype(jnp.bfloat16)
    values = (
        projected[:, query_cols + key_cols :]
        .astype(jnp.bfloat16)
        .reshape(tok_rows, local_groups, HEAD)
    )
    doc_marks = (doc_ids + 1).astype(jnp.bfloat16)
    prev_keys, prev_values, prev_docs = shifted((keys, values, doc_marks), "seq", 1)
    all_keys = jnp.concatenate([prev_keys, keys], axis=0)
    all_values = jnp.concatenate([prev_values, values], axis=0)
    query_docs = doc_marks.astype(jnp.float32)
    key_docs = jnp.concatenate([prev_docs.astype(jnp.float32), query_docs], axis=0)
    key_positions = jnp.concatenate([positions - tok_rows, positions], axis=0)
    allowed = (key_docs[None, :] == query_docs[:, None]) & (
        key_positions[None, :] <= positions[:, None]
    )
    grads = cotangent.reshape(tok_rows, local_groups, GROUP, HEAD)
    context, query_grads, key_grads, value_grads = attention_block(
        queries.reshape(tok_rows, local_groups, GROUP, HEAD), all_keys, all_values, grads, allowed
    )
    back_keys, back_values = (
        shifted(key_grads[:tok_rows].astype(jnp.bfloat16), "seq", -1).astype(jnp.float32),
        shifted(value_grads[:tok_rows].astype(jnp.bfloat16), "seq", -1).astype(jnp.float32),
    )
    key_total = key_grads[tok_rows:] + back_keys
    value_total = value_grads[tok_rows:] + back_values
    query_pre = (
        unrotate(query_grads.reshape(tok_rows, local_heads, HEAD), cosine, sine)
        .astype(jnp.bfloat16)
        .reshape(tok_rows, query_cols)
    )
    key_pre = unrotate(key_total, cosine, sine).astype(jnp.bfloat16).reshape(tok_rows, key_cols)
    value_pre = value_total.astype(jnp.bfloat16).reshape(tok_rows, key_cols)
    proj_grads = jnp.concatenate([query_pre, key_pre, value_pre], axis=1)
    selected = lax.dot_general(
        one_hot[head_rows:], proj_grads[head_rows:], (((0,), (0,)), ((), ())),
        preferred_element_type=jnp.float32,
    ).astype(jnp.bfloat16)
    norm_part = jnp.einsum(
        "tkc,jrc->jtkr",
        selected.reshape(tp_count, per, selected.shape[1]),
        gathered.reshape(seq_count, slot_cols, gathered.shape[1]),
        preferred_element_type=jnp.float32,
    )
    embed_part = norm_backward(
        all_mine.transpose(2, 0, 1, 3).astype(jnp.float32),
        norm_part,
        rms_gain.reshape(seq_count, 1, 1, slot_cols),
        (0, 3),
    )
    got_back = lax.all_to_all(
        embed_part.astype(jnp.bfloat16).reshape(devices, per, slot_cols),
        ("seq", "tp"), 0, 0, tiled=True,
    )
    mine_back = jnp.sum(
        got_back.reshape(seq_count, tp_count, per, slot_cols).astype(jnp.float32), axis=1
    ).astype(jnp.bfloat16)
    all_back = exchange_gather(mine_back, "tp").reshape(tp_count * seq_count * per, slot_cols)
    block_of = token_slot // CAPD
    lane_of = token_slot % CAPD
    back_index = (lane_of // per) * (seq_count * per) + block_of * per + lane_of % per
    pick = (
        back_index[:, None] == jnp.arange(all_back.shape[0], dtype=jnp.int32)[None, :]
    ).astype(jnp.bfloat16)
    token_grads = jnp.dot(pick, all_back, preferred_element_type=jnp.float32).astype(jnp.bfloat16)
    own_rows = vis_feat.shape[0]
    feature_part = jnp.einsum(
        "bqd,fd->bqf",
        token_grads.reshape(seq_count, own_rows, slot_cols),
        proj_weight,
        preferred_element_type=jnp.float32,
    )
    feature_grads = exchange_sum(feature_part, "seq")
    scaled = feature_grads * ln_gain[None, :]
    grad_total, grad_inner = jnp.sum(
        exchange_gather(
            jnp.stack([jnp.sum(scaled, axis=1), jnp.sum(scaled * centred, axis=1)]), "tp"
        ),
        axis=0,
    )
    vis_grad = (
        inv_std[:, None]
        * (scaled - (grad_total / VF)[:, None] - centred * (grad_inner / VF)[:, None])
    ).astype(jnp.bfloat16)
    return (context.reshape(tok_rows, query_cols), vis_grad)


def solution(mesh):
    return jax.shard_map(
        on_device,
        mesh=mesh,
        in_specs=(
            P("seq", "tp"),
            P("tp"),
            P("tp", "seq"),
            P("seq", None),
            P(),
            P("seq", "tp"),
            P("seq", "tp"),
            P("seq", "tp"),
            P("seq"),
            P("seq"),
            P(),
            P(),
            P("seq", "tp"),
        ),
        out_specs=(P("seq", "tp"), P("seq", "tp")),
        check_vma=False,
    )
```

```python
import math

import jax
import jax.numpy as jnp
from jax import lax
from jax.sharding import PartitionSpec as P

VF = 12800
HEAD = 128
CAPD = 32
GROUP = 4


ln_eps = 1e-05
rms_eps = 1e-06
rope_base = 1000000.0
masked_score = -1e30


def shifted(x, axis, by):
    peers = lax.axis_size(axis)
    pairs = [(i, i + by) for i in range(peers) if 0 <= i + by < peers]
    return lax.ppermute(x, axis, pairs)


def bit_of(axis, b):
    return (lax.axis_index(axis) // (1 << b)) % 2


def bit_pairs(axis, b):
    peers = lax.axis_size(axis)
    return [(i, i ^ (1 << b)) for i in range(peers)]


def group_index(axis, bits):
    return sum(bit_of(axis, b) * (1 << k) for k, b in enumerate(bits))


def group_pairs(axis, bits, o):
    peers = lax.axis_size(axis)
    mask = sum(((o >> k) & 1) << b for k, b in enumerate(bits))
    return [(i, i ^ mask) for i in range(peers)]


def group_scatter(x, axis, bits, dim=0):
    me = group_index(axis, bits)
    acc = lax.dynamic_index_in_dim(x, me, dim, keepdims=False).astype(jnp.float32)
    for o in range(1, 1 << len(bits)):
        send = lax.dynamic_index_in_dim(x, jnp.bitwise_xor(me, o), dim, keepdims=False)
        got = lax.ppermute(send.astype(jnp.bfloat16), axis, group_pairs(axis, bits, o))
        acc = acc + got.astype(jnp.float32)
    return acc


def group_gather(x, axis, bits):
    me = group_index(axis, bits)
    g = 1 << len(bits)
    parts = [x] + [lax.ppermute(x, axis, group_pairs(axis, bits, o)) for o in range(1, g)]
    order = jnp.bitwise_xor(jnp.arange(g, dtype=jnp.int32), me)
    return jnp.take(jnp.stack(parts), order, axis=0)


def staged_scatter(x, axis, groups):
    acc = x
    for bits in groups:
        g = 1 << len(bits)
        lead = acc.reshape((acc.shape[0] // g, g) + acc.shape[1:])
        acc = group_scatter(lead, axis, bits, dim=1)
    return acc[0]


def staged_gather(x, axis, groups):
    acc = x
    for bits in groups:
        acc = group_gather(acc, axis, bits)
    count = len(groups)
    return acc.transpose(list(range(count - 1, -1, -1)) + list(range(count, acc.ndim)))


def exchange_sum(x, axis):
    got = lax.all_to_all(x.astype(jnp.bfloat16), axis, 0, 0, tiled=True)
    return jnp.sum(got.astype(jnp.float32), axis=0)


def exchange_gather(x, axis):
    peers = lax.axis_size(axis)
    return lax.all_to_all(jnp.broadcast_to(x[None], (peers,) + x.shape), axis, 0, 0, tiled=True)


def exchange_position(axis, groups, source):
    me = lax.axis_index(axis)
    place = jnp.zeros_like(source)
    step = 1
    for bits in groups:
        group_of = lambda d: sum(((d // (1 << b)) % 2) * (1 << k) for k, b in enumerate(bits))
        place = place + jnp.bitwise_xor(group_of(source), group_of(me)) * step
        step = step * (1 << len(bits))
    return place


def staged_gather_unordered(x, axis, groups):
    acc = x
    for bits in groups:
        g = 1 << len(bits)
        acc = jnp.stack([acc] + [lax.ppermute(acc, axis, group_pairs(axis, bits, o)) for o in range(1, g)])
    return acc


def log2(n):
    return n.bit_length() - 1


def rope_tables(positions, head_width):
    half = head_width // 2
    frequency = rope_base ** (-(jnp.arange(half).astype(jnp.float32) * 2.0 / head_width))
    angle = positions.astype(jnp.float32)[:, None] * frequency[None, :]
    return (jnp.cos(angle), jnp.sin(angle))


def rotate(values, cosine, sine):
    half = values.shape[-1] // 2
    first = values[..., :half]
    second = values[..., half:]
    cos_rows = cosine[:, None, :]
    sin_rows = sine[:, None, :]
    return jnp.concatenate(
        [first * cos_rows - second * sin_rows, second * cos_rows + first * sin_rows], axis=-1
    )


def unrotate(grads, cosine, sine):
    half = grads.shape[-1] // 2
    first = grads[..., :half]
    second = grads[..., half:]
    cos_rows = cosine[:, None, :]
    sin_rows = sine[:, None, :]
    return jnp.concatenate(
        [first * cos_rows + second * sin_rows, second * cos_rows - first * sin_rows], axis=-1
    )


def norm_backward(rows, grads, gain, axes):
    inv_rms = lax.rsqrt(jnp.mean(rows * rows, axis=axes, keepdims=True) + rms_eps)
    scaled = grads * gain
    inner = jnp.mean(rows * scaled, axis=axes, keepdims=True)
    return inv_rms * scaled - rows * (inv_rms * inv_rms * inv_rms) * inner


def attention_block(queries, keys, values, grads, allowed):
    scale = 1.0 / math.sqrt(queries.shape[-1])
    scores = jnp.einsum("qhgd,khd->hgqk", queries, keys, preferred_element_type=jnp.float32) * scale
    masked = jnp.where(allowed[None, None], scores, masked_score)
    peak = jnp.max(masked, axis=-1, keepdims=True)
    raised = jnp.where(allowed[None, None], jnp.exp(masked - peak), 0.0)
    shares = raised / jnp.sum(raised, axis=-1, keepdims=True)
    shares_low = shares.astype(jnp.bfloat16)
    context = jnp.einsum(
        "hgqk,khd->qhgd", shares_low, values, preferred_element_type=jnp.float32
    ).astype(jnp.bfloat16)
    share_grads = jnp.einsum("qhgd,khd->hgqk", grads, values, preferred_element_type=jnp.float32)
    delta = jnp.sum(shares * share_grads, axis=-1, keepdims=True)
    score_grads = (shares * (share_grads - delta) * scale).astype(jnp.bfloat16)
    query_grads = jnp.einsum(
        "hgqk,khd->qhgd", score_grads, keys, preferred_element_type=jnp.float32
    )
    key_grads = jnp.einsum(
        "hgqk,qhgd->khd", score_grads, queries, preferred_element_type=jnp.float32
    )
    value_grads = jnp.einsum(
        "hgqk,qhgd->khd", shares_low, grads, preferred_element_type=jnp.float32
    )
    return (context, query_grads, key_grads, value_grads)


def on_device(
    vis_feat,
    ln_gain,
    proj_weight,
    text_embed,
    rms_gain,
    wq,
    wk,
    wv,
    doc_ids,
    vis_slot,
    slot_token,
    token_slot,
    cotangent,
):
    seq_count = lax.axis_size("seq")
    my_index = lax.axis_index("seq")
    tok_rows = text_embed.shape[0]
    slot_cols = proj_weight.shape[1]
    features = vis_feat.astype(jnp.float32)
    tp_count = lax.axis_size("tp")
    tp_bits = log2(tp_count)
    seq_bits = log2(seq_count)
    tp_all = [list(range(tp_bits))]
    seq_up = [[0], [1, 2], [3, 4]] if seq_bits == 5 else [[b] for b in range(seq_bits)]
    seq_down = seq_up[::-1]
    row_total, row_squares = jnp.sum(
        exchange_gather(
            jnp.stack([jnp.sum(features, axis=1), jnp.sum(features * features, axis=1)]), "tp"
        ),
        axis=0,
    )
    row_mean = row_total / VF
    row_var = row_squares / VF - row_mean * row_mean
    inv_std = lax.rsqrt(row_var + ln_eps)
    centred = (features - row_mean[:, None]) * inv_std[:, None]
    vis_normed = (centred * ln_gain[None, :]).astype(jnp.bfloat16)
    vis_rows = vis_feat.shape[0]
    all_normed = staged_gather_unordered(vis_normed, "seq", seq_down)
    partial_embed = jnp.dot(
        all_normed.reshape(seq_count * vis_rows, vis_feat.shape[1]),
        proj_weight,
        preferred_element_type=jnp.float32,
    )
    slot_live = (slot_token >= 0)[:, None]
    slot_index = jnp.maximum(slot_token, 0)
    devices = seq_count * tp_count
    per = CAPD // tp_count
    token_place = (
        exchange_position("seq", seq_down, slot_index // vis_rows) * vis_rows + slot_index % vis_rows
    )
    route = (
        (token_place[:, None] == jnp.arange(seq_count * vis_rows, dtype=jnp.int32)[None, :])
        & slot_live
    ).astype(jnp.bfloat16)
    outgoing = jnp.dot(
        route, partial_embed.astype(jnp.bfloat16), preferred_element_type=jnp.float32
    ).reshape(devices, per, slot_cols)
    got = lax.all_to_all(outgoing.astype(jnp.bfloat16), ("seq", "tp"), 0, 0, tiled=True)
    mine = jnp.sum(
        got.reshape(seq_count, tp_count, per, slot_cols).astype(jnp.float32), axis=1
    ).astype(jnp.bfloat16)
    all_mine = exchange_gather(mine.transpose(1, 0, 2), "tp")
    arrived = all_mine.reshape(CAPD, seq_count * slot_cols)
    lanes = jnp.arange(CAPD, dtype=jnp.int32)
    one_hot = (vis_slot[:, None] == lanes[None, :]).astype(jnp.bfloat16)
    head_rows = tok_rows - CAPD
    tail_slot = vis_slot[head_rows:]
    placed = jnp.dot(
        one_hot[head_rows:], arrived, preferred_element_type=jnp.float32
    ).astype(jnp.bfloat16)
    hidden_tail = jnp.where((tail_slot >= 0)[:, None], placed, text_embed[head_rows:])

    def rms_normed(hidden):
        hidden_wide = hidden.astype(jnp.float32)
        inv_rms = lax.rsqrt(jnp.mean(hidden_wide * hidden_wide, axis=1, keepdims=True) + rms_eps)
        return (hidden_wide * inv_rms * rms_gain[None, :]).astype(jnp.bfloat16)

    normed = lax.dynamic_update_slice_in_dim(
        rms_normed(text_embed), rms_normed(hidden_tail), head_rows, 0
    )
    stacked = jnp.concatenate([wq, wk, wv], axis=1)
    query_cols = wq.shape[1]
    key_cols = wk.shape[1]
    gathered = lax.all_gather(stacked, "seq", axis=0, tiled=True)
    projected = jnp.dot(normed, gathered, preferred_element_type=jnp.float32)
    local_heads = query_cols // HEAD
    local_groups = key_cols // HEAD
    positions = my_index * tok_rows + jnp.arange(tok_rows, dtype=jnp.int32)
    cosine, sine = rope_tables(positions, HEAD)
    queries = rotate(
        projected[:, :query_cols].reshape(tok_rows, local_heads, HEAD), cosine, sine
    ).astype(jnp.bfloat16)
    keys = rotate(
        projected[:, query_cols : query_cols + key_cols].reshape(tok_rows, local_groups, HEAD),
        cosine,
        sine,
    ).astype(jnp.bfloat16)
    values = (
        projected[:, query_cols + key_cols :]
        .astype(jnp.bfloat16)
        .reshape(tok_rows, local_groups, HEAD)
    )
    doc_marks = (doc_ids + 1).astype(jnp.bfloat16)
    prev_pair, prev_docs = shifted((jnp.concatenate([keys, values], axis=1), doc_marks), "seq", 1)
    prev_keys, prev_values = prev_pair[:, :local_groups], prev_pair[:, local_groups:]
    all_keys = jnp.concatenate([prev_keys, keys], axis=0)
    all_values = jnp.concatenate([prev_values, values], axis=0)
    query_docs = doc_marks.astype(jnp.float32)
    key_docs = jnp.concatenate([prev_docs.astype(jnp.float32), query_docs], axis=0)
    key_positions = jnp.concatenate([positions - tok_rows, positions], axis=0)
    allowed = (key_docs[None, :] == query_docs[:, None]) & (
        key_positions[None, :] <= positions[:, None]
    )
    grads = cotangent.reshape(tok_rows, local_groups, GROUP, HEAD)
    context, query_grads, key_grads, value_grads = attention_block(
        queries.reshape(tok_rows, local_groups, GROUP, HEAD), all_keys, all_values, grads, allowed
    )
    back_pair = shifted(
        jnp.concatenate([key_grads[:tok_rows], value_grads[:tok_rows]], axis=1).astype(jnp.bfloat16),
        "seq", -1,
    ).astype(jnp.float32)
    back_keys, back_values = back_pair[:, :local_groups], back_pair[:, local_groups:]
    key_total = key_grads[tok_rows:] + back_keys
    value_total = value_grads[tok_rows:] + back_values
    query_pre = (
        unrotate(query_grads.reshape(tok_rows, local_heads, HEAD), cosine, sine)
        .astype(jnp.bfloat16)
        .reshape(tok_rows, query_cols)
    )
    key_pre = unrotate(key_total, cosine, sine).astype(jnp.bfloat16).reshape(tok_rows, key_cols)
    value_pre = value_total.astype(jnp.bfloat16).reshape(tok_rows, key_cols)
    proj_grads = jnp.concatenate([query_pre, key_pre, value_pre], axis=1)
    selected = lax.dot_general(
        one_hot, proj_grads, (((0,), (0,)), ((), ())), preferred_element_type=jnp.float32
    ).astype(jnp.bfloat16)
    norm_part = jnp.einsum(
        "tkc,jrc->jtkr",
        selected.reshape(tp_count, per, selected.shape[1]),
        gathered.reshape(seq_count, slot_cols, gathered.shape[1]),
        preferred_element_type=jnp.float32,
    )
    embed_part = norm_backward(
        all_mine.transpose(2, 0, 1, 3).astype(jnp.float32),
        norm_part,
        rms_gain.reshape(seq_count, 1, 1, slot_cols),
        (0, 3),
    )
    got_back = lax.all_to_all(
        embed_part.astype(jnp.bfloat16).reshape(devices, per, slot_cols),
        ("seq", "tp"), 0, 0, tiled=True,
    )
    mine_back = jnp.sum(
        got_back.reshape(seq_count, tp_count, per, slot_cols).astype(jnp.float32), axis=1
    ).astype(jnp.bfloat16)
    all_back = exchange_gather(mine_back, "tp").reshape(tp_count * seq_count * per, slot_cols)
    block_of = token_slot // CAPD
    lane_of = token_slot % CAPD
    back_index = (lane_of // per) * (seq_count * per) + block_of * per + lane_of % per
    pick = (
        back_index[:, None] == jnp.arange(all_back.shape[0], dtype=jnp.int32)[None, :]
    ).astype(jnp.bfloat16)
    token_grads = jnp.dot(pick, all_back, preferred_element_type=jnp.float32).astype(jnp.bfloat16)
    own_rows = vis_feat.shape[0]
    feature_part = jnp.einsum(
        "bqd,fd->bqf",
        token_grads.reshape(seq_count, own_rows, slot_cols),
        proj_weight,
        preferred_element_type=jnp.float32,
    )
    feature_grads = exchange_sum(feature_part, "seq")
    scaled = feature_grads * ln_gain[None, :]
    grad_total, grad_inner = jnp.sum(
        exchange_gather(
            jnp.stack([jnp.sum(scaled, axis=1), jnp.sum(scaled * centred, axis=1)]), "tp"
        ),
        axis=0,
    )
    vis_grad = (
        inv_std[:, None]
        * (scaled - (grad_total / VF)[:, None] - centred * (grad_inner / VF)[:, None])
    ).astype(jnp.bfloat16)
    return (context.reshape(tok_rows, query_cols), vis_grad)


def solution(mesh):
    return jax.shard_map(
        on_device,
        mesh=mesh,
        in_specs=(
            P("seq", "tp"),
            P("tp"),
            P("tp", "seq"),
            P("seq", None),
            P(),
            P("seq", "tp"),
            P("seq", "tp"),
            P("seq", "tp"),
            P("seq"),
            P("seq"),
            P(),
            P(),
            P("seq", "tp"),
        ),
        out_specs=(P("seq", "tp"), P("seq", "tp")),
        check_vma=False,
    )
```

```python
import math

import jax
import jax.numpy as jnp
from jax import lax
from jax.sharding import PartitionSpec as P

VF = 12800
HEAD = 128
CAPD = 32
GROUP = 4


ln_eps = 1e-05
rms_eps = 1e-06
rope_base = 1000000.0
masked_score = -1e30


def shifted(x, axis, by):
    peers = lax.axis_size(axis)
    pairs = [(i, i + by) for i in range(peers) if 0 <= i + by < peers]
    return lax.ppermute(x, axis, pairs)


def bit_of(axis, b):
    return (lax.axis_index(axis) // (1 << b)) % 2


def bit_pairs(axis, b):
    peers = lax.axis_size(axis)
    return [(i, i ^ (1 << b)) for i in range(peers)]


def group_index(axis, bits):
    return sum(bit_of(axis, b) * (1 << k) for k, b in enumerate(bits))


def group_pairs(axis, bits, o):
    peers = lax.axis_size(axis)
    mask = sum(((o >> k) & 1) << b for k, b in enumerate(bits))
    return [(i, i ^ mask) for i in range(peers)]


def group_scatter(x, axis, bits, dim=0):
    me = group_index(axis, bits)
    acc = lax.dynamic_index_in_dim(x, me, dim, keepdims=False).astype(jnp.float32)
    for o in range(1, 1 << len(bits)):
        send = lax.dynamic_index_in_dim(x, jnp.bitwise_xor(me, o), dim, keepdims=False)
        got = lax.ppermute(send.astype(jnp.bfloat16), axis, group_pairs(axis, bits, o))
        acc = acc + got.astype(jnp.float32)
    return acc


def group_gather(x, axis, bits):
    me = group_index(axis, bits)
    g = 1 << len(bits)
    parts = [x] + [lax.ppermute(x, axis, group_pairs(axis, bits, o)) for o in range(1, g)]
    order = jnp.bitwise_xor(jnp.arange(g, dtype=jnp.int32), me)
    return jnp.take(jnp.stack(parts), order, axis=0)


def staged_scatter(x, axis, groups):
    acc = x
    for bits in groups:
        g = 1 << len(bits)
        lead = acc.reshape((acc.shape[0] // g, g) + acc.shape[1:])
        acc = group_scatter(lead, axis, bits, dim=1)
    return acc[0]


def staged_gather(x, axis, groups):
    acc = x
    for bits in groups:
        acc = group_gather(acc, axis, bits)
    count = len(groups)
    return acc.transpose(list(range(count - 1, -1, -1)) + list(range(count, acc.ndim)))


def exchange_sum(x, axis):
    got = lax.all_to_all(x.astype(jnp.bfloat16), axis, 0, 0, tiled=True)
    return jnp.sum(got.astype(jnp.float32), axis=0)


def exchange_gather(x, axis):
    peers = lax.axis_size(axis)
    return lax.all_to_all(jnp.broadcast_to(x[None], (peers,) + x.shape), axis, 0, 0, tiled=True)


def exchange_position(axis, groups, source):
    me = lax.axis_index(axis)
    place = jnp.zeros_like(source)
    step = 1
    for bits in groups:
        group_of = lambda d: sum(((d // (1 << b)) % 2) * (1 << k) for k, b in enumerate(bits))
        place = place + jnp.bitwise_xor(group_of(source), group_of(me)) * step
        step = step * (1 << len(bits))
    return place


def staged_gather_unordered(x, axis, groups):
    acc = x
    for bits in groups:
        g = 1 << len(bits)
        acc = jnp.stack([acc] + [lax.ppermute(acc, axis, group_pairs(axis, bits, o)) for o in range(1, g)])
    return acc


def log2(n):
    return n.bit_length() - 1


def rope_tables(positions, head_width):
    half = head_width // 2
    frequency = rope_base ** (-(jnp.arange(half).astype(jnp.float32) * 2.0 / head_width))
    angle = positions.astype(jnp.float32)[:, None] * frequency[None, :]
    return (jnp.cos(angle), jnp.sin(angle))


def rotate(values, cosine, sine):
    half = values.shape[-1] // 2
    first = values[..., :half]
    second = values[..., half:]
    cos_rows = cosine[:, None, :]
    sin_rows = sine[:, None, :]
    return jnp.concatenate(
        [first * cos_rows - second * sin_rows, second * cos_rows + first * sin_rows], axis=-1
    )


def unrotate(grads, cosine, sine):
    half = grads.shape[-1] // 2
    first = grads[..., :half]
    second = grads[..., half:]
    cos_rows = cosine[:, None, :]
    sin_rows = sine[:, None, :]
    return jnp.concatenate(
        [first * cos_rows + second * sin_rows, second * cos_rows - first * sin_rows], axis=-1
    )


def norm_backward(rows, grads, gain, axes):
    inv_rms = lax.rsqrt(jnp.mean(rows * rows, axis=axes, keepdims=True) + rms_eps)
    scaled = grads * gain
    inner = jnp.mean(rows * scaled, axis=axes, keepdims=True)
    return inv_rms * scaled - rows * (inv_rms * inv_rms * inv_rms) * inner


def attention_block(queries, keys, values, grads, allowed):
    scale = 1.0 / math.sqrt(queries.shape[-1])
    scores = jnp.einsum("qhgd,khd->hgqk", queries, keys, preferred_element_type=jnp.float32) * scale
    masked = jnp.where(allowed[None, None], scores, masked_score)
    peak = jnp.max(masked, axis=-1, keepdims=True)
    raised = jnp.where(allowed[None, None], jnp.exp(masked - peak), 0.0)
    shares = raised / jnp.sum(raised, axis=-1, keepdims=True)
    shares_low = shares.astype(jnp.bfloat16)
    context = jnp.einsum(
        "hgqk,khd->qhgd", shares_low, values, preferred_element_type=jnp.float32
    ).astype(jnp.bfloat16)
    share_grads = jnp.einsum("qhgd,khd->hgqk", grads, values, preferred_element_type=jnp.float32)
    delta = jnp.sum(shares * share_grads, axis=-1, keepdims=True)
    score_grads = (shares * (share_grads - delta) * scale).astype(jnp.bfloat16)
    query_grads = jnp.einsum(
        "hgqk,khd->qhgd", score_grads, keys, preferred_element_type=jnp.float32
    )
    key_grads = jnp.einsum(
        "hgqk,qhgd->khd", score_grads, queries, preferred_element_type=jnp.float32
    )
    value_grads = jnp.einsum(
        "hgqk,qhgd->khd", shares_low, grads, preferred_element_type=jnp.float32
    )
    return (context, query_grads, key_grads, value_grads)


def on_device(
    vis_feat,
    ln_gain,
    proj_weight,
    text_embed,
    rms_gain,
    wq,
    wk,
    wv,
    doc_ids,
    vis_slot,
    slot_token,
    token_slot,
    cotangent,
):
    seq_count = lax.axis_size("seq")
    my_index = lax.axis_index("seq")
    tok_rows = text_embed.shape[0]
    slot_cols = proj_weight.shape[1]
    features = vis_feat.astype(jnp.float32)
    tp_count = lax.axis_size("tp")
    tp_bits = log2(tp_count)
    seq_bits = log2(seq_count)
    tp_all = [list(range(tp_bits))]
    seq_up = [[0], [1, 2], [3, 4]] if seq_bits == 5 else [[b] for b in range(seq_bits)]
    seq_down = seq_up[::-1]
    row_total, row_squares = jnp.sum(
        exchange_gather(
            jnp.stack([jnp.sum(features, axis=1), jnp.sum(features * features, axis=1)]), "tp"
        ),
        axis=0,
    )
    row_mean = row_total / VF
    row_var = row_squares / VF - row_mean * row_mean
    inv_std = lax.rsqrt(row_var + ln_eps)
    centred = (features - row_mean[:, None]) * inv_std[:, None]
    vis_normed = (centred * ln_gain[None, :]).astype(jnp.bfloat16)
    vis_rows = vis_feat.shape[0]
    all_normed = staged_gather_unordered(vis_normed, "seq", seq_down)
    partial_embed = jnp.dot(
        all_normed.reshape(seq_count * vis_rows, vis_feat.shape[1]),
        proj_weight,
        preferred_element_type=jnp.float32,
    )
    slot_live = (slot_token >= 0)[:, None]
    slot_index = jnp.maximum(slot_token, 0)
    devices = seq_count * tp_count
    per = CAPD // tp_count
    token_place = (
        exchange_position("seq", seq_down, slot_index // vis_rows) * vis_rows + slot_index % vis_rows
    )
    route = (
        (token_place[:, None] == jnp.arange(seq_count * vis_rows, dtype=jnp.int32)[None, :])
        & slot_live
    ).astype(jnp.bfloat16)
    outgoing = jnp.dot(
        route, partial_embed.astype(jnp.bfloat16), preferred_element_type=jnp.float32
    ).reshape(devices, per, slot_cols)
    got = lax.all_to_all(outgoing.astype(jnp.bfloat16), ("seq", "tp"), 0, 0, tiled=True)
    mine = jnp.sum(
        got.reshape(seq_count, tp_count, per, slot_cols).astype(jnp.float32), axis=1
    ).astype(jnp.bfloat16)
    all_mine = exchange_gather(mine.transpose(1, 0, 2), "tp")
    arrived = all_mine.reshape(CAPD, seq_count * slot_cols)
    lanes = jnp.arange(CAPD, dtype=jnp.int32)
    one_hot = (vis_slot[:, None] == lanes[None, :]).astype(jnp.bfloat16)
    head_rows = tok_rows - CAPD
    tail_slot = vis_slot[head_rows:]
    placed = jnp.dot(
        one_hot[head_rows:], arrived, preferred_element_type=jnp.float32
    ).astype(jnp.bfloat16)
    hidden_tail = jnp.where((tail_slot >= 0)[:, None], placed, text_embed[head_rows:])

    def rms_normed(hidden):
        hidden_wide = hidden.astype(jnp.float32)
        inv_rms = lax.rsqrt(jnp.mean(hidden_wide * hidden_wide, axis=1, keepdims=True) + rms_eps)
        return (hidden_wide * inv_rms * rms_gain[None, :]).astype(jnp.bfloat16)

    normed = lax.dynamic_update_slice_in_dim(
        rms_normed(text_embed), rms_normed(hidden_tail), head_rows, 0
    )
    stacked = jnp.concatenate([wq, wk, wv], axis=1)
    query_cols = wq.shape[1]
    key_cols = wk.shape[1]
    gathered = lax.all_gather(stacked, "seq", axis=0, tiled=True)
    projected = jnp.dot(normed, gathered, preferred_element_type=jnp.float32)
    local_heads = query_cols // HEAD
    local_groups = key_cols // HEAD
    positions = my_index * tok_rows + jnp.arange(tok_rows, dtype=jnp.int32)
    cosine, sine = rope_tables(positions, HEAD)
    queries = rotate(
        projected[:, :query_cols].reshape(tok_rows, local_heads, HEAD), cosine, sine
    ).astype(jnp.bfloat16)
    keys = rotate(
        projected[:, query_cols : query_cols + key_cols].reshape(tok_rows, local_groups, HEAD),
        cosine,
        sine,
    ).astype(jnp.bfloat16)
    values = (
        projected[:, query_cols + key_cols :]
        .astype(jnp.bfloat16)
        .reshape(tok_rows, local_groups, HEAD)
    )
    doc_marks = (doc_ids + 1).astype(jnp.bfloat16)
    prev_pair, prev_docs = shifted((jnp.concatenate([keys, values], axis=1), doc_marks), "seq", 1)
    prev_keys, prev_values = prev_pair[:, :local_groups], prev_pair[:, local_groups:]
    all_keys = jnp.concatenate([prev_keys, keys], axis=0)
    all_values = jnp.concatenate([prev_values, values], axis=0)
    query_docs = doc_marks.astype(jnp.float32)
    key_docs = jnp.concatenate([prev_docs.astype(jnp.float32), query_docs], axis=0)
    key_positions = jnp.concatenate([positions - tok_rows, positions], axis=0)
    allowed = (key_docs[None, :] == query_docs[:, None]) & (
        key_positions[None, :] <= positions[:, None]
    )
    grads = cotangent.reshape(tok_rows, local_groups, GROUP, HEAD)
    context, query_grads, key_grads, value_grads = attention_block(
        queries.reshape(tok_rows, local_groups, GROUP, HEAD), all_keys, all_values, grads, allowed
    )
    back_pair = shifted(
        jnp.concatenate([key_grads[:tok_rows], value_grads[:tok_rows]], axis=1).astype(jnp.bfloat16),
        "seq", -1,
    ).astype(jnp.float32)
    back_keys, back_values = back_pair[:, :local_groups], back_pair[:, local_groups:]
    key_total = key_grads[tok_rows:] + back_keys
    value_total = value_grads[tok_rows:] + back_values
    query_pre = (
        unrotate(query_grads.reshape(tok_rows, local_heads, HEAD), cosine, sine)
        .astype(jnp.bfloat16)
        .reshape(tok_rows, query_cols)
    )
    key_pre = unrotate(key_total, cosine, sine).astype(jnp.bfloat16).reshape(tok_rows, key_cols)
    value_pre = value_total.astype(jnp.bfloat16).reshape(tok_rows, key_cols)
    proj_grads = jnp.concatenate([query_pre, key_pre, value_pre], axis=1)
    selected = lax.dot_general(
        one_hot[head_rows:], proj_grads[head_rows:], (((0,), (0,)), ((), ())),
        preferred_element_type=jnp.float32,
    ).astype(jnp.bfloat16)
    norm_part = jnp.einsum(
        "tkc,jrc->jtkr",
        selected.reshape(tp_count, per, selected.shape[1]),
        gathered.reshape(seq_count, slot_cols, gathered.shape[1]),
        preferred_element_type=jnp.float32,
    )
    embed_part = norm_backward(
        all_mine.transpose(2, 0, 1, 3).astype(jnp.float32),
        norm_part,
        rms_gain.reshape(seq_count, 1, 1, slot_cols),
        (0, 3),
    )
    got_back = lax.all_to_all(
        embed_part.astype(jnp.bfloat16).reshape(devices, per, slot_cols),
        ("seq", "tp"), 0, 0, tiled=True,
    )
    mine_back = jnp.sum(
        got_back.reshape(seq_count, tp_count, per, slot_cols).astype(jnp.float32), axis=1
    ).astype(jnp.bfloat16)
    all_back = exchange_gather(mine_back, "tp").reshape(tp_count * seq_count * per, slot_cols)
    block_of = token_slot // CAPD
    lane_of = token_slot % CAPD
    back_index = (lane_of // per) * (seq_count * per) + block_of * per + lane_of % per
    pick = (
        back_index[:, None] == jnp.arange(all_back.shape[0], dtype=jnp.int32)[None, :]
    ).astype(jnp.bfloat16)
    token_grads = jnp.dot(pick, all_back, preferred_element_type=jnp.float32).astype(jnp.bfloat16)
    own_rows = vis_feat.shape[0]
    feature_part = jnp.einsum(
        "bqd,fd->bqf",
        token_grads.reshape(seq_count, own_rows, slot_cols),
        proj_weight,
        preferred_element_type=jnp.float32,
    )
    feature_grads = exchange_sum(feature_part, "seq")
    scaled = feature_grads * ln_gain[None, :]
    grad_total, grad_inner = jnp.sum(
        exchange_gather(
            jnp.stack([jnp.sum(scaled, axis=1), jnp.sum(scaled * centred, axis=1)]), "tp"
        ),
        axis=0,
    )
    vis_grad = (
        inv_std[:, None]
        * (scaled - (grad_total / VF)[:, None] - centred * (grad_inner / VF)[:, None])
    ).astype(jnp.bfloat16)
    return (context.reshape(tok_rows, query_cols), vis_grad)


def solution(mesh):
    return jax.shard_map(
        on_device,
        mesh=mesh,
        in_specs=(
            P("seq", "tp"),
            P("tp"),
            P("tp", "seq"),
            P("seq", None),
            P(),
            P("seq", "tp"),
            P("seq", "tp"),
            P("seq", "tp"),
            P("seq"),
            P("seq"),
            P(),
            P(),
            P("seq", "tp"),
        ),
        out_specs=(P("seq", "tp"), P("seq", "tp")),
        check_vma=False,
    )
```
